32 devices in a mesh: groups: 2 (over y), freq: 4 (over z), src: 2 (over x), vp: 2 (over core).
Axes of the slice: x: 2, y: 2, z: 4, core: 2. Of those that a mesh axis runs over, the one named last changes fastest.
Arguments:
- focus_direct: bfloat16 [4, 2, 192, 8192], P('freq', None, ('groups', 'vp'), 'src'), parts along dimension 2, may hold values from -6 to 6
- u_factors: bfloat16 [4, 32, 2, 32, 2048], P('freq', 'src'), may hold values from -0.1875 to 0.1875
- v_factors: bfloat16 [4, 8, 2, 32, 8192], P('freq', None, None, None, 'src'), may hold values from -0.375 to 0.375
- tile_ranks: int32 [4, 8, 32], P('freq', None, 'src'), may hold values from 16 to 32
- onset_rec: int32 [192, 2048], P(('groups', 'vp'), 'src'), parts along dimension 0, may hold values from 64 to 191
- onset_src: int32 [192, 8192], P(('groups', 'vp'), 'src'), parts along dimension 0, may hold values from 64 to 191
Outputs:
- focus_plus: bfloat16 [4, 2, 192, 8192], P('freq', None, ('groups', 'vp'), 'src'), parts along dimension 2
- focus_minus: bfloat16 [4, 2, 192, 2048], P('freq', None, ('groups', 'vp'), 'src'), parts along dimension 2
The draws below stay inside these ranges and needn't reach their ends.
There are 2 independent parts, one for each index of `groups`. The reference program is written for one: setup_inputs(seed, part) draws one part's arguments, and reference() takes and returns one part's arrays. A program takes and returns all parts, laid end to end along the dimension named above; an argument that names none is the same for every part. Nothing has to cross between parts.
All inputs are finite; a program needn't handle non-finite values.
Results may differ from the reference program's by a relative error of at most 0.018.
Values may be sent and summed in bfloat16 or wider, within the bound.
No kernel may reach another device: no remote copies, remote signals or barrier semaphores. Data moves between devices by JAX's collectives and lax.ppermute only.
A program may use at most 128 MiB of HBM per device.

```python
import math
import jax
import jax.numpy as jnp
from jax import lax

NR = 2048
NS = 8192
TILE = 256
RANK = 32
NT = 256
FLO = 8
ITERS = 2
NF = 4
VP = 96
RT = 8
CT = 32


def with_ends(values, own_key, least, top_value):
    shape = values.shape
    index_at = [jax.random.randint(jax.random.fold_in(own_key, axis), (), 0, shape[axis]) for axis in range(len(shape))]
    values = values.at[tuple(index_at)].set(least)
    longest = shape.index(max(shape))
    index_at[longest] = (index_at[longest] + 1) % shape[longest]
    return values.at[tuple(index_at)].set(top_value)


def steps_of(rng, dims, cuts, low, high):
    def one(position, shards_of):
        heights = jax.random.uniform(jax.random.fold_in(jax.random.fold_in(rng, 6), position), (shards_of,), jnp.float32, low / len(cuts), high / len(cuts))
        return jnp.repeat(jnp.exp(heights), dims[position] // shards_of).reshape((-1,) + (1,) * (len(dims) - position - 1))

    factor_of = one(*cuts[0])
    for cut in cuts[1:]:
        factor_of = factor_of * one(*cut)
    return factor_of


def centred(stream_key, dims, width, reach, split=(), kind=jnp.bfloat16):
    values = jax.random.normal(stream_key, dims, jnp.float32) * width
    if len(split) > 0:
        values = steps_of(stream_key, dims, split, -0.22, 0.18) * values
    return jnp.clip(values, min=-reach, max=reach).astype(kind)


def setup_inputs(seed: int = 0, part: int = 0) -> dict:
    splits = jax.random.split(jax.random.key(seed), 7)
    part_splits = jax.random.split(jax.random.fold_in(splits[6], part), 7)
    return {
        "focus_direct": centred(part_splits[0], (NF, 2, VP, NS), 1.0, 6.0, ((0, 4), (2, 2), (3, 2))),
        "u_factors": centred(splits[1], (NF, CT, 2, RANK, NR), (RANK * NS // TILE) ** -0.5, 0.1875, ((0, 4), (1, 2))),
        "v_factors": centred(splits[2], (NF, RT, 2, RANK, NS), TILE ** -0.5, 0.375, ((0, 4), (4, 2))),
        "tile_ranks": with_ends(jax.random.randint(splits[3], (NF, RT, CT), RANK // 2, RANK + 1), jax.random.fold_in(splits[3], 1), RANK // 2, RANK).astype(jnp.int32),
        "onset_rec": with_ends(jax.random.randint(part_splits[4], (VP, NR), NT // 4, 3 * NT // 4), jax.random.fold_in(part_splits[4], 1), NT // 4, (3 * NT // 4) - 1).astype(jnp.int32),
        "onset_src": with_ends(jax.random.randint(part_splits[5], (VP, NS), NT // 4, 3 * NT // 4), jax.random.fold_in(part_splits[5], 1), NT // 4, (3 * NT // 4) - 1).astype(jnp.int32),
    }


def make_tables(count):
    index = FLO + jnp.arange(count, dtype=jnp.int32)
    sample = jnp.arange(NT, dtype=jnp.int32)
    phase = ((index[:, None] * sample[None, :]) % NT).astype(jnp.float32) * (2.0 * math.pi / NT)
    cosine = jnp.cos(phase)
    sine = jnp.sin(phase)
    inverse = jnp.stack([cosine, -sine]) * (2.0 / NT)
    forward = jnp.stack([cosine, -sine])
    return inverse, forward


def window_trace(spectrum, onset, inverse, forward):
    signal = jnp.einsum("fcm,cft->mt", spectrum, inverse, precision=lax.Precision.HIGHEST)
    keep = jnp.arange(NT, dtype=jnp.int32)[None, :] < onset[:, None]
    signal = jnp.where(keep, signal, jnp.zeros_like(signal))
    return jnp.einsum("mt,cft->fcm", signal, forward, precision=lax.Precision.HIGHEST)


def window(spectrum, onset):
    inverse, forward = make_tables(spectrum.shape[0])
    moved = jnp.moveaxis(spectrum, 2, 0)
    result = lax.map(lambda pair: window_trace(pair[0], pair[1], inverse, forward), (moved, onset))
    return jnp.moveaxis(result, 0, 2)


def rank_mask(ranks):
    return (jnp.arange(RANK, dtype=jnp.int32)[None, None, :] < ranks[:, :, None])[:, None]


def round_half(values):
    rounded = values.astype(jnp.bfloat16)
    rounded = lax.optimization_barrier(rounded)
    return rounded.astype(jnp.float32)


def forward_one(args):
    u_fac, v_fac, ranks, focus = args
    source = focus.astype(jnp.float32).reshape(2, VP, CT, TILE)
    v_tiles = v_fac.astype(jnp.float32).reshape(RT, 2, RANK, CT, TILE)
    u_tiles = u_fac.astype(jnp.float32).reshape(CT, 2, RANK, RT, TILE)
    z_real = jnp.einsum("irjt,vjt->ivjr", v_tiles[:, 0], source[0]) + jnp.einsum("irjt,vjt->ivjr", v_tiles[:, 1], source[1])
    z_imag = jnp.einsum("irjt,vjt->ivjr", v_tiles[:, 0], source[1]) - jnp.einsum("irjt,vjt->ivjr", v_tiles[:, 1], source[0])
    mask = rank_mask(ranks)
    z_real = round_half(jnp.where(mask, z_real, 0.0))
    z_imag = round_half(jnp.where(mask, z_imag, 0.0))
    y_real = jnp.einsum("jrit,ivjr->vit", u_tiles[:, 0], z_real) - jnp.einsum("jrit,ivjr->vit", u_tiles[:, 1], z_imag)
    y_imag = jnp.einsum("jrit,ivjr->vit", u_tiles[:, 0], z_imag) + jnp.einsum("jrit,ivjr->vit", u_tiles[:, 1], z_real)
    return jnp.stack([y_real.reshape(VP, NR), y_imag.reshape(VP, NR)])


def adjoint_one(args):
    u_fac, v_fac, ranks, focus = args
    receiver = focus.astype(jnp.float32).reshape(2, VP, RT, TILE)
    v_tiles = v_fac.astype(jnp.float32).reshape(RT, 2, RANK, CT, TILE)
    u_tiles = u_fac.astype(jnp.float32).reshape(CT, 2, RANK, RT, TILE)
    w_real = jnp.einsum("jrit,vit->ivjr", u_tiles[:, 0], receiver[0]) + jnp.einsum("jrit,vit->ivjr", u_tiles[:, 1], receiver[1])
    w_imag = jnp.einsum("jrit,vit->ivjr", u_tiles[:, 0], receiver[1]) - jnp.einsum("jrit,vit->ivjr", u_tiles[:, 1], receiver[0])
    mask = rank_mask(ranks)
    w_real = round_half(jnp.where(mask, w_real, 0.0))
    w_imag = round_half(jnp.where(mask, w_imag, 0.0))
    x_real = jnp.einsum("irjt,ivjr->vjt", v_tiles[:, 0], w_real) - jnp.einsum("irjt,ivjr->vjt", v_tiles[:, 1], w_imag)
    x_imag = jnp.einsum("irjt,ivjr->vjt", v_tiles[:, 0], w_imag) + jnp.einsum("irjt,ivjr->vjt", v_tiles[:, 1], w_real)
    return jnp.stack([x_real.reshape(VP, NS), x_imag.reshape(VP, NS)])


def reference(focus_direct, u_factors, v_factors, tile_ranks, onset_rec, onset_src):
    plus = focus_direct
    minus = None
    for sweep in range(ITERS):
        reflected = lax.map(forward_one, (u_factors, v_factors, tile_ranks, plus))
        minus = window(reflected, onset_rec).astype(jnp.bfloat16)
        adjoint = lax.map(adjoint_one, (u_factors, v_factors, tile_ranks, minus))
        returned = window(adjoint, onset_src)
        plus = (focus_direct.astype(jnp.float32) + returned).astype(jnp.bfloat16)
    return plus, minus
```

```python
import math

import jax
import jax.numpy as jnp
from jax import lax
from jax.sharding import PartitionSpec as P

TILE = 256
RANK = 32
NT = 256
FLO = 8
ITERS = 2
GATHER_MAX = 4


def make_tables(count):
    index = FLO + jnp.arange(count, dtype=jnp.int32)
    sample = jnp.arange(NT, dtype=jnp.int32)
    phase = (index[:, None] * sample[None, :] % NT).astype(jnp.float32) * (2.0 * math.pi / NT)
    cosine = jnp.cos(phase)
    sine = jnp.sin(phase)
    inverse = jnp.stack([cosine, -sine]) * (2.0 / NT)
    forward = jnp.stack([cosine, -sine])
    return (inverse, forward)


def window_gather(count, onset):
    if count > GATHER_MAX:
        return onset
    inverse, forward = make_tables(count)
    terms = jnp.einsum("cft,dgt->tfcgd", forward, inverse, precision=lax.Precision.HIGHEST)
    table = jnp.cumsum(terms.reshape(NT, 4 * count * count), axis=0)
    high = table.astype(jnp.bfloat16)
    rest = table - high.astype(jnp.float32)
    middle = rest.astype(jnp.bfloat16)
    low = (rest - middle.astype(jnp.float32)).astype(jnp.bfloat16)
    place = jnp.clip(onset, 0, NT) - 1
    pick = (lax.broadcasted_iota(jnp.int32, (NT,) + onset.shape, 0) == place[None]).astype(jnp.bfloat16)
    parts = [
        jnp.einsum("kq,kvm->qvm", part, pick, preferred_element_type=jnp.float32)
        for part in (high, middle, low)
    ]
    picked = (parts[0] + parts[1]) + parts[2]
    return picked.reshape((2 * count, 2 * count) + onset.shape)


def window_direct(spectrum, onset):
    inverse, forward = make_tables(spectrum.shape[0])
    signal = jnp.einsum("fcvm,cft->vmt", spectrum, inverse, precision=lax.Precision.HIGHEST)
    keep = jnp.arange(NT, dtype=jnp.int32)[None, None, :] < onset[:, :, None]
    signal = jnp.where(keep, signal, jnp.zeros_like(signal))
    return jnp.einsum("vmt,cft->fcvm", signal, forward, precision=lax.Precision.HIGHEST)


def window(spectrum, picked):
    count = spectrum.shape[0]
    if count > GATHER_MAX:
        return window_direct(spectrum, picked)
    flat = spectrum.reshape((2 * count,) + spectrum.shape[2:])
    result = jnp.sum(picked * flat[None], axis=1)
    return result.reshape(spectrum.shape)


def coefficients(v_fac, mask, focus):
    points = focus.shape[1]
    row_tiles = v_fac.shape[0]
    col_tiles = v_fac.shape[-1] // TILE
    source = focus.reshape(2, points, col_tiles, TILE)
    v_tiles = v_fac.reshape(row_tiles, 2, RANK, col_tiles, TILE)
    form = "irjt,vjt->ivjr"
    z_real = jnp.einsum(
        form, v_tiles[:, 0], source[0], preferred_element_type=jnp.float32
    ) + jnp.einsum(form, v_tiles[:, 1], source[1], preferred_element_type=jnp.float32)
    z_imag = jnp.einsum(
        form, v_tiles[:, 0], source[1], preferred_element_type=jnp.float32
    ) - jnp.einsum(form, v_tiles[:, 1], source[0], preferred_element_type=jnp.float32)
    z_real = jnp.where(mask, z_real, 0.0).astype(jnp.bfloat16)
    z_imag = jnp.where(mask, z_imag, 0.0).astype(jnp.bfloat16)
    return jnp.stack([z_real, z_imag])


def expand_rows(u_fac, coeff):
    col_tiles = u_fac.shape[0]
    row_tiles = u_fac.shape[-1] // TILE
    points = coeff.shape[2]
    u_tiles = u_fac.reshape(col_tiles, 2, RANK, row_tiles, TILE)
    other = "jrit,ivjr->vit"
    y_real = jnp.einsum(
        other, u_tiles[:, 0], coeff[0], preferred_element_type=jnp.float32
    ) - jnp.einsum(other, u_tiles[:, 1], coeff[1], preferred_element_type=jnp.float32)
    y_imag = jnp.einsum(
        other, u_tiles[:, 0], coeff[1], preferred_element_type=jnp.float32
    ) + jnp.einsum(other, u_tiles[:, 1], coeff[0], preferred_element_type=jnp.float32)
    return jnp.stack([y_real.reshape(points, -1), y_imag.reshape(points, -1)])


def forward_local(u_fac, v_fac, mask, focus):
    return expand_rows(u_fac, coefficients(v_fac, mask, focus))


def adjoint_local(u_fac, v_fac, mask, focus):
    points = focus.shape[1]
    col_tiles = u_fac.shape[0]
    row_tiles = v_fac.shape[0]
    receiver = focus.reshape(2, points, row_tiles, TILE)
    v_tiles = v_fac.reshape(row_tiles, 2, RANK, col_tiles, TILE)
    u_tiles = u_fac.reshape(col_tiles, 2, RANK, row_tiles, TILE)
    form = "jrit,vit->ivjr"
    w_real = jnp.einsum(
        form, u_tiles[:, 0], receiver[0], preferred_element_type=jnp.float32
    ) + jnp.einsum(form, u_tiles[:, 1], receiver[1], preferred_element_type=jnp.float32)
    w_imag = jnp.einsum(
        form, u_tiles[:, 0], receiver[1], preferred_element_type=jnp.float32
    ) - jnp.einsum(form, u_tiles[:, 1], receiver[0], preferred_element_type=jnp.float32)
    w_real = jnp.where(mask, w_real, 0.0).astype(jnp.bfloat16)
    w_imag = jnp.where(mask, w_imag, 0.0).astype(jnp.bfloat16)
    other = "irjt,ivjr->vjt"
    x_real = jnp.einsum(
        other, v_tiles[:, 0], w_real, preferred_element_type=jnp.float32
    ) - jnp.einsum(other, v_tiles[:, 1], w_imag, preferred_element_type=jnp.float32)
    x_imag = jnp.einsum(
        other, v_tiles[:, 0], w_imag, preferred_element_type=jnp.float32
    ) + jnp.einsum(other, v_tiles[:, 1], w_real, preferred_element_type=jnp.float32)
    return jnp.stack([x_real.reshape(points, -1), x_imag.reshape(points, -1)])


def per_device(focus_direct, u_factors, v_factors, tile_ranks, onset_rec, onset_src):
    freq_count = lax.axis_size("freq")
    rank_index = jnp.arange(RANK, dtype=jnp.int32)
    masks = (rank_index[None, None, None, :] < tile_ranks[:, :, :, None])[:, :, None]
    rec_block = onset_rec.shape[1]
    rec_piece = rec_block // freq_count
    src_piece = onset_src.shape[1] // freq_count
    freq_place = lax.axis_index("freq")
    rec_onset = lax.dynamic_slice_in_dim(onset_rec, freq_place * rec_piece, rec_piece, 1)
    src_onset = lax.dynamic_slice_in_dim(onset_src, freq_place * src_piece, src_piece, 1)
    rec_picked = window_gather(freq_count, rec_onset)
    src_picked = window_gather(freq_count, src_onset)
    plus = focus_direct
    minus = None
    for sweep in range(ITERS):
        partial_terms = jax.vmap(forward_local)(u_factors, v_factors, masks, plus)
        summed = lax.psum_scatter(
            partial_terms.astype(jnp.bfloat16), "src", scatter_dimension=3, tiled=True
        ).astype(jnp.float32)
        traces = lax.all_to_all(
            summed.astype(jnp.bfloat16), "freq", split_axis=3, concat_axis=0, tiled=True
        ).astype(summed.dtype)
        windowed = window(traces, rec_picked).astype(jnp.bfloat16)
        minus = lax.all_to_all(windowed, "freq", split_axis=0, concat_axis=3, tiled=True)
        minus_all = lax.all_gather(minus, "src", axis=3, tiled=True)
        adjoint = jax.vmap(adjoint_local)(u_factors, v_factors, masks, minus_all)
        source_traces = lax.all_to_all(
            adjoint.astype(jnp.bfloat16), "freq", split_axis=3, concat_axis=0, tiled=True
        ).astype(adjoint.dtype)
        src_windowed = window(source_traces, src_picked)
        returned = lax.all_to_all(
            src_windowed.astype(jnp.bfloat16), "freq", split_axis=0, concat_axis=3, tiled=True
        ).astype(src_windowed.dtype)
        plus = (focus_direct.astype(jnp.float32) + returned).astype(jnp.bfloat16)
    return (plus, minus)


def solution(mesh):
    placed = (
        P("freq", None, ("groups", "vp"), "src"),
        P("freq", "src", None, None, None),
        P("freq", None, None, None, "src"),
        P("freq", None, "src"),
        P(("groups", "vp"), "src"),
        P(("groups", "vp"), "src"),
    )
    return jax.shard_map(
        per_device,
        mesh=mesh,
        in_specs=placed,
        out_specs=(
            P("freq", None, ("groups", "vp"), "src"),
            P("freq", None, ("groups", "vp"), "src"),
        ),
        check_vma=False,
    )
```

```python
import math

import jax
import jax.numpy as jnp
from jax import lax
from jax.sharding import PartitionSpec as P

TILE = 256
RANK = 32
NT = 256
FLO = 8
ITERS = 2
GATHER_MAX = 4


def make_tables(count):
    index = FLO + jnp.arange(count, dtype=jnp.int32)
    sample = jnp.arange(NT, dtype=jnp.int32)
    phase = (index[:, None] * sample[None, :] % NT).astype(jnp.float32) * (2.0 * math.pi / NT)
    cosine = jnp.cos(phase)
    sine = jnp.sin(phase)
    inverse = jnp.stack([cosine, -sine]) * (2.0 / NT)
    forward = jnp.stack([cosine, -sine])
    return (inverse, forward)


def window_gather(count, onset):
    if count > GATHER_MAX:
        return onset
    inverse, forward = make_tables(count)
    terms = jnp.einsum("cft,dgt->tfcgd", forward, inverse, precision=lax.Precision.HIGHEST)
    size = 4 * count * count
    table = jnp.cumsum(terms.reshape(NT, size), axis=0)
    high = table.astype(jnp.bfloat16)
    rest = table - high.astype(jnp.float32)
    middle = rest.astype(jnp.bfloat16)
    low = (rest - middle.astype(jnp.float32)).astype(jnp.bfloat16)
    stacked = jnp.concatenate([high, middle, low], axis=1)
    place = jnp.clip(onset, 0, NT) - 1
    pick = (lax.broadcasted_iota(jnp.int32, (NT,) + onset.shape, 0) == place[None]).astype(jnp.bfloat16)
    parts = jnp.einsum("kq,kbvm->qbvm", stacked, pick, preferred_element_type=jnp.float32)
    return (parts[:size] + parts[size : 2 * size]) + parts[2 * size :]


def window(spectrum, picked):
    count = spectrum.shape[0]
    if count > GATHER_MAX:
        inverse, forward = make_tables(count)
        signal = jnp.einsum("fbcvm,cft->bvmt", spectrum, inverse, precision=lax.Precision.HIGHEST)
        keep = lax.broadcasted_iota(jnp.int32, signal.shape, 3) < picked[..., None]
        signal = jnp.where(keep, signal, jnp.zeros_like(signal))
        return jnp.einsum("bvmt,cft->fbcvm", signal, forward, precision=lax.Precision.HIGHEST)
    rest = spectrum.shape[1:2] + spectrum.shape[3:]
    matrix = picked.reshape((count, 2, count, 2) + rest)
    source = jnp.transpose(spectrum, (0, 2, 1, 3, 4))
    result = jnp.sum(matrix * source[None, None], axis=(2, 3))
    return jnp.transpose(result, (0, 2, 1, 3, 4))


def piece_count(tiles, parts):
    return parts // math.gcd(tiles, parts)


def to_pieces(x, parts):
    tiles, comps, points, width = x.shape
    k = piece_count(tiles, parts)
    if k == 1:
        return x
    x = x.reshape(tiles, comps, points, k, width // k)
    return jnp.transpose(x, (0, 3, 1, 2, 4)).reshape(tiles * k, comps, points, width // k)


def from_pieces(x, tiles):
    count, comps, points, width = x.shape
    k = count // tiles
    if k == 1:
        return x
    x = x.reshape(tiles, k, comps, points, width)
    return jnp.transpose(x, (0, 2, 3, 1, 4)).reshape(tiles, comps, points, k * width)


def onset_pieces(onset, tiles, parts, place):
    points = onset.shape[0]
    k = piece_count(tiles, parts)
    blocks = tiles * k
    each = blocks // parts
    split = onset.reshape(points, blocks, TILE // k)
    split = jnp.transpose(split, (1, 0, 2))
    return lax.dynamic_slice_in_dim(split, place * each, each, 0)


def exchange(x, parts):
    tiles = x.shape[0]
    pieces = to_pieces(x, parts)
    got = lax.all_to_all(pieces, "freq", split_axis=0, concat_axis=0, tiled=True)
    return got.reshape((parts, got.shape[0] // parts) + got.shape[1:])


def exchange_back(y, tiles):
    flat = y.reshape((y.shape[0] * y.shape[1],) + y.shape[2:])
    got = lax.all_to_all(flat, "freq", split_axis=0, concat_axis=0, tiled=True)
    return from_pieces(got, tiles)


def coefficients(v_tiles, mask, plus):
    form = "irjt,jvt->ivjr"
    p_re = plus[:, 0]
    p_im = plus[:, 1]
    z_real = jnp.einsum(
        form, v_tiles[:, 0], p_re, preferred_element_type=jnp.float32
    ) + jnp.einsum(form, v_tiles[:, 1], p_im, preferred_element_type=jnp.float32)
    z_imag = jnp.einsum(
        form, v_tiles[:, 0], p_im, preferred_element_type=jnp.float32
    ) - jnp.einsum(form, v_tiles[:, 1], p_re, preferred_element_type=jnp.float32)
    z_real = jnp.where(mask, z_real, 0.0).astype(jnp.bfloat16)
    z_imag = jnp.where(mask, z_imag, 0.0).astype(jnp.bfloat16)
    return z_real, z_imag


def expand_rows(u_tiles, z_real, z_imag):
    other = "jrit,ivjr->ivt"
    y_real = jnp.einsum(
        other, u_tiles[:, 0], z_real, preferred_element_type=jnp.float32
    ) - jnp.einsum(other, u_tiles[:, 1], z_imag, preferred_element_type=jnp.float32)
    y_imag = jnp.einsum(
        other, u_tiles[:, 0], z_imag, preferred_element_type=jnp.float32
    ) + jnp.einsum(other, u_tiles[:, 1], z_real, preferred_element_type=jnp.float32)
    return jnp.stack([y_real, y_imag], axis=1)


def adjoint_local(u_tiles, v_tiles, mask, minus):
    form = "jrit,ivt->ivjr"
    m_re = minus[:, 0]
    m_im = minus[:, 1]
    w_real = jnp.einsum(
        form, u_tiles[:, 0], m_re, preferred_element_type=jnp.float32
    ) + jnp.einsum(form, u_tiles[:, 1], m_im, preferred_element_type=jnp.float32)
    w_imag = jnp.einsum(
        form, u_tiles[:, 0], m_im, preferred_element_type=jnp.float32
    ) - jnp.einsum(form, u_tiles[:, 1], m_re, preferred_element_type=jnp.float32)
    w_real = jnp.where(mask, w_real, 0.0).astype(jnp.bfloat16)
    w_imag = jnp.where(mask, w_imag, 0.0).astype(jnp.bfloat16)
    other = "irjt,ivjr->jvt"
    x_real = jnp.einsum(
        other, v_tiles[:, 0], w_real, preferred_element_type=jnp.float32
    ) - jnp.einsum(other, v_tiles[:, 1], w_imag, preferred_element_type=jnp.float32)
    x_imag = jnp.einsum(
        other, v_tiles[:, 0], w_imag, preferred_element_type=jnp.float32
    ) + jnp.einsum(other, v_tiles[:, 1], w_real, preferred_element_type=jnp.float32)
    return jnp.stack([x_real, x_imag], axis=1)


def tile_major(x):
    comps, points, width = x.shape
    return jnp.transpose(x.reshape(comps, points, width // TILE, TILE), (2, 0, 1, 3))


def tile_minor(x):
    tiles, comps, points, width = x.shape
    return jnp.transpose(x, (1, 2, 0, 3)).reshape(comps, points, tiles * width)


def per_device(focus_direct, u_factors, v_factors, tile_ranks, onset_rec, onset_src):
    parts = lax.axis_size("freq")
    place = lax.axis_index("freq")
    u_fac = u_factors[0]
    v_fac = v_factors[0]
    col_tiles = u_fac.shape[0]
    row_tiles = v_fac.shape[0]
    u_tiles = u_fac.reshape(col_tiles, 2, RANK, row_tiles, TILE)
    v_tiles = v_fac.reshape(row_tiles, 2, RANK, col_tiles, TILE)
    rank_index = jnp.arange(RANK, dtype=jnp.int32)
    mask = (rank_index[None, None, :] < tile_ranks[0][:, :, None])[:, None]
    rec_tiles = onset_rec.shape[1] // TILE
    rec_picked = window_gather(parts, onset_pieces(onset_rec, rec_tiles, parts, place))
    src_picked = window_gather(parts, onset_pieces(onset_src, col_tiles, parts, place))
    direct = tile_major(focus_direct[0])
    direct_f32 = direct.astype(jnp.float32)
    plus = direct
    minus = None
    for sweep in range(ITERS):
        z_real, z_imag = coefficients(v_tiles, mask, plus)
        partial_terms = expand_rows(u_tiles, z_real, z_imag)
        summed = lax.psum_scatter(
            partial_terms.astype(jnp.bfloat16), "src", scatter_dimension=0, tiled=True
        )
        traces = exchange(summed, parts).astype(jnp.float32)
        windowed = window(traces, rec_picked).astype(jnp.bfloat16)
        minus = exchange_back(windowed, rec_tiles)
        minus_all = lax.all_gather(minus, "src", axis=0, tiled=True)
        adjoint = adjoint_local(u_tiles, v_tiles, mask, minus_all)
        source_traces = exchange(adjoint.astype(jnp.bfloat16), parts).astype(jnp.float32)
        src_windowed = window(source_traces, src_picked).astype(jnp.bfloat16)
        returned = exchange_back(src_windowed, col_tiles).astype(jnp.float32)
        plus = (direct_f32 + returned).astype(jnp.bfloat16)
    return (tile_minor(plus)[None], tile_minor(minus)[None])


def solution(mesh):
    placed = (
        P("freq", None, ("groups", "vp"), "src"),
        P("freq", "src", None, None, None),
        P("freq", None, None, None, "src"),
        P("freq", None, "src"),
        P(("groups", "vp"), "src"),
        P(("groups", "vp"), "src"),
    )
    return jax.shard_map(
        per_device,
        mesh=mesh,
        in_specs=placed,
        out_specs=(
            P("freq", None, ("groups", "vp"), "src"),
            P("freq", None, ("groups", "vp"), "src"),
        ),
        check_vma=False,
    )
```

```python
import math

import jax
import jax.numpy as jnp
from jax import lax
from jax.experimental import pallas as pl
from jax.sharding import PartitionSpec as P

TILE = 256
RANK = 32
NT = 256
FLO = 8
ITERS = 2
GATHER_MAX = 4


def make_tables(count):
    index = FLO + jnp.arange(count, dtype=jnp.int32)
    sample = jnp.arange(NT, dtype=jnp.int32)
    phase = (index[:, None] * sample[None, :] % NT).astype(jnp.float32) * (2.0 * math.pi / NT)
    cosine = jnp.cos(phase)
    sine = jnp.sin(phase)
    inverse = jnp.stack([cosine, -sine]) * (2.0 / NT)
    forward = jnp.stack([cosine, -sine])
    return (inverse, forward)


def gather_kernel(table_ref, onset_ref, out_ref):
    rows = onset_ref.shape[1]
    width = onset_ref.shape[2]
    size = out_ref.shape[0]
    sample = lax.broadcasted_iota(jnp.int32, (NT, width), 0)
    for row in range(rows):
        place = jnp.clip(onset_ref[0, row : row + 1, :], 0, NT) - 1
        pick = (sample == place).astype(jnp.bfloat16)
        parts = jnp.dot(table_ref[...], pick, preferred_element_type=jnp.float32)
        out_ref[:, 0, row, :] = (parts[:size] + parts[size : 2 * size]) + parts[2 * size :]


def window_gather(count, onset):
    if count > GATHER_MAX:
        return onset
    inverse, forward = make_tables(count)
    terms = jnp.einsum("cft,dgt->tgdfc", forward, inverse, precision=lax.Precision.HIGHEST)
    size = 4 * count * count
    table = jnp.cumsum(terms.reshape(NT, size), axis=0)
    high = table.astype(jnp.bfloat16)
    rest = table - high.astype(jnp.float32)
    middle = rest.astype(jnp.bfloat16)
    low = (rest - middle.astype(jnp.float32)).astype(jnp.bfloat16)
    stacked = jnp.concatenate([high, middle, low], axis=1).T
    blocks, points, width = onset.shape
    rows = 8
    return pl.pallas_call(
        gather_kernel,
        grid=(blocks, points // rows),
        in_specs=[
            pl.BlockSpec((3 * size, NT), lambda b, r: (0, 0)),
            pl.BlockSpec((1, rows, width), lambda b, r: (b, r, 0)),
        ],
        out_specs=pl.BlockSpec((size, 1, rows, width), lambda b, r: (0, b, r, 0)),
        out_shape=jax.ShapeDtypeStruct((size, blocks, points, width), jnp.float32),
    )(stacked, onset)


def window_kernel(matrix_ref, spectrum_ref, out_ref):
    count = spectrum_ref.shape[0]
    comps = 2 * count
    source = [spectrum_ref[q // 2, 0, q % 2].astype(jnp.float32) for q in range(comps)]
    for target in range(comps):
        total = matrix_ref[target, 0] * source[0]
        for q in range(1, comps):
            total = total + matrix_ref[q * comps + target, 0] * source[q]
        out_ref[target // 2, 0, target % 2] = total.astype(out_ref.dtype)


def window(spectrum, picked):
    count = spectrum.shape[0]
    if count > GATHER_MAX:
        inverse, forward = make_tables(count)
        signal = jnp.einsum(
            "fbcvm,cft->bvmt", spectrum.astype(jnp.float32), inverse, precision=lax.Precision.HIGHEST
        )
        keep = lax.broadcasted_iota(jnp.int32, signal.shape, 3) < picked[..., None]
        signal = jnp.where(keep, signal, jnp.zeros_like(signal))
        result = jnp.einsum("bvmt,cft->fbcvm", signal, forward, precision=lax.Precision.HIGHEST)
        return result.astype(jnp.bfloat16)
    _, blocks, comps, points, width = spectrum.shape
    size = picked.shape[0]
    return pl.pallas_call(
        window_kernel,
        grid=(blocks,),
        in_specs=[
            pl.BlockSpec((size, 1, points, width), lambda b: (0, b, 0, 0)),
            pl.BlockSpec((count, 1, comps, points, width), lambda b: (0, b, 0, 0, 0)),
        ],
        out_specs=pl.BlockSpec((count, 1, comps, points, width), lambda b: (0, b, 0, 0, 0)),
        out_shape=jax.ShapeDtypeStruct(spectrum.shape, jnp.bfloat16),
    )(picked, spectrum)


def piece_count(tiles, parts):
    return parts // math.gcd(tiles, parts)


def to_pieces(x, parts):
    tiles, comps, points, width = x.shape
    k = piece_count(tiles, parts)
    if k == 1:
        return x
    x = x.reshape(tiles, comps, points, k, width // k)
    return jnp.transpose(x, (0, 3, 1, 2, 4)).reshape(tiles * k, comps, points, width // k)


def from_pieces(x, tiles):
    count, comps, points, width = x.shape
    k = count // tiles
    if k == 1:
        return x
    x = x.reshape(tiles, k, comps, points, width)
    return jnp.transpose(x, (0, 2, 3, 1, 4)).reshape(tiles, comps, points, k * width)


def onset_pieces(onset, tiles, parts, place):
    points = onset.shape[0]
    k = piece_count(tiles, parts)
    blocks = tiles * k
    each = blocks // parts
    split = onset.reshape(points, blocks, TILE // k)
    split = jnp.transpose(split, (1, 0, 2))
    return lax.dynamic_slice_in_dim(split, place * each, each, 0)


def exchange(x, parts):
    tiles = x.shape[0]
    pieces = to_pieces(x, parts)
    got = lax.all_to_all(pieces, "freq", split_axis=0, concat_axis=0, tiled=True)
    return got.reshape((parts, got.shape[0] // parts) + got.shape[1:])


def exchange_back(y, tiles):
    flat = y.reshape((y.shape[0] * y.shape[1],) + y.shape[2:])
    got = lax.all_to_all(flat, "freq", split_axis=0, concat_axis=0, tiled=True)
    return from_pieces(got, tiles)


def coefficients(v_tiles, mask, plus):
    form = "irjt,jvt->ivjr"
    p_re = plus[:, 0]
    p_im = plus[:, 1]
    z_real = jnp.einsum(
        form, v_tiles[:, 0], p_re, preferred_element_type=jnp.float32
    ) + jnp.einsum(form, v_tiles[:, 1], p_im, preferred_element_type=jnp.float32)
    z_imag = jnp.einsum(
        form, v_tiles[:, 0], p_im, preferred_element_type=jnp.float32
    ) - jnp.einsum(form, v_tiles[:, 1], p_re, preferred_element_type=jnp.float32)
    z_real = jnp.where(mask, z_real, 0.0).astype(jnp.bfloat16)
    z_imag = jnp.where(mask, z_imag, 0.0).astype(jnp.bfloat16)
    return z_real, z_imag


def expand_rows(u_tiles, z_real, z_imag):
    other = "jrit,ivjr->ivt"
    y_real = jnp.einsum(
        other, u_tiles[:, 0], z_real, preferred_element_type=jnp.float32
    ) - jnp.einsum(other, u_tiles[:, 1], z_imag, preferred_element_type=jnp.float32)
    y_imag = jnp.einsum(
        other, u_tiles[:, 0], z_imag, preferred_element_type=jnp.float32
    ) + jnp.einsum(other, u_tiles[:, 1], z_real, preferred_element_type=jnp.float32)
    return jnp.stack([y_real, y_imag], axis=1)


def adjoint_local(u_tiles, v_tiles, mask, minus):
    form = "jrit,ivt->ivjr"
    m_re = minus[:, 0]
    m_im = minus[:, 1]
    w_real = jnp.einsum(
        form, u_tiles[:, 0], m_re, preferred_element_type=jnp.float32
    ) + jnp.einsum(form, u_tiles[:, 1], m_im, preferred_element_type=jnp.float32)
    w_imag = jnp.einsum(
        form, u_tiles[:, 0], m_im, preferred_element_type=jnp.float32
    ) - jnp.einsum(form, u_tiles[:, 1], m_re, preferred_element_type=jnp.float32)
    w_real = jnp.where(mask, w_real, 0.0).astype(jnp.bfloat16)
    w_imag = jnp.where(mask, w_imag, 0.0).astype(jnp.bfloat16)
    other = "irjt,ivjr->jvt"
    x_real = jnp.einsum(
        other, v_tiles[:, 0], w_real, preferred_element_type=jnp.float32
    ) - jnp.einsum(other, v_tiles[:, 1], w_imag, preferred_element_type=jnp.float32)
    x_imag = jnp.einsum(
        other, v_tiles[:, 0], w_imag, preferred_element_type=jnp.float32
    ) + jnp.einsum(other, v_tiles[:, 1], w_real, preferred_element_type=jnp.float32)
    return jnp.stack([x_real, x_imag], axis=1)


def reduce_src(partial):
    count = lax.axis_size("src")
    if count != 2:
        return lax.psum_scatter(
            partial.astype(jnp.bfloat16), "src", scatter_dimension=0, tiled=True
        )
    place = lax.axis_index("src")
    half = partial.shape[0] // 2
    mine = lax.dynamic_slice_in_dim(partial, place * half, half, 0)
    other = lax.dynamic_slice_in_dim(partial, (1 - place) * half, half, 0)
    got = lax.ppermute(other.astype(jnp.bfloat16), "src", perm=[(0, 1), (1, 0)])
    return (mine.astype(jnp.bfloat16).astype(jnp.float32) + got.astype(jnp.float32)).astype(jnp.bfloat16)


def tile_major(x):
    comps, points, width = x.shape
    return jnp.transpose(x.reshape(comps, points, width // TILE, TILE), (2, 0, 1, 3))


def tile_minor(x):
    tiles, comps, points, width = x.shape
    return jnp.transpose(x, (1, 2, 0, 3)).reshape(comps, points, tiles * width)


def per_device(focus_direct, u_factors, v_factors, tile_ranks, onset_rec, onset_src):
    parts = lax.axis_size("freq")
    place = lax.axis_index("freq")
    u_fac = u_factors[0]
    v_fac = v_factors[0]
    col_tiles = u_fac.shape[0]
    row_tiles = v_fac.shape[0]
    u_tiles = u_fac.reshape(col_tiles, 2, RANK, row_tiles, TILE)
    v_tiles = v_fac.reshape(row_tiles, 2, RANK, col_tiles, TILE)
    rank_index = jnp.arange(RANK, dtype=jnp.int32)
    mask = (rank_index[None, None, :] < tile_ranks[0][:, :, None])[:, None]
    rec_tiles = onset_rec.shape[1] // TILE
    rec_picked = window_gather(parts, onset_pieces(onset_rec, rec_tiles, parts, place))
    src_picked = window_gather(parts, onset_pieces(onset_src, col_tiles, parts, place))
    direct = tile_major(focus_direct[0])
    direct_f32 = direct.astype(jnp.float32)
    plus = direct
    minus = None
    for sweep in range(ITERS):
        z_real, z_imag = coefficients(v_tiles, mask, plus)
        partial_terms = expand_rows(u_tiles, z_real, z_imag)
        summed = reduce_src(partial_terms)
        traces = exchange(summed, parts)
        windowed = window(traces, rec_picked)
        minus = exchange_back(windowed, rec_tiles)
        minus_all = lax.all_gather(minus, "src", axis=0, tiled=True)
        adjoint = adjoint_local(u_tiles, v_tiles, mask, minus_all)
        source_traces = exchange(adjoint.astype(jnp.bfloat16), parts)
        src_windowed = window(source_traces, src_picked)
        returned = exchange_back(src_windowed, col_tiles).astype(jnp.float32)
        plus = (direct_f32 + returned).astype(jnp.bfloat16)
    return (tile_minor(plus)[None], tile_minor(minus)[None])


def solution(mesh):
    placed = (
        P("freq", None, ("groups", "vp"), "src"),
        P("freq", "src", None, None, None),
        P("freq", None, None, None, "src"),
        P("freq", None, "src"),
        P(("groups", "vp"), "src"),
        P(("groups", "vp"), "src"),
    )
    return jax.shard_map(
        per_device,
        mesh=mesh,
        in_specs=placed,
        out_specs=(
            P("freq", None, ("groups", "vp"), "src"),
            P("freq", None, ("groups", "vp"), "src"),
        ),
        check_vma=False,
    )
```

```python
import math

import jax
import jax.numpy as jnp
from jax import lax
from jax.experimental import pallas as pl
from jax.sharding import PartitionSpec as P

TILE = 256
RANK = 32
NT = 256
FLO = 8
ITERS = 2
GATHER_MAX = 4
PERMUTE_MAX = 4
CHAINS = 2


def make_tables(count):
    index = FLO + jnp.arange(count, dtype=jnp.int32)
    sample = jnp.arange(NT, dtype=jnp.int32)
    phase = (index[:, None] * sample[None, :] % NT).astype(jnp.float32) * (2.0 * math.pi / NT)
    cosine = jnp.cos(phase)
    sine = jnp.sin(phase)
    inverse = jnp.stack([cosine, -sine]) * (2.0 / NT)
    forward = jnp.stack([cosine, -sine])
    return (inverse, forward)


def gather_kernel(table_ref, onset_ref, out_ref):
    rows = onset_ref.shape[1]
    width = onset_ref.shape[2]
    size = out_ref.shape[0]
    sample = lax.broadcasted_iota(jnp.int32, (NT, width), 0)
    for row in range(rows):
        place = jnp.clip(onset_ref[0, row : row + 1, :], 0, NT) - 1
        pick = (sample == place).astype(jnp.bfloat16)
        parts = jnp.dot(table_ref[...], pick, preferred_element_type=jnp.float32)
        out_ref[:, 0, row, :] = (parts[:size] + parts[size : 2 * size]) + parts[2 * size :]


def window_gather(count, onset):
    if count > GATHER_MAX:
        return onset
    inverse, forward = make_tables(count)
    terms = jnp.einsum("cft,dgt->tgdfc", forward, inverse, precision=lax.Precision.HIGHEST)
    size = 4 * count * count
    table = jnp.cumsum(terms.reshape(NT, size), axis=0)
    high = table.astype(jnp.bfloat16)
    rest = table - high.astype(jnp.float32)
    middle = rest.astype(jnp.bfloat16)
    low = (rest - middle.astype(jnp.float32)).astype(jnp.bfloat16)
    stacked = jnp.concatenate([high, middle, low], axis=1).T
    blocks, points, width = onset.shape
    rows = 8
    return pl.pallas_call(
        gather_kernel,
        grid=(blocks, points // rows),
        in_specs=[
            pl.BlockSpec((3 * size, NT), lambda b, r: (0, 0)),
            pl.BlockSpec((1, rows, width), lambda b, r: (b, r, 0)),
        ],
        out_specs=pl.BlockSpec((size, 1, rows, width), lambda b, r: (0, b, r, 0)),
        out_shape=jax.ShapeDtypeStruct((size, blocks, points, width), jnp.float32),
    )(stacked, onset)


def window_kernel(matrix_ref, spectrum_ref, out_ref):
    count = spectrum_ref.shape[0]
    comps = 2 * count
    source = [spectrum_ref[q // 2, 0, q % 2].astype(jnp.float32) for q in range(comps)]
    for target in range(comps):
        total = matrix_ref[target, 0] * source[0]
        for q in range(1, comps):
            total = total + matrix_ref[q * comps + target, 0] * source[q]
        out_ref[target // 2, 0, target % 2] = total.astype(out_ref.dtype)


def window(spectrum, picked):
    count = spectrum.shape[0]
    if count > GATHER_MAX:
        inverse, forward = make_tables(count)
        signal = jnp.einsum(
            "fbcvm,cft->bvmt", spectrum.astype(jnp.float32), inverse, precision=lax.Precision.HIGHEST
        )
        keep = lax.broadcasted_iota(jnp.int32, signal.shape, 3) < picked[..., None]
        signal = jnp.where(keep, signal, jnp.zeros_like(signal))
        result = jnp.einsum("bvmt,cft->fbcvm", signal, forward, precision=lax.Precision.HIGHEST)
        return result.astype(jnp.bfloat16)
    _, blocks, comps, points, width = spectrum.shape
    size = picked.shape[0]
    return pl.pallas_call(
        window_kernel,
        grid=(blocks,),
        in_specs=[
            pl.BlockSpec((size, 1, points, width), lambda b: (0, b, 0, 0)),
            pl.BlockSpec((count, 1, comps, points, width), lambda b: (0, b, 0, 0, 0)),
        ],
        out_specs=pl.BlockSpec((count, 1, comps, points, width), lambda b: (0, b, 0, 0, 0)),
        out_shape=jax.ShapeDtypeStruct(spectrum.shape, jnp.bfloat16),
    )(picked, spectrum)


def piece_count(tiles, parts):
    return parts // math.gcd(tiles, parts)


def to_pieces(x, parts):
    tiles, comps, points, width = x.shape
    k = piece_count(tiles, parts)
    if k == 1:
        return x
    x = x.reshape(tiles, comps, points, k, width // k)
    return jnp.transpose(x, (0, 3, 1, 2, 4)).reshape(tiles * k, comps, points, width // k)


def from_pieces(x, tiles):
    count, comps, points, width = x.shape
    k = count // tiles
    if k == 1:
        return x
    x = x.reshape(tiles, k, comps, points, width)
    return jnp.transpose(x, (0, 2, 3, 1, 4)).reshape(tiles, comps, points, k * width)


def onset_pieces(onset, tiles, parts, place):
    points = onset.shape[0]
    k = piece_count(tiles, parts)
    blocks = tiles * k
    each = blocks // parts
    split = onset.reshape(points, blocks, TILE // k)
    split = jnp.transpose(split, (1, 0, 2))
    return lax.dynamic_slice_in_dim(split, place * each, each, 0)


def swap_blocks(x, parts):
    if parts == 1:
        return x
    if parts > PERMUTE_MAX:
        return lax.all_to_all(x, "freq", split_axis=0, concat_axis=0, tiled=True)
    place = lax.axis_index("freq")
    each = x.shape[0] // parts
    blocks = x.reshape((parts, each) + x.shape[1:])
    got = [lax.dynamic_index_in_dim(blocks, place, 0, keepdims=False)]
    for shift in range(1, parts):
        send = lax.dynamic_index_in_dim(blocks, (place + shift) % parts, 0, keepdims=False)
        got.append(lax.ppermute(send, "freq", perm=[(i, (i + shift) % parts) for i in range(parts)]))
    stacked = jnp.stack(got)
    order = (place - jnp.arange(parts, dtype=jnp.int32)) % parts
    return jnp.take(stacked, order, axis=0).reshape(x.shape)


def gather_src(x):
    count = lax.axis_size("src")
    if count != 2:
        return lax.all_gather(x, "src", axis=0, tiled=True)
    place = lax.axis_index("src")
    got = lax.ppermute(x, "src", perm=[(0, 1), (1, 0)])
    pair = jnp.stack([x, got])
    order = jnp.stack([place, 1 - place])
    return jnp.take(pair, order, axis=0).reshape((2 * x.shape[0],) + x.shape[1:])


def exchange(x, parts):
    tiles = x.shape[0]
    pieces = to_pieces(x, parts)
    got = swap_blocks(pieces, parts)
    return got.reshape((parts, got.shape[0] // parts) + got.shape[1:])


def exchange_back(y, tiles, parts):
    flat = y.reshape((y.shape[0] * y.shape[1],) + y.shape[2:])
    got = swap_blocks(flat, parts)
    return from_pieces(got, tiles)


def coefficients(v_tiles, mask, plus):
    form = "irjt,jvt->ivjr"
    p_re = plus[:, 0]
    p_im = plus[:, 1]
    z_real = jnp.einsum(
        form, v_tiles[:, 0], p_re, preferred_element_type=jnp.float32
    ) + jnp.einsum(form, v_tiles[:, 1], p_im, preferred_element_type=jnp.float32)
    z_imag = jnp.einsum(
        form, v_tiles[:, 0], p_im, preferred_element_type=jnp.float32
    ) - jnp.einsum(form, v_tiles[:, 1], p_re, preferred_element_type=jnp.float32)
    z_real = jnp.where(mask, z_real, 0.0).astype(jnp.bfloat16)
    z_imag = jnp.where(mask, z_imag, 0.0).astype(jnp.bfloat16)
    return z_real, z_imag


def expand_rows(u_tiles, z_real, z_imag):
    other = "jrit,ivjr->ivt"
    y_real = jnp.einsum(
        other, u_tiles[:, 0], z_real, preferred_element_type=jnp.float32
    ) - jnp.einsum(other, u_tiles[:, 1], z_imag, preferred_element_type=jnp.float32)
    y_imag = jnp.einsum(
        other, u_tiles[:, 0], z_imag, preferred_element_type=jnp.float32
    ) + jnp.einsum(other, u_tiles[:, 1], z_real, preferred_element_type=jnp.float32)
    return jnp.stack([y_real, y_imag], axis=1)


def adjoint_local(u_tiles, v_tiles, mask, minus):
    form = "jrit,ivt->ivjr"
    m_re = minus[:, 0]
    m_im = minus[:, 1]
    w_real = jnp.einsum(
        form, u_tiles[:, 0], m_re, preferred_element_type=jnp.float32
    ) + jnp.einsum(form, u_tiles[:, 1], m_im, preferred_element_type=jnp.float32)
    w_imag = jnp.einsum(
        form, u_tiles[:, 0], m_im, preferred_element_type=jnp.float32
    ) - jnp.einsum(form, u_tiles[:, 1], m_re, preferred_element_type=jnp.float32)
    w_real = jnp.where(mask, w_real, 0.0).astype(jnp.bfloat16)
    w_imag = jnp.where(mask, w_imag, 0.0).astype(jnp.bfloat16)
    other = "irjt,ivjr->jvt"
    x_real = jnp.einsum(
        other, v_tiles[:, 0], w_real, preferred_element_type=jnp.float32
    ) - jnp.einsum(other, v_tiles[:, 1], w_imag, preferred_element_type=jnp.float32)
    x_imag = jnp.einsum(
        other, v_tiles[:, 0], w_imag, preferred_element_type=jnp.float32
    ) + jnp.einsum(other, v_tiles[:, 1], w_real, preferred_element_type=jnp.float32)
    return jnp.stack([x_real, x_imag], axis=1)


def reduce_src(partial):
    count = lax.axis_size("src")
    if count != 2:
        return lax.psum_scatter(
            partial.astype(jnp.bfloat16), "src", scatter_dimension=0, tiled=True
        )
    place = lax.axis_index("src")
    half = partial.shape[0] // 2
    mine = lax.dynamic_slice_in_dim(partial, place * half, half, 0)
    other = lax.dynamic_slice_in_dim(partial, (1 - place) * half, half, 0)
    got = lax.ppermute(other.astype(jnp.bfloat16), "src", perm=[(0, 1), (1, 0)])
    return (mine.astype(jnp.bfloat16).astype(jnp.float32) + got.astype(jnp.float32)).astype(jnp.bfloat16)


def tile_major(x):
    comps, points, width = x.shape
    return jnp.transpose(x.reshape(comps, points, width // TILE, TILE), (2, 0, 1, 3))


def tile_minor(x):
    tiles, comps, points, width = x.shape
    return jnp.transpose(x, (1, 2, 0, 3)).reshape(comps, points, tiles * width)


def per_device(focus_direct, u_factors, v_factors, tile_ranks, onset_rec, onset_src):
    parts = lax.axis_size("freq")
    place = lax.axis_index("freq")
    u_fac = u_factors[0]
    v_fac = v_factors[0]
    col_tiles = u_fac.shape[0]
    row_tiles = v_fac.shape[0]
    u_tiles = u_fac.reshape(col_tiles, 2, RANK, row_tiles, TILE)
    v_tiles = v_fac.reshape(row_tiles, 2, RANK, col_tiles, TILE)
    rank_index = jnp.arange(RANK, dtype=jnp.int32)
    mask = (rank_index[None, None, :] < tile_ranks[0][:, :, None])[:, None]
    rec_tiles = onset_rec.shape[1] // TILE
    points = focus_direct.shape[2]
    chains = CHAINS if points % (8 * CHAINS) == 0 else 1
    each = points // chains
    rec_picked = []
    src_picked = []
    direct = []
    for c in range(chains):
        cut = slice(c * each, (c + 1) * each)
        rec_picked.append(window_gather(parts, onset_pieces(onset_rec[cut], rec_tiles, parts, place)))
        src_picked.append(window_gather(parts, onset_pieces(onset_src[cut], col_tiles, parts, place)))
        direct.append(tile_major(focus_direct[0][:, cut]))
    plus = list(direct)
    minus = [None] * chains
    for sweep in range(ITERS):
        for c in range(chains):
            z_real, z_imag = coefficients(v_tiles, mask, plus[c])
            partial_terms = expand_rows(u_tiles, z_real, z_imag)
            summed = reduce_src(partial_terms)
            traces = exchange(summed, parts)
            windowed = window(traces, rec_picked[c])
            minus[c] = exchange_back(windowed, rec_tiles, parts)
            minus_all = gather_src(minus[c])
            adjoint = adjoint_local(u_tiles, v_tiles, mask, minus_all)
            source_traces = exchange(adjoint.astype(jnp.bfloat16), parts)
            src_windowed = window(source_traces, src_picked[c])
            returned = exchange_back(src_windowed, col_tiles, parts).astype(jnp.float32)
            plus[c] = (direct[c].astype(jnp.float32) + returned).astype(jnp.bfloat16)
    plus_out = jnp.concatenate([tile_minor(p) for p in plus], axis=1)
    minus_out = jnp.concatenate([tile_minor(m) for m in minus], axis=1)
    return (plus_out[None], minus_out[None])


def solution(mesh):
    placed = (
        P("freq", None, ("groups", "vp"), "src"),
        P("freq", "src", None, None, None),
        P("freq", None, None, None, "src"),
        P("freq", None, "src"),
        P(("groups", "vp"), "src"),
        P(("groups", "vp"), "src"),
    )
    return jax.shard_map(
        per_device,
        mesh=mesh,
        in_specs=placed,
        out_specs=(
            P("freq", None, ("groups", "vp"), "src"),
            P("freq", None, ("groups", "vp"), "src"),
        ),
        check_vma=False,
    )
```

```python
import math

import jax
import jax.numpy as jnp
from jax import lax
from jax.experimental import pallas as pl
from jax.sharding import PartitionSpec as P

TILE = 256
RANK = 32
NT = 256
FLO = 8
ITERS = 2
GATHER_MAX = 4


def make_tables(count):
    index = FLO + jnp.arange(count, dtype=jnp.int32)
    sample = jnp.arange(NT, dtype=jnp.int32)
    phase = (index[:, None] * sample[None, :] % NT).astype(jnp.float32) * (2.0 * math.pi / NT)
    cosine = jnp.cos(phase)
    sine = jnp.sin(phase)
    inverse = jnp.stack([cosine, -sine]) * (2.0 / NT)
    forward = jnp.stack([cosine, -sine])
    return (inverse, forward)


def gather_kernel(table_ref, onset_ref, out_ref):
    rows = onset_ref.shape[1]
    width = onset_ref.shape[2]
    size = out_ref.shape[0]
    sample = lax.broadcasted_iota(jnp.int32, (NT, width), 0)
    for row in range(rows):
        place = jnp.clip(onset_ref[0, row : row + 1, :], 0, NT) - 1
        pick = (sample == place).astype(jnp.bfloat16)
        parts = jnp.dot(table_ref[...], pick, preferred_element_type=jnp.float32)
        out_ref[:, 0, row, :] = parts[:size] + parts[size:]


def window_gather(count, onset):
    if count > GATHER_MAX:
        return onset
    inverse, forward = make_tables(count)
    terms = jnp.einsum("cft,dgt->tgdfc", forward, inverse, precision=lax.Precision.HIGHEST)
    size = 4 * count * count
    table = jnp.cumsum(terms.reshape(NT, size), axis=0)
    high = table.astype(jnp.bfloat16)
    rest = table - high.astype(jnp.float32)
    low = rest.astype(jnp.bfloat16)
    stacked = jnp.concatenate([high, low], axis=1).T
    blocks, points, width = onset.shape
    rows = 8
    return pl.pallas_call(
        gather_kernel,
        grid=(blocks, points // rows),
        in_specs=[
            pl.BlockSpec((2 * size, NT), lambda b, r: (0, 0)),
            pl.BlockSpec((1, rows, width), lambda b, r: (b, r, 0)),
        ],
        out_specs=pl.BlockSpec((size, 1, rows, width), lambda b, r: (0, b, r, 0)),
        out_shape=jax.ShapeDtypeStruct((size, blocks, points, width), jnp.float32),
    )(stacked, onset)


def window_kernel(matrix_ref, spectrum_ref, out_ref):
    count = spectrum_ref.shape[0]
    comps = 2 * count
    source = [spectrum_ref[q // 2, 0, q % 2].astype(jnp.float32) for q in range(comps)]
    for target in range(comps):
        total = matrix_ref[target, 0] * source[0]
        for q in range(1, comps):
            total = total + matrix_ref[q * comps + target, 0] * source[q]
        out_ref[target // 2, 0, target % 2] = total.astype(out_ref.dtype)


def window(spectrum, picked):
    count = spectrum.shape[0]
    if count > GATHER_MAX:
        inverse, forward = make_tables(count)
        signal = jnp.einsum(
            "fbcvm,cft->bvmt", spectrum.astype(jnp.float32), inverse, precision=lax.Precision.HIGHEST
        )
        keep = lax.broadcasted_iota(jnp.int32, signal.shape, 3) < picked[..., None]
        signal = jnp.where(keep, signal, jnp.zeros_like(signal))
        result = jnp.einsum("bvmt,cft->fbcvm", signal, forward, precision=lax.Precision.HIGHEST)
        return result.astype(jnp.bfloat16)
    _, blocks, comps, points, width = spectrum.shape
    size = picked.shape[0]
    return pl.pallas_call(
        window_kernel,
        grid=(blocks,),
        in_specs=[
            pl.BlockSpec((size, 1, points, width), lambda b: (0, b, 0, 0)),
            pl.BlockSpec((count, 1, comps, points, width), lambda b: (0, b, 0, 0, 0)),
        ],
        out_specs=pl.BlockSpec((count, 1, comps, points, width), lambda b: (0, b, 0, 0, 0)),
        out_shape=jax.ShapeDtypeStruct(spectrum.shape, jnp.bfloat16),
    )(picked, spectrum)


def piece_count(tiles, parts):
    return parts // math.gcd(tiles, parts)


def to_pieces(x, parts):
    tiles, comps, points, width = x.shape
    k = piece_count(tiles, parts)
    if k == 1:
        return x
    x = x.reshape(tiles, comps, points, k, width // k)
    return jnp.transpose(x, (0, 3, 1, 2, 4)).reshape(tiles * k, comps, points, width // k)


def from_pieces(x, tiles):
    count, comps, points, width = x.shape
    k = count // tiles
    if k == 1:
        return x
    x = x.reshape(tiles, k, comps, points, width)
    return jnp.transpose(x, (0, 2, 3, 1, 4)).reshape(tiles, comps, points, k * width)


def onset_pieces(onset, tiles, parts, place):
    points = onset.shape[0]
    k = piece_count(tiles, parts)
    blocks = tiles * k
    each = blocks // parts
    split = onset.reshape(points, blocks, TILE // k)
    split = jnp.transpose(split, (1, 0, 2))
    return lax.dynamic_slice_in_dim(split, place * each, each, 0)


def exchange(x, parts):
    tiles = x.shape[0]
    pieces = to_pieces(x, parts)
    got = lax.all_to_all(pieces, "freq", split_axis=0, concat_axis=0, tiled=True)
    return got.reshape((parts, got.shape[0] // parts) + got.shape[1:])


def exchange_back(y, tiles):
    flat = y.reshape((y.shape[0] * y.shape[1],) + y.shape[2:])
    got = lax.all_to_all(flat, "freq", split_axis=0, concat_axis=0, tiled=True)
    return from_pieces(got, tiles)


def coefficients(v_tiles, mask, plus):
    form = "irjt,jvt->ivjr"
    p_re = plus[:, 0]
    p_im = plus[:, 1]
    z_real = jnp.einsum(
        form, v_tiles[:, 0], p_re, preferred_element_type=jnp.float32
    ) + jnp.einsum(form, v_tiles[:, 1], p_im, preferred_element_type=jnp.float32)
    z_imag = jnp.einsum(
        form, v_tiles[:, 0], p_im, preferred_element_type=jnp.float32
    ) - jnp.einsum(form, v_tiles[:, 1], p_re, preferred_element_type=jnp.float32)
    z_real = jnp.where(mask, z_real, 0.0).astype(jnp.bfloat16)
    z_imag = jnp.where(mask, z_imag, 0.0).astype(jnp.bfloat16)
    return z_real, z_imag


def expand_rows(u_tiles, z_real, z_imag):
    other = "jrit,ivjr->ivt"
    y_real = jnp.einsum(
        other, u_tiles[:, 0], z_real, preferred_element_type=jnp.float32
    ) - jnp.einsum(other, u_tiles[:, 1], z_imag, preferred_element_type=jnp.float32)
    y_imag = jnp.einsum(
        other, u_tiles[:, 0], z_imag, preferred_element_type=jnp.float32
    ) + jnp.einsum(other, u_tiles[:, 1], z_real, preferred_element_type=jnp.float32)
    return jnp.stack([y_real, y_imag], axis=1)


def adjoint_local(u_tiles, v_tiles, mask, minus):
    form = "jrit,ivt->ivjr"
    m_re = minus[:, 0]
    m_im = minus[:, 1]
    w_real = jnp.einsum(
        form, u_tiles[:, 0], m_re, preferred_element_type=jnp.float32
    ) + jnp.einsum(form, u_tiles[:, 1], m_im, preferred_element_type=jnp.float32)
    w_imag = jnp.einsum(
        form, u_tiles[:, 0], m_im, preferred_element_type=jnp.float32
    ) - jnp.einsum(form, u_tiles[:, 1], m_re, preferred_element_type=jnp.float32)
    w_real = jnp.where(mask, w_real, 0.0).astype(jnp.bfloat16)
    w_imag = jnp.where(mask, w_imag, 0.0).astype(jnp.bfloat16)
    other = "irjt,ivjr->jvt"
    x_real = jnp.einsum(
        other, v_tiles[:, 0], w_real, preferred_element_type=jnp.float32
    ) - jnp.einsum(other, v_tiles[:, 1], w_imag, preferred_element_type=jnp.float32)
    x_imag = jnp.einsum(
        other, v_tiles[:, 0], w_imag, preferred_element_type=jnp.float32
    ) + jnp.einsum(other, v_tiles[:, 1], w_real, preferred_element_type=jnp.float32)
    return jnp.stack([x_real, x_imag], axis=1)


def reduce_src(partial):
    count = lax.axis_size("src")
    if count != 2:
        return lax.psum_scatter(
            partial.astype(jnp.bfloat16), "src", scatter_dimension=0, tiled=True
        )
    place = lax.axis_index("src")
    half = partial.shape[0] // 2
    mine = lax.dynamic_slice_in_dim(partial, place * half, half, 0)
    other = lax.dynamic_slice_in_dim(partial, (1 - place) * half, half, 0)
    got = lax.ppermute(other.astype(jnp.bfloat16), "src", perm=[(0, 1), (1, 0)])
    return (mine.astype(jnp.bfloat16).astype(jnp.float32) + got.astype(jnp.float32)).astype(jnp.bfloat16)


def tile_major(x):
    comps, points, width = x.shape
    return jnp.transpose(x.reshape(comps, points, width // TILE, TILE), (2, 0, 1, 3))


def tile_minor(x):
    tiles, comps, points, width = x.shape
    return jnp.transpose(x, (1, 2, 0, 3)).reshape(comps, points, tiles * width)


def per_device(focus_direct, u_factors, v_factors, tile_ranks, onset_rec, onset_src):
    parts = lax.axis_size("freq")
    place = lax.axis_index("freq")
    u_fac = u_factors[0]
    v_fac = v_factors[0]
    col_tiles = u_fac.shape[0]
    row_tiles = v_fac.shape[0]
    u_tiles = u_fac.reshape(col_tiles, 2, RANK, row_tiles, TILE)
    v_tiles = v_fac.reshape(row_tiles, 2, RANK, col_tiles, TILE)
    rank_index = jnp.arange(RANK, dtype=jnp.int32)
    mask = (rank_index[None, None, :] < tile_ranks[0][:, :, None])[:, None]
    rec_tiles = onset_rec.shape[1] // TILE
    rec_picked = window_gather(parts, onset_pieces(onset_rec, rec_tiles, parts, place))
    src_picked = window_gather(parts, onset_pieces(onset_src, col_tiles, parts, place))
    direct = tile_major(focus_direct[0])
    direct_f32 = direct.astype(jnp.float32)
    plus = direct
    minus = None
    for sweep in range(ITERS):
        z_real, z_imag = coefficients(v_tiles, mask, plus)
        partial_terms = expand_rows(u_tiles, z_real, z_imag)
        summed = reduce_src(partial_terms)
        traces = exchange(summed, parts)
        windowed = window(traces, rec_picked)
        minus = exchange_back(windowed, rec_tiles)
        minus_all = lax.all_gather(minus, "src", axis=0, tiled=True)
        adjoint = adjoint_local(u_tiles, v_tiles, mask, minus_all)
        source_traces = exchange(adjoint.astype(jnp.bfloat16), parts)
        src_windowed = window(source_traces, src_picked)
        returned = exchange_back(src_windowed, col_tiles).astype(jnp.float32)
        plus = (direct_f32 + returned).astype(jnp.bfloat16)
    return (tile_minor(plus)[None], tile_minor(minus)[None])


def solution(mesh):
    placed = (
        P("freq", None, ("groups", "vp"), "src"),
        P("freq", "src", None, None, None),
        P("freq", None, None, None, "src"),
        P("freq", None, "src"),
        P(("groups", "vp"), "src"),
        P(("groups", "vp"), "src"),
    )
    return jax.shard_map(
        per_device,
        mesh=mesh,
        in_specs=placed,
        out_specs=(
            P("freq", None, ("groups", "vp"), "src"),
            P("freq", None, ("groups", "vp"), "src"),
        ),
        check_vma=False,
    )
```

```python
import math

import jax
import jax.numpy as jnp
from jax import lax
from jax.experimental import pallas as pl
from jax.sharding import PartitionSpec as P

TILE = 256
RANK = 32
NT = 256
FLO = 8
ITERS = 2
GATHER_MAX = 4
PERMUTE_MAX = 1
CHAINS = 2


def make_tables(count):
    index = FLO + jnp.arange(count, dtype=jnp.int32)
    sample = jnp.arange(NT, dtype=jnp.int32)
    phase = (index[:, None] * sample[None, :] % NT).astype(jnp.float32) * (2.0 * math.pi / NT)
    cosine = jnp.cos(phase)
    sine = jnp.sin(phase)
    inverse = jnp.stack([cosine, -sine]) * (2.0 / NT)
    forward = jnp.stack([cosine, -sine])
    return (inverse, forward)


def gather_kernel(table_ref, onset_ref, out_ref):
    rows = onset_ref.shape[1]
    width = onset_ref.shape[2]
    size = out_ref.shape[0]
    sample = lax.broadcasted_iota(jnp.int32, (NT, width), 0)
    for row in range(rows):
        place = jnp.clip(onset_ref[0, row : row + 1, :], 0, NT) - 1
        pick = (sample == place).astype(jnp.bfloat16)
        parts = jnp.dot(table_ref[...], pick, preferred_element_type=jnp.float32)
        out_ref[:, 0, row, :] = parts[:size] + parts[size:]


def window_gather(count, onset):
    if count > GATHER_MAX:
        return onset
    inverse, forward = make_tables(count)
    terms = jnp.einsum("cft,dgt->tgdfc", forward, inverse, precision=lax.Precision.HIGHEST)
    size = 4 * count * count
    table = jnp.cumsum(terms.reshape(NT, size), axis=0)
    high = table.astype(jnp.bfloat16)
    rest = table - high.astype(jnp.float32)
    low = rest.astype(jnp.bfloat16)
    stacked = jnp.concatenate([high, low], axis=1).T
    blocks, points, width = onset.shape
    rows = 8
    return pl.pallas_call(
        gather_kernel,
        grid=(blocks, points // rows),
        in_specs=[
            pl.BlockSpec((2 * size, NT), lambda b, r: (0, 0)),
            pl.BlockSpec((1, rows, width), lambda b, r: (b, r, 0)),
        ],
        out_specs=pl.BlockSpec((size, 1, rows, width), lambda b, r: (0, b, r, 0)),
        out_shape=jax.ShapeDtypeStruct((size, blocks, points, width), jnp.float32),
    )(stacked, onset)


def window_kernel(matrix_ref, spectrum_ref, out_ref):
    count = spectrum_ref.shape[0]
    comps = 2 * count
    source = [spectrum_ref[q // 2, 0, q % 2].astype(jnp.float32) for q in range(comps)]
    for target in range(comps):
        total = matrix_ref[target, 0] * source[0]
        for q in range(1, comps):
            total = total + matrix_ref[q * comps + target, 0] * source[q]
        out_ref[target // 2, 0, target % 2] = total.astype(out_ref.dtype)


def window(spectrum, picked):
    count = spectrum.shape[0]
    if count > GATHER_MAX:
        inverse, forward = make_tables(count)
        signal = jnp.einsum(
            "fbcvm,cft->bvmt", spectrum.astype(jnp.float32), inverse, precision=lax.Precision.HIGHEST
        )
        keep = lax.broadcasted_iota(jnp.int32, signal.shape, 3) < picked[..., None]
        signal = jnp.where(keep, signal, jnp.zeros_like(signal))
        result = jnp.einsum("bvmt,cft->fbcvm", signal, forward, precision=lax.Precision.HIGHEST)
        return result.astype(jnp.bfloat16)
    _, blocks, comps, points, width = spectrum.shape
    size = picked.shape[0]
    return pl.pallas_call(
        window_kernel,
        grid=(blocks,),
        in_specs=[
            pl.BlockSpec((size, 1, points, width), lambda b: (0, b, 0, 0)),
            pl.BlockSpec((count, 1, comps, points, width), lambda b: (0, b, 0, 0, 0)),
        ],
        out_specs=pl.BlockSpec((count, 1, comps, points, width), lambda b: (0, b, 0, 0, 0)),
        out_shape=jax.ShapeDtypeStruct(spectrum.shape, jnp.bfloat16),
    )(picked, spectrum)


def piece_count(tiles, parts):
    return parts // math.gcd(tiles, parts)


def to_pieces(x, parts):
    tiles, comps, points, width = x.shape
    k = piece_count(tiles, parts)
    if k == 1:
        return x
    x = x.reshape(tiles, comps, points, k, width // k)
    return jnp.transpose(x, (0, 3, 1, 2, 4)).reshape(tiles * k, comps, points, width // k)


def from_pieces(x, tiles):
    count, comps, points, width = x.shape
    k = count // tiles
    if k == 1:
        return x
    x = x.reshape(tiles, k, comps, points, width)
    return jnp.transpose(x, (0, 2, 3, 1, 4)).reshape(tiles, comps, points, k * width)


def onset_pieces(onset, tiles, parts, place):
    points = onset.shape[0]
    k = piece_count(tiles, parts)
    blocks = tiles * k
    each = blocks // parts
    split = onset.reshape(points, blocks, TILE // k)
    split = jnp.transpose(split, (1, 0, 2))
    return lax.dynamic_slice_in_dim(split, place * each, each, 0)


def swap_blocks(x, parts):
    if parts == 1:
        return x
    if parts > PERMUTE_MAX:
        return lax.all_to_all(x, "freq", split_axis=0, concat_axis=0, tiled=True)
    place = lax.axis_index("freq")
    each = x.shape[0] // parts
    blocks = x.reshape((parts, each) + x.shape[1:])
    got = [lax.dynamic_index_in_dim(blocks, place, 0, keepdims=False)]
    for shift in range(1, parts):
        send = lax.dynamic_index_in_dim(blocks, (place + shift) % parts, 0, keepdims=False)
        got.append(lax.ppermute(send, "freq", perm=[(i, (i + shift) % parts) for i in range(parts)]))
    stacked = jnp.stack(got)
    order = (place - jnp.arange(parts, dtype=jnp.int32)) % parts
    return jnp.take(stacked, order, axis=0).reshape(x.shape)


def gather_src(x):
    count = lax.axis_size("src")
    if count != 2 or PERMUTE_MAX < 2:
        return lax.all_gather(x, "src", axis=0, tiled=True)
    place = lax.axis_index("src")
    got = lax.ppermute(x, "src", perm=[(0, 1), (1, 0)])
    pair = jnp.stack([x, got])
    order = jnp.stack([place, 1 - place])
    return jnp.take(pair, order, axis=0).reshape((2 * x.shape[0],) + x.shape[1:])


def exchange(x, parts):
    tiles = x.shape[0]
    pieces = to_pieces(x, parts)
    got = swap_blocks(pieces, parts)
    return got.reshape((parts, got.shape[0] // parts) + got.shape[1:])


def exchange_back(y, tiles, parts):
    flat = y.reshape((y.shape[0] * y.shape[1],) + y.shape[2:])
    got = swap_blocks(flat, parts)
    return from_pieces(got, tiles)


def coefficients(v_tiles, mask, plus):
    form = "irjt,jvt->ivjr"
    p_re = plus[:, 0]
    p_im = plus[:, 1]
    z_real = jnp.einsum(
        form, v_tiles[:, 0], p_re, preferred_element_type=jnp.float32
    ) + jnp.einsum(form, v_tiles[:, 1], p_im, preferred_element_type=jnp.float32)
    z_imag = jnp.einsum(
        form, v_tiles[:, 0], p_im, preferred_element_type=jnp.float32
    ) - jnp.einsum(form, v_tiles[:, 1], p_re, preferred_element_type=jnp.float32)
    z_real = jnp.where(mask, z_real, 0.0).astype(jnp.bfloat16)
    z_imag = jnp.where(mask, z_imag, 0.0).astype(jnp.bfloat16)
    return z_real, z_imag


def expand_rows(u_tiles, z_real, z_imag):
    other = "jrit,ivjr->ivt"
    y_real = jnp.einsum(
        other, u_tiles[:, 0], z_real, preferred_element_type=jnp.float32
    ) - jnp.einsum(other, u_tiles[:, 1], z_imag, preferred_element_type=jnp.float32)
    y_imag = jnp.einsum(
        other, u_tiles[:, 0], z_imag, preferred_element_type=jnp.float32
    ) + jnp.einsum(other, u_tiles[:, 1], z_real, preferred_element_type=jnp.float32)
    return jnp.stack([y_real, y_imag], axis=1)


def adjoint_local(u_tiles, v_tiles, mask, minus):
    form = "jrit,ivt->ivjr"
    m_re = minus[:, 0]
    m_im = minus[:, 1]
    w_real = jnp.einsum(
        form, u_tiles[:, 0], m_re, preferred_element_type=jnp.float32
    ) + jnp.einsum(form, u_tiles[:, 1], m_im, preferred_element_type=jnp.float32)
    w_imag = jnp.einsum(
        form, u_tiles[:, 0], m_im, preferred_element_type=jnp.float32
    ) - jnp.einsum(form, u_tiles[:, 1], m_re, preferred_element_type=jnp.float32)
    w_real = jnp.where(mask, w_real, 0.0).astype(jnp.bfloat16)
    w_imag = jnp.where(mask, w_imag, 0.0).astype(jnp.bfloat16)
    other = "irjt,ivjr->jvt"
    x_real = jnp.einsum(
        other, v_tiles[:, 0], w_real, preferred_element_type=jnp.float32
    ) - jnp.einsum(other, v_tiles[:, 1], w_imag, preferred_element_type=jnp.float32)
    x_imag = jnp.einsum(
        other, v_tiles[:, 0], w_imag, preferred_element_type=jnp.float32
    ) + jnp.einsum(other, v_tiles[:, 1], w_real, preferred_element_type=jnp.float32)
    return jnp.stack([x_real, x_imag], axis=1)


def reduce_src(partial):
    count = lax.axis_size("src")
    if count != 2:
        return lax.psum_scatter(
            partial.astype(jnp.bfloat16), "src", scatter_dimension=0, tiled=True
        )
    place = lax.axis_index("src")
    half = partial.shape[0] // 2
    mine = lax.dynamic_slice_in_dim(partial, place * half, half, 0)
    other = lax.dynamic_slice_in_dim(partial, (1 - place) * half, half, 0)
    got = lax.ppermute(other.astype(jnp.bfloat16), "src", perm=[(0, 1), (1, 0)])
    return (mine.astype(jnp.bfloat16).astype(jnp.float32) + got.astype(jnp.float32)).astype(jnp.bfloat16)


def tile_major(x):
    comps, points, width = x.shape
    return jnp.transpose(x.reshape(comps, points, width // TILE, TILE), (2, 0, 1, 3))


def tile_minor(x):
    tiles, comps, points, width = x.shape
    return jnp.transpose(x, (1, 2, 0, 3)).reshape(comps, points, tiles * width)


def per_device(focus_direct, u_factors, v_factors, tile_ranks, onset_rec, onset_src):
    parts = lax.axis_size("freq")
    place = lax.axis_index("freq")
    u_fac = u_factors[0]
    v_fac = v_factors[0]
    col_tiles = u_fac.shape[0]
    row_tiles = v_fac.shape[0]
    u_tiles = u_fac.reshape(col_tiles, 2, RANK, row_tiles, TILE)
    v_tiles = v_fac.reshape(row_tiles, 2, RANK, col_tiles, TILE)
    rank_index = jnp.arange(RANK, dtype=jnp.int32)
    mask = (rank_index[None, None, :] < tile_ranks[0][:, :, None])[:, None]
    rec_tiles = onset_rec.shape[1] // TILE
    points = focus_direct.shape[2]
    chains = CHAINS if points % (8 * CHAINS) == 0 else 1
    each = points // chains
    rec_picked = []
    src_picked = []
    direct = []
    for c in range(chains):
        cut = slice(c * each, (c + 1) * each)
        rec_picked.append(window_gather(parts, onset_pieces(onset_rec[cut], rec_tiles, parts, place)))
        src_picked.append(window_gather(parts, onset_pieces(onset_src[cut], col_tiles, parts, place)))
        direct.append(tile_major(focus_direct[0][:, cut]))
    plus = list(direct)
    minus = [None] * chains
    for sweep in range(ITERS):
        for c in range(chains):
            z_real, z_imag = coefficients(v_tiles, mask, plus[c])
            partial_terms = expand_rows(u_tiles, z_real, z_imag)
            summed = reduce_src(partial_terms)
            traces = exchange(summed, parts)
            windowed = window(traces, rec_picked[c])
            minus[c] = exchange_back(windowed, rec_tiles, parts)
            minus_all = gather_src(minus[c])
            adjoint = adjoint_local(u_tiles, v_tiles, mask, minus_all)
            source_traces = exchange(adjoint.astype(jnp.bfloat16), parts)
            src_windowed = window(source_traces, src_picked[c])
            returned = exchange_back(src_windowed, col_tiles, parts).astype(jnp.float32)
            plus[c] = (direct[c].astype(jnp.float32) + returned).astype(jnp.bfloat16)
    plus_out = jnp.concatenate([tile_minor(p) for p in plus], axis=1)
    minus_out = jnp.concatenate([tile_minor(m) for m in minus], axis=1)
    return (plus_out[None], minus_out[None])


def solution(mesh):
    placed = (
        P("freq", None, ("groups", "vp"), "src"),
        P("freq", "src", None, None, None),
        P("freq", None, None, None, "src"),
        P("freq", None, "src"),
        P(("groups", "vp"), "src"),
        P(("groups", "vp"), "src"),
    )
    return jax.shard_map(
        per_device,
        mesh=mesh,
        in_specs=placed,
        out_specs=(
            P("freq", None, ("groups", "vp"), "src"),
            P("freq", None, ("groups", "vp"), "src"),
        ),
        check_vma=False,
    )
```

```python
import math

import jax
import jax.numpy as jnp
from jax import lax
from jax.experimental import pallas as pl
from jax.sharding import PartitionSpec as P

TILE = 256
RANK = 32
NT = 256
FLO = 8
ITERS = 2
GATHER_MAX = 4


def make_tables(count):
    index = FLO + jnp.arange(count, dtype=jnp.int32)
    sample = jnp.arange(NT, dtype=jnp.int32)
    phase = (index[:, None] * sample[None, :] % NT).astype(jnp.float32) * (2.0 * math.pi / NT)
    cosine = jnp.cos(phase)
    sine = jnp.sin(phase)
    inverse = jnp.stack([cosine, -sine]) * (2.0 / NT)
    forward = jnp.stack([cosine, -sine])
    return (inverse, forward)


def gather_kernel(table_ref, onset_ref, out_ref):
    rows = onset_ref.shape[1]
    width = onset_ref.shape[2]
    size = out_ref.shape[0]
    sample = lax.broadcasted_iota(jnp.int32, (NT, width), 0)
    for row in range(rows):
        place = jnp.clip(onset_ref[0, row : row + 1, :], 0, NT) - 1
        pick = (sample == place).astype(jnp.bfloat16)
        parts = jnp.dot(table_ref[...], pick, preferred_element_type=jnp.float32)
        out_ref[:, 0, row, :] = parts[:size] + parts[size:]


def window_gather(count, onset):
    if count > GATHER_MAX:
        return onset
    inverse, forward = make_tables(count)
    terms = jnp.einsum("cft,dgt->tgdfc", forward, inverse, precision=lax.Precision.HIGHEST)
    size = 4 * count * count
    table = jnp.cumsum(terms.reshape(NT, size), axis=0)
    high = table.astype(jnp.bfloat16)
    rest = table - high.astype(jnp.float32)
    low = rest.astype(jnp.bfloat16)
    stacked = jnp.concatenate([high, low], axis=1).T
    blocks, points, width = onset.shape
    rows = 8
    return pl.pallas_call(
        gather_kernel,
        grid=(blocks, points // rows),
        in_specs=[
            pl.BlockSpec((2 * size, NT), lambda b, r: (0, 0)),
            pl.BlockSpec((1, rows, width), lambda b, r: (b, r, 0)),
        ],
        out_specs=pl.BlockSpec((size, 1, rows, width), lambda b, r: (0, b, r, 0)),
        out_shape=jax.ShapeDtypeStruct((size, blocks, points, width), jnp.float32),
    )(stacked, onset)


def window_kernel(matrix_ref, spectrum_ref, out_ref):
    count = spectrum_ref.shape[0]
    comps = 2 * count
    source = [spectrum_ref[q // 2, 0, q % 2].astype(jnp.float32) for q in range(comps)]
    for target in range(comps):
        total = matrix_ref[target, 0] * source[0]
        for q in range(1, comps):
            total = total + matrix_ref[q * comps + target, 0] * source[q]
        out_ref[target // 2, 0, target % 2] = total.astype(out_ref.dtype)


def window(spectrum, picked):
    count = spectrum.shape[0]
    if count > GATHER_MAX:
        inverse, forward = make_tables(count)
        signal = jnp.einsum(
            "fbcvm,cft->bvmt", spectrum.astype(jnp.float32), inverse, precision=lax.Precision.HIGHEST
        )
        keep = lax.broadcasted_iota(jnp.int32, signal.shape, 3) < picked[..., None]
        signal = jnp.where(keep, signal, jnp.zeros_like(signal))
        result = jnp.einsum("bvmt,cft->fbcvm", signal, forward, precision=lax.Precision.HIGHEST)
        return result.astype(jnp.bfloat16)
    _, blocks, comps, points, width = spectrum.shape
    size = picked.shape[0]
    return pl.pallas_call(
        window_kernel,
        grid=(blocks,),
        in_specs=[
            pl.BlockSpec((size, 1, points, width), lambda b: (0, b, 0, 0)),
            pl.BlockSpec((count, 1, comps, points, width), lambda b: (0, b, 0, 0, 0)),
        ],
        out_specs=pl.BlockSpec((count, 1, comps, points, width), lambda b: (0, b, 0, 0, 0)),
        out_shape=jax.ShapeDtypeStruct(spectrum.shape, jnp.bfloat16),
    )(picked, spectrum)


def piece_count(tiles, parts):
    return parts // math.gcd(tiles, parts)


def to_pieces(x, parts):
    tiles, comps, points, width = x.shape
    k = piece_count(tiles, parts)
    if k == 1:
        return x
    x = x.reshape(tiles, comps, points, k, width // k)
    return jnp.transpose(x, (0, 3, 1, 2, 4)).reshape(tiles * k, comps, points, width // k)


def from_pieces(x, tiles):
    count, comps, points, width = x.shape
    k = count // tiles
    if k == 1:
        return x
    x = x.reshape(tiles, k, comps, points, width)
    return jnp.transpose(x, (0, 2, 3, 1, 4)).reshape(tiles, comps, points, k * width)


def onset_pieces(onset, tiles, parts, place):
    points = onset.shape[0]
    k = piece_count(tiles, parts)
    blocks = tiles * k
    each = blocks // parts
    split = onset.reshape(points, blocks, TILE // k)
    split = jnp.transpose(split, (1, 0, 2))
    return lax.dynamic_slice_in_dim(split, place * each, each, 0)


def exchange(x, parts):
    tiles = x.shape[0]
    pieces = to_pieces(x, parts)
    got = lax.all_to_all(pieces, "freq", split_axis=0, concat_axis=0, tiled=True)
    return got.reshape((parts, got.shape[0] // parts) + got.shape[1:])


def exchange_back(y, tiles):
    flat = y.reshape((y.shape[0] * y.shape[1],) + y.shape[2:])
    got = lax.all_to_all(flat, "freq", split_axis=0, concat_axis=0, tiled=True)
    return from_pieces(got, tiles)


def coefficients(v_tiles, mask, plus):
    form = "irjt,jvt->ivjr"
    p_re = plus[:, 0]
    p_im = plus[:, 1]
    z_real = jnp.einsum(
        form, v_tiles[:, 0], p_re, preferred_element_type=jnp.float32
    ) + jnp.einsum(form, v_tiles[:, 1], p_im, preferred_element_type=jnp.float32)
    z_imag = jnp.einsum(
        form, v_tiles[:, 0], p_im, preferred_element_type=jnp.float32
    ) - jnp.einsum(form, v_tiles[:, 1], p_re, preferred_element_type=jnp.float32)
    z_real = jnp.where(mask, z_real, 0.0).astype(jnp.bfloat16)
    z_imag = jnp.where(mask, z_imag, 0.0).astype(jnp.bfloat16)
    return z_real, z_imag


def expand_rows(u_tiles, z_real, z_imag):
    other = "jrit,ivjr->ivt"
    y_real = jnp.einsum(
        other, u_tiles[:, 0], z_real, preferred_element_type=jnp.float32
    ) - jnp.einsum(other, u_tiles[:, 1], z_imag, preferred_element_type=jnp.float32)
    y_imag = jnp.einsum(
        other, u_tiles[:, 0], z_imag, preferred_element_type=jnp.float32
    ) + jnp.einsum(other, u_tiles[:, 1], z_real, preferred_element_type=jnp.float32)
    return jnp.stack([y_real, y_imag], axis=1)


def adjoint_local(u_tiles, v_tiles, mask, minus):
    form = "jrit,ivt->ivjr"
    m_re = minus[:, 0]
    m_im = minus[:, 1]
    w_real = jnp.einsum(
        form, u_tiles[:, 0], m_re, preferred_element_type=jnp.float32
    ) + jnp.einsum(form, u_tiles[:, 1], m_im, preferred_element_type=jnp.float32)
    w_imag = jnp.einsum(
        form, u_tiles[:, 0], m_im, preferred_element_type=jnp.float32
    ) - jnp.einsum(form, u_tiles[:, 1], m_re, preferred_element_type=jnp.float32)
    w_real = jnp.where(mask, w_real, 0.0).astype(jnp.bfloat16)
    w_imag = jnp.where(mask, w_imag, 0.0).astype(jnp.bfloat16)
    other = "irjt,ivjr->jvt"
    x_real = jnp.einsum(
        other, v_tiles[:, 0], w_real, preferred_element_type=jnp.float32
    ) - jnp.einsum(other, v_tiles[:, 1], w_imag, preferred_element_type=jnp.float32)
    x_imag = jnp.einsum(
        other, v_tiles[:, 0], w_imag, preferred_element_type=jnp.float32
    ) + jnp.einsum(other, v_tiles[:, 1], w_real, preferred_element_type=jnp.float32)
    return jnp.stack([x_real, x_imag], axis=1)


def reduce_src(partial):
    count = lax.axis_size("src")
    if count != 2:
        return lax.psum_scatter(
            partial.astype(jnp.bfloat16), "src", scatter_dimension=0, tiled=True
        )
    place = lax.axis_index("src")
    half = partial.shape[0] // 2
    mine = lax.dynamic_slice_in_dim(partial, place * half, half, 0)
    other = lax.dynamic_slice_in_dim(partial, (1 - place) * half, half, 0)
    got = lax.ppermute(other.astype(jnp.bfloat16), "src", perm=[(0, 1), (1, 0)])
    return (mine.astype(jnp.bfloat16).astype(jnp.float32) + got.astype(jnp.float32)).astype(jnp.bfloat16)


def tile_major(x):
    comps, points, width = x.shape
    return jnp.transpose(x.reshape(comps, points, width // TILE, TILE), (2, 0, 1, 3))


def tile_minor(x):
    tiles, comps, points, width = x.shape
    return jnp.transpose(x, (1, 2, 0, 3)).reshape(comps, points, tiles * width)


def per_device(focus_direct, u_factors, v_factors, tile_ranks, onset_rec, onset_src):
    parts = lax.axis_size("freq")
    place = lax.axis_index("freq")
    u_fac = u_factors[0]
    v_fac = v_factors[0]
    col_tiles = u_fac.shape[0]
    row_tiles = v_fac.shape[0]
    u_tiles = u_fac.reshape(col_tiles, 2, RANK, row_tiles, TILE)
    v_tiles = v_fac.reshape(row_tiles, 2, RANK, col_tiles, TILE)
    rank_index = jnp.arange(RANK, dtype=jnp.int32)
    mask = (rank_index[None, None, :] < tile_ranks[0][:, :, None])[:, None]
    rec_tiles = onset_rec.shape[1] // TILE
    rec_picked = window_gather(parts, onset_pieces(onset_rec, rec_tiles, parts, place))
    src_picked = window_gather(parts, onset_pieces(onset_src, col_tiles, parts, place))
    direct = tile_major(focus_direct[0])
    direct_f32 = direct.astype(jnp.float32)

    def sweep(_, state):
        plus, _ = state
        z_real, z_imag = coefficients(v_tiles, mask, plus)
        partial_terms = expand_rows(u_tiles, z_real, z_imag)
        summed = reduce_src(partial_terms)
        traces = exchange(summed, parts)
        windowed = window(traces, rec_picked)
        minus = exchange_back(windowed, rec_tiles)
        minus_all = lax.all_gather(minus, "src", axis=0, tiled=True)
        adjoint = adjoint_local(u_tiles, v_tiles, mask, minus_all)
        source_traces = exchange(adjoint.astype(jnp.bfloat16), parts)
        src_windowed = window(source_traces, src_picked)
        returned = exchange_back(src_windowed, col_tiles).astype(jnp.float32)
        return ((direct_f32 + returned).astype(jnp.bfloat16), minus)

    start = jnp.zeros((rec_tiles,) + direct.shape[1:], jnp.bfloat16)
    plus, minus = lax.fori_loop(0, ITERS, sweep, (direct, start))
    return (tile_minor(plus)[None], tile_minor(minus)[None])


def solution(mesh):
    placed = (
        P("freq", None, ("groups", "vp"), "src"),
        P("freq", "src", None, None, None),
        P("freq", None, None, None, "src"),
        P("freq", None, "src"),
        P(("groups", "vp"), "src"),
        P(("groups", "vp"), "src"),
    )
    return jax.shard_map(
        per_device,
        mesh=mesh,
        in_specs=placed,
        out_specs=(
            P("freq", None, ("groups", "vp"), "src"),
            P("freq", None, ("groups", "vp"), "src"),
        ),
        check_vma=False,
    )
```

```python
import math

import jax
import jax.numpy as jnp
from jax import lax
from jax.experimental import pallas as pl
from jax.sharding import PartitionSpec as P

TILE = 256
RANK = 32
NT = 256
FLO = 8
ITERS = 2
GATHER_MAX = 4


def make_tables(count):
    index = FLO + jnp.arange(count, dtype=jnp.int32)
    sample = jnp.arange(NT, dtype=jnp.int32)
    phase = (index[:, None] * sample[None, :] % NT).astype(jnp.float32) * (2.0 * math.pi / NT)
    cosine = jnp.cos(phase)
    sine = jnp.sin(phase)
    inverse = jnp.stack([cosine, -sine]) * (2.0 / NT)
    forward = jnp.stack([cosine, -sine])
    return (inverse, forward)


def gather_kernel(table_ref, onset_ref, out_ref):
    rows = onset_ref.shape[1]
    width = onset_ref.shape[2]
    sample = lax.broadcasted_iota(jnp.int32, (NT, width), 0)
    for row in range(rows):
        place = jnp.clip(onset_ref[0, row : row + 1, :], 0, NT) - 1
        pick = (sample == place).astype(jnp.bfloat16)
        parts = jnp.dot(table_ref[...], pick, preferred_element_type=jnp.float32)
        out_ref[:, 0, row, :] = parts.astype(out_ref.dtype)


def window_gather(count, onset):
    if count > GATHER_MAX:
        return onset
    inverse, forward = make_tables(count)
    terms = jnp.einsum("cft,dgt->tgdfc", forward, inverse, precision=lax.Precision.HIGHEST)
    size = 4 * count * count
    table = jnp.cumsum(terms.reshape(NT, size), axis=0)
    stacked = table.astype(jnp.bfloat16).T
    blocks, points, width = onset.shape
    rows = 8
    return pl.pallas_call(
        gather_kernel,
        grid=(blocks, points // rows),
        in_specs=[
            pl.BlockSpec((size, NT), lambda b, r: (0, 0)),
            pl.BlockSpec((1, rows, width), lambda b, r: (b, r, 0)),
        ],
        out_specs=pl.BlockSpec((size, 1, rows, width), lambda b, r: (0, b, r, 0)),
        out_shape=jax.ShapeDtypeStruct((size, blocks, points, width), jnp.bfloat16),
    )(stacked, onset)


def window_kernel(matrix_ref, spectrum_ref, out_ref):
    count = spectrum_ref.shape[0]
    comps = 2 * count
    source = [spectrum_ref[q // 2, 0, q % 2].astype(jnp.float32) for q in range(comps)]
    for target in range(comps):
        total = matrix_ref[target, 0].astype(jnp.float32) * source[0]
        for q in range(1, comps):
            total = total + matrix_ref[q * comps + target, 0].astype(jnp.float32) * source[q]
        out_ref[target // 2, 0, target % 2] = total.astype(out_ref.dtype)


def window(spectrum, picked):
    count = spectrum.shape[0]
    if count > GATHER_MAX:
        inverse, forward = make_tables(count)
        signal = jnp.einsum(
            "fbcvm,cft->bvmt", spectrum.astype(jnp.float32), inverse, precision=lax.Precision.HIGHEST
        )
        keep = lax.broadcasted_iota(jnp.int32, signal.shape, 3) < picked[..., None]
        signal = jnp.where(keep, signal, jnp.zeros_like(signal))
        result = jnp.einsum("bvmt,cft->fbcvm", signal, forward, precision=lax.Precision.HIGHEST)
        return result.astype(jnp.bfloat16)
    _, blocks, comps, points, width = spectrum.shape
    size = picked.shape[0]
    rows = 16 if points % 16 == 0 else points
    return pl.pallas_call(
        window_kernel,
        grid=(blocks, points // rows),
        in_specs=[
            pl.BlockSpec((size, 1, rows, width), lambda b, r: (0, b, r, 0)),
            pl.BlockSpec((count, 1, comps, rows, width), lambda b, r: (0, b, 0, r, 0)),
        ],
        out_specs=pl.BlockSpec((count, 1, comps, rows, width), lambda b, r: (0, b, 0, r, 0)),
        out_shape=jax.ShapeDtypeStruct(spectrum.shape, jnp.bfloat16),
    )(picked, spectrum)


def piece_count(tiles, parts):
    return parts // math.gcd(tiles, parts)


def to_pieces(x, parts):
    tiles, comps, points, width = x.shape
    k = piece_count(tiles, parts)
    if k == 1:
        return x
    x = x.reshape(tiles, comps, points, k, width // k)
    return jnp.transpose(x, (0, 3, 1, 2, 4)).reshape(tiles * k, comps, points, width // k)


def from_pieces(x, tiles):
    count, comps, points, width = x.shape
    k = count // tiles
    if k == 1:
        return x
    x = x.reshape(tiles, k, comps, points, width)
    return jnp.transpose(x, (0, 2, 3, 1, 4)).reshape(tiles, comps, points, k * width)


def onset_pieces(onset, tiles, parts, place):
    points = onset.shape[0]
    k = piece_count(tiles, parts)
    blocks = tiles * k
    each = blocks // parts
    split = onset.reshape(points, blocks, TILE // k)
    split = jnp.transpose(split, (1, 0, 2))
    return lax.dynamic_slice_in_dim(split, place * each, each, 0)


def exchange(x, parts):
    tiles = x.shape[0]
    pieces = to_pieces(x, parts)
    got = lax.all_to_all(pieces, "freq", split_axis=0, concat_axis=0, tiled=True)
    return got.reshape((parts, got.shape[0] // parts) + got.shape[1:])


def exchange_back(y, tiles):
    flat = y.reshape((y.shape[0] * y.shape[1],) + y.shape[2:])
    got = lax.all_to_all(flat, "freq", split_axis=0, concat_axis=0, tiled=True)
    return from_pieces(got, tiles)


def coefficients(v_tiles, mask, plus):
    form = "irjt,jvt->ivjr"
    p_re = plus[:, 0]
    p_im = plus[:, 1]
    z_real = jnp.einsum(
        form, v_tiles[:, 0], p_re, preferred_element_type=jnp.float32
    ) + jnp.einsum(form, v_tiles[:, 1], p_im, preferred_element_type=jnp.float32)
    z_imag = jnp.einsum(
        form, v_tiles[:, 0], p_im, preferred_element_type=jnp.float32
    ) - jnp.einsum(form, v_tiles[:, 1], p_re, preferred_element_type=jnp.float32)
    z_real = jnp.where(mask, z_real, 0.0).astype(jnp.bfloat16)
    z_imag = jnp.where(mask, z_imag, 0.0).astype(jnp.bfloat16)
    return z_real, z_imag


def expand_rows(u_tiles, z_real, z_imag):
    other = "jrit,ivjr->ivt"
    y_real = jnp.einsum(
        other, u_tiles[:, 0], z_real, preferred_element_type=jnp.float32
    ) - jnp.einsum(other, u_tiles[:, 1], z_imag, preferred_element_type=jnp.float32)
    y_imag = jnp.einsum(
        other, u_tiles[:, 0], z_imag, preferred_element_type=jnp.float32
    ) + jnp.einsum(other, u_tiles[:, 1], z_real, preferred_element_type=jnp.float32)
    return jnp.stack([y_real, y_imag], axis=1)


def adjoint_local(u_tiles, v_tiles, mask, minus):
    form = "jrit,ivt->ivjr"
    m_re = minus[:, 0]
    m_im = minus[:, 1]
    w_real = jnp.einsum(
        form, u_tiles[:, 0], m_re, preferred_element_type=jnp.float32
    ) + jnp.einsum(form, u_tiles[:, 1], m_im, preferred_element_type=jnp.float32)
    w_imag = jnp.einsum(
        form, u_tiles[:, 0], m_im, preferred_element_type=jnp.float32
    ) - jnp.einsum(form, u_tiles[:, 1], m_re, preferred_element_type=jnp.float32)
    w_real = jnp.where(mask, w_real, 0.0).astype(jnp.bfloat16)
    w_imag = jnp.where(mask, w_imag, 0.0).astype(jnp.bfloat16)
    other = "irjt,ivjr->jvt"
    x_real = jnp.einsum(
        other, v_tiles[:, 0], w_real, preferred_element_type=jnp.float32
    ) - jnp.einsum(other, v_tiles[:, 1], w_imag, preferred_element_type=jnp.float32)
    x_imag = jnp.einsum(
        other, v_tiles[:, 0], w_imag, preferred_element_type=jnp.float32
    ) + jnp.einsum(other, v_tiles[:, 1], w_real, preferred_element_type=jnp.float32)
    return jnp.stack([x_real, x_imag], axis=1)


def reduce_src(partial):
    count = lax.axis_size("src")
    if count != 2:
        return lax.psum_scatter(
            partial.astype(jnp.bfloat16), "src", scatter_dimension=0, tiled=True
        )
    place = lax.axis_index("src")
    half = partial.shape[0] // 2
    mine = lax.dynamic_slice_in_dim(partial, place * half, half, 0)
    other = lax.dynamic_slice_in_dim(partial, (1 - place) * half, half, 0)
    got = lax.ppermute(other.astype(jnp.bfloat16), "src", perm=[(0, 1), (1, 0)])
    return (mine.astype(jnp.bfloat16).astype(jnp.float32) + got.astype(jnp.float32)).astype(jnp.bfloat16)


def tile_major(x):
    comps, points, width = x.shape
    return jnp.transpose(x.reshape(comps, points, width // TILE, TILE), (2, 0, 1, 3))


def tile_minor(x):
    tiles, comps, points, width = x.shape
    return jnp.transpose(x, (1, 2, 0, 3)).reshape(comps, points, tiles * width)


def per_device(focus_direct, u_factors, v_factors, tile_ranks, onset_rec, onset_src):
    parts = lax.axis_size("freq")
    place = lax.axis_index("freq")
    u_fac = u_factors[0]
    v_fac = v_factors[0]
    col_tiles = u_fac.shape[0]
    row_tiles = v_fac.shape[0]
    u_tiles = u_fac.reshape(col_tiles, 2, RANK, row_tiles, TILE)
    v_tiles = v_fac.reshape(row_tiles, 2, RANK, col_tiles, TILE)
    rank_index = jnp.arange(RANK, dtype=jnp.int32)
    mask = (rank_index[None, None, :] < tile_ranks[0][:, :, None])[:, None]
    rec_tiles = onset_rec.shape[1] // TILE
    rec_picked = window_gather(parts, onset_pieces(onset_rec, rec_tiles, parts, place))
    src_picked = window_gather(parts, onset_pieces(onset_src, col_tiles, parts, place))
    direct = tile_major(focus_direct[0])
    direct_f32 = direct.astype(jnp.float32)
    plus = direct
    minus = None
    for sweep in range(ITERS):
        z_real, z_imag = coefficients(v_tiles, mask, plus)
        partial_terms = expand_rows(u_tiles, z_real, z_imag)
        summed = reduce_src(partial_terms)
        traces = exchange(summed, parts)
        windowed = window(traces, rec_picked)
        minus = exchange_back(windowed, rec_tiles)
        minus_all = lax.all_gather(minus, "src", axis=0, tiled=True)
        adjoint = adjoint_local(u_tiles, v_tiles, mask, minus_all)
        source_traces = exchange(adjoint.astype(jnp.bfloat16), parts)
        src_windowed = window(source_traces, src_picked)
        returned = exchange_back(src_windowed, col_tiles).astype(jnp.float32)
        plus = (direct_f32 + returned).astype(jnp.bfloat16)
    return (tile_minor(plus)[None], tile_minor(minus)[None])


def solution(mesh):
    placed = (
        P("freq", None, ("groups", "vp"), "src"),
        P("freq", "src", None, None, None),
        P("freq", None, None, None, "src"),
        P("freq", None, "src"),
        P(("groups", "vp"), "src"),
        P(("groups", "vp"), "src"),
    )
    return jax.shard_map(
        per_device,
        mesh=mesh,
        in_specs=placed,
        out_specs=(
            P("freq", None, ("groups", "vp"), "src"),
            P("freq", None, ("groups", "vp"), "src"),
        ),
        check_vma=False,
    )
```

```python
import math

import jax
import jax.numpy as jnp
from jax import lax
from jax.experimental import pallas as pl
from jax.sharding import PartitionSpec as P

TILE = 256
RANK = 32
NT = 256
FLO = 8
ITERS = 2
GATHER_MAX = 4


def make_tables(count):
    index = FLO + jnp.arange(count, dtype=jnp.int32)
    sample = jnp.arange(NT, dtype=jnp.int32)
    phase = (index[:, None] * sample[None, :] % NT).astype(jnp.float32) * (2.0 * math.pi / NT)
    cosine = jnp.cos(phase)
    sine = jnp.sin(phase)
    inverse = jnp.stack([cosine, -sine]) * (2.0 / NT)
    forward = jnp.stack([cosine, -sine])
    return (inverse, forward)


def gather_kernel(table_ref, onset_ref, out_ref):
    rows = onset_ref.shape[1]
    width = onset_ref.shape[2]
    size = out_ref.shape[0]
    sample = lax.broadcasted_iota(jnp.int32, (NT, width), 0)
    for row in range(rows):
        place = jnp.clip(onset_ref[0, row : row + 1, :], 0, NT) - 1
        pick = (sample == place).astype(jnp.bfloat16)
        parts = jnp.dot(table_ref[...], pick, preferred_element_type=jnp.float32)
        out_ref[:, 0, row, :] = parts[:size] + parts[size:]


def window_gather(count, onset):
    if count > GATHER_MAX:
        return onset
    inverse, forward = make_tables(count)
    terms = jnp.einsum("cft,dgt->tgdfc", forward, inverse, precision=lax.Precision.HIGHEST)
    size = 4 * count * count
    table = jnp.cumsum(terms.reshape(NT, size), axis=0)
    high = table.astype(jnp.bfloat16)
    rest = table - high.astype(jnp.float32)
    low = rest.astype(jnp.bfloat16)
    stacked = jnp.concatenate([high, low], axis=1).T
    blocks, points, width = onset.shape
    rows = 8
    return pl.pallas_call(
        gather_kernel,
        grid=(blocks, points // rows),
        in_specs=[
            pl.BlockSpec((2 * size, NT), lambda b, r: (0, 0)),
            pl.BlockSpec((1, rows, width), lambda b, r: (b, r, 0)),
        ],
        out_specs=pl.BlockSpec((size, 1, rows, width), lambda b, r: (0, b, r, 0)),
        out_shape=jax.ShapeDtypeStruct((size, blocks, points, width), jnp.float32),
    )(stacked, onset)


def window_kernel(matrix_ref, spectrum_ref, out_ref):
    count = spectrum_ref.shape[0]
    comps = 2 * count
    source = [spectrum_ref[q // 2, 0, q % 2].astype(jnp.float32) for q in range(comps)]
    for target in range(comps):
        total = matrix_ref[target, 0] * source[0]
        for q in range(1, comps):
            total = total + matrix_ref[q * comps + target, 0] * source[q]
        out_ref[target // 2, 0, target % 2] = total.astype(out_ref.dtype)


def window(spectrum, picked):
    count = spectrum.shape[0]
    if count > GATHER_MAX:
        inverse, forward = make_tables(count)
        signal = jnp.einsum(
            "fbcvm,cft->bvmt", spectrum.astype(jnp.float32), inverse, precision=lax.Precision.HIGHEST
        )
        keep = lax.broadcasted_iota(jnp.int32, signal.shape, 3) < picked[..., None]
        signal = jnp.where(keep, signal, jnp.zeros_like(signal))
        result = jnp.einsum("bvmt,cft->fbcvm", signal, forward, precision=lax.Precision.HIGHEST)
        return result.astype(jnp.bfloat16)
    _, blocks, comps, points, width = spectrum.shape
    size = picked.shape[0]
    return pl.pallas_call(
        window_kernel,
        grid=(blocks,),
        in_specs=[
            pl.BlockSpec((size, 1, points, width), lambda b: (0, b, 0, 0)),
            pl.BlockSpec((count, 1, comps, points, width), lambda b: (0, b, 0, 0, 0)),
        ],
        out_specs=pl.BlockSpec((count, 1, comps, points, width), lambda b: (0, b, 0, 0, 0)),
        out_shape=jax.ShapeDtypeStruct(spectrum.shape, jnp.bfloat16),
    )(picked, spectrum)


def piece_count(tiles, parts):
    return parts // math.gcd(tiles, parts)


def to_pieces(x, parts):
    tiles, comps, points, width = x.shape
    k = piece_count(tiles, parts)
    if k == 1:
        return x
    x = x.reshape(tiles, comps, points, k, width // k)
    return jnp.transpose(x, (0, 3, 1, 2, 4)).reshape(tiles * k, comps, points, width // k)


def from_pieces(x, tiles):
    count, comps, points, width = x.shape
    k = count // tiles
    if k == 1:
        return x
    x = x.reshape(tiles, k, comps, points, width)
    return jnp.transpose(x, (0, 2, 3, 1, 4)).reshape(tiles, comps, points, k * width)


def onset_pieces(onset, tiles, parts, place):
    points = onset.shape[0]
    k = piece_count(tiles, parts)
    blocks = tiles * k
    each = blocks // parts
    split = onset.reshape(points, blocks, TILE // k)
    split = jnp.transpose(split, (1, 0, 2))
    return lax.dynamic_slice_in_dim(split, place * each, each, 0)


def exchange(x, parts):
    tiles = x.shape[0]
    pieces = to_pieces(x, parts)
    got = lax.all_to_all(pieces, "freq", split_axis=0, concat_axis=0, tiled=True)
    return got.reshape((parts, got.shape[0] // parts) + got.shape[1:])


def exchange_back(y, tiles):
    flat = y.reshape((y.shape[0] * y.shape[1],) + y.shape[2:])
    got = lax.all_to_all(flat, "freq", split_axis=0, concat_axis=0, tiled=True)
    return from_pieces(got, tiles)


def rec_exchange(partial, parts):
    count = lax.axis_size("src")
    half = partial.shape[0] // count
    split = partial.astype(jnp.bfloat16).reshape((count, half) + partial.shape[1:])
    pieces = jnp.stack([to_pieces(split[s], parts) for s in range(count)])
    each = pieces.shape[1] // parts
    pieces = pieces.reshape((count, parts, each) + pieces.shape[2:])
    send = jnp.swapaxes(pieces, 0, 1).reshape((parts * count * each,) + pieces.shape[3:])
    got = lax.all_to_all(send, ("freq", "src"), 0, 0, tiled=True)
    got = got.reshape((parts, count, each) + got.shape[1:]).astype(jnp.float32)
    return jnp.sum(got, axis=1).astype(jnp.bfloat16)


def rec_back(windowed, half):
    count = lax.axis_size("src")
    parts, each = windowed.shape[:2]
    rest = windowed.shape[2:]
    send = jnp.broadcast_to(windowed[:, None], (parts, count, each) + rest)
    got = lax.all_to_all(send.reshape((parts * count * each,) + rest), ("freq", "src"), 0, 0, tiled=True)
    got = got.reshape((parts, count, each) + rest)
    halves = [from_pieces(got[:, s].reshape((parts * each,) + rest), half) for s in range(count)]
    every = jnp.concatenate(halves, axis=0)
    own = lax.dynamic_slice_in_dim(every, lax.axis_index("src") * half, half, 0)
    return own, every


def coefficients(v_tiles, mask, plus):
    form = "irjt,jvt->ivjr"
    p_re = plus[:, 0]
    p_im = plus[:, 1]
    z_real = jnp.einsum(
        form, v_tiles[:, 0], p_re, preferred_element_type=jnp.float32
    ) + jnp.einsum(form, v_tiles[:, 1], p_im, preferred_element_type=jnp.float32)
    z_imag = jnp.einsum(
        form, v_tiles[:, 0], p_im, preferred_element_type=jnp.float32
    ) - jnp.einsum(form, v_tiles[:, 1], p_re, preferred_element_type=jnp.float32)
    z_real = jnp.where(mask, z_real, 0.0).astype(jnp.bfloat16)
    z_imag = jnp.where(mask, z_imag, 0.0).astype(jnp.bfloat16)
    return z_real, z_imag


def expand_rows(u_tiles, z_real, z_imag):
    other = "jrit,ivjr->ivt"
    y_real = jnp.einsum(
        other, u_tiles[:, 0], z_real, preferred_element_type=jnp.float32
    ) - jnp.einsum(other, u_tiles[:, 1], z_imag, preferred_element_type=jnp.float32)
    y_imag = jnp.einsum(
        other, u_tiles[:, 0], z_imag, preferred_element_type=jnp.float32
    ) + jnp.einsum(other, u_tiles[:, 1], z_real, preferred_element_type=jnp.float32)
    return jnp.stack([y_real, y_imag], axis=1)


def adjoint_local(u_tiles, v_tiles, mask, minus):
    form = "jrit,ivt->ivjr"
    m_re = minus[:, 0]
    m_im = minus[:, 1]
    w_real = jnp.einsum(
        form, u_tiles[:, 0], m_re, preferred_element_type=jnp.float32
    ) + jnp.einsum(form, u_tiles[:, 1], m_im, preferred_element_type=jnp.float32)
    w_imag = jnp.einsum(
        form, u_tiles[:, 0], m_im, preferred_element_type=jnp.float32
    ) - jnp.einsum(form, u_tiles[:, 1], m_re, preferred_element_type=jnp.float32)
    w_real = jnp.where(mask, w_real, 0.0).astype(jnp.bfloat16)
    w_imag = jnp.where(mask, w_imag, 0.0).astype(jnp.bfloat16)
    other = "irjt,ivjr->jvt"
    x_real = jnp.einsum(
        other, v_tiles[:, 0], w_real, preferred_element_type=jnp.float32
    ) - jnp.einsum(other, v_tiles[:, 1], w_imag, preferred_element_type=jnp.float32)
    x_imag = jnp.einsum(
        other, v_tiles[:, 0], w_imag, preferred_element_type=jnp.float32
    ) + jnp.einsum(other, v_tiles[:, 1], w_real, preferred_element_type=jnp.float32)
    return jnp.stack([x_real, x_imag], axis=1)


def reduce_src(partial):
    count = lax.axis_size("src")
    if count != 2:
        return lax.psum_scatter(
            partial.astype(jnp.bfloat16), "src", scatter_dimension=0, tiled=True
        )
    place = lax.axis_index("src")
    half = partial.shape[0] // 2
    mine = lax.dynamic_slice_in_dim(partial, place * half, half, 0)
    other = lax.dynamic_slice_in_dim(partial, (1 - place) * half, half, 0)
    got = lax.ppermute(other.astype(jnp.bfloat16), "src", perm=[(0, 1), (1, 0)])
    return (mine.astype(jnp.bfloat16).astype(jnp.float32) + got.astype(jnp.float32)).astype(jnp.bfloat16)


def tile_major(x):
    comps, points, width = x.shape
    return jnp.transpose(x.reshape(comps, points, width // TILE, TILE), (2, 0, 1, 3))


def tile_minor(x):
    tiles, comps, points, width = x.shape
    return jnp.transpose(x, (1, 2, 0, 3)).reshape(comps, points, tiles * width)


def per_device(focus_direct, u_factors, v_factors, tile_ranks, onset_rec, onset_src):
    parts = lax.axis_size("freq")
    place = lax.axis_index("freq")
    u_fac = u_factors[0]
    v_fac = v_factors[0]
    col_tiles = u_fac.shape[0]
    row_tiles = v_fac.shape[0]
    u_tiles = u_fac.reshape(col_tiles, 2, RANK, row_tiles, TILE)
    v_tiles = v_fac.reshape(row_tiles, 2, RANK, col_tiles, TILE)
    rank_index = jnp.arange(RANK, dtype=jnp.int32)
    mask = (rank_index[None, None, :] < tile_ranks[0][:, :, None])[:, None]
    rec_tiles = onset_rec.shape[1] // TILE
    rec_picked = window_gather(parts, onset_pieces(onset_rec, rec_tiles, parts, place))
    src_picked = window_gather(parts, onset_pieces(onset_src, col_tiles, parts, place))
    direct = tile_major(focus_direct[0])
    direct_f32 = direct.astype(jnp.float32)
    plus = direct
    minus = None
    for sweep in range(ITERS):
        z_real, z_imag = coefficients(v_tiles, mask, plus)
        partial_terms = expand_rows(u_tiles, z_real, z_imag)
        traces = rec_exchange(partial_terms, parts)
        windowed = window(traces, rec_picked)
        minus, minus_all = rec_back(windowed, rec_tiles)
        adjoint = adjoint_local(u_tiles, v_tiles, mask, minus_all)
        source_traces = exchange(adjoint.astype(jnp.bfloat16), parts)
        src_windowed = window(source_traces, src_picked)
        returned = exchange_back(src_windowed, col_tiles).astype(jnp.float32)
        plus = (direct_f32 + returned).astype(jnp.bfloat16)
    return (tile_minor(plus)[None], tile_minor(minus)[None])


def solution(mesh):
    placed = (
        P("freq", None, ("groups", "vp"), "src"),
        P("freq", "src", None, None, None),
        P("freq", None, None, None, "src"),
        P("freq", None, "src"),
        P(("groups", "vp"), "src"),
        P(("groups", "vp"), "src"),
    )
    return jax.shard_map(
        per_device,
        mesh=mesh,
        in_specs=placed,
        out_specs=(
            P("freq", None, ("groups", "vp"), "src"),
            P("freq", None, ("groups", "vp"), "src"),
        ),
        check_vma=False,
    )
```

```python
import math

import jax
import jax.numpy as jnp
from jax import lax
from jax.experimental import pallas as pl
from jax.sharding import PartitionSpec as P

TILE = 256
RANK = 32
NT = 256
FLO = 8
ITERS = 2
GATHER_MAX = 4


def make_tables(count):
    index = FLO + jnp.arange(count, dtype=jnp.int32)
    sample = jnp.arange(NT, dtype=jnp.int32)
    phase = (index[:, None] * sample[None, :] % NT).astype(jnp.float32) * (2.0 * math.pi / NT)
    cosine = jnp.cos(phase)
    sine = jnp.sin(phase)
    inverse = jnp.stack([cosine, -sine]) * (2.0 / NT)
    forward = jnp.stack([cosine, -sine])
    return (inverse, forward)


def gather_kernel(table_ref, onset_ref, out_ref):
    rows = onset_ref.shape[1]
    width = onset_ref.shape[2]
    size = out_ref.shape[0]
    sample = lax.broadcasted_iota(jnp.int32, (NT, width), 0)
    for row in range(rows):
        place = jnp.clip(onset_ref[0, row : row + 1, :], 0, NT) - 1
        pick = (sample == place).astype(jnp.bfloat16)
        parts = jnp.dot(table_ref[...], pick, preferred_element_type=jnp.float32)
        out_ref[:, 0, row, :] = parts[:size] + parts[size:]


def window_gather(count, onset):
    if count > GATHER_MAX:
        return onset
    inverse, forward = make_tables(count)
    terms = jnp.einsum("cft,dgt->tgdfc", forward, inverse, precision=lax.Precision.HIGHEST)
    size = 4 * count * count
    table = jnp.cumsum(terms.reshape(NT, size), axis=0)
    high = table.astype(jnp.bfloat16)
    rest = table - high.astype(jnp.float32)
    low = rest.astype(jnp.bfloat16)
    stacked = jnp.concatenate([high, low], axis=1).T
    blocks, points, width = onset.shape
    rows = 8
    return pl.pallas_call(
        gather_kernel,
        grid=(blocks, points // rows),
        in_specs=[
            pl.BlockSpec((2 * size, NT), lambda b, r: (0, 0)),
            pl.BlockSpec((1, rows, width), lambda b, r: (b, r, 0)),
        ],
        out_specs=pl.BlockSpec((size, 1, rows, width), lambda b, r: (0, b, r, 0)),
        out_shape=jax.ShapeDtypeStruct((size, blocks, points, width), jnp.float32),
    )(stacked, onset)


def window_kernel(matrix_ref, spectrum_ref, out_ref):
    count = spectrum_ref.shape[0]
    comps = 2 * count
    source = [spectrum_ref[q // 2, 0, q % 2].astype(jnp.float32) for q in range(comps)]
    for target in range(comps):
        total = matrix_ref[target, 0] * source[0]
        for q in range(1, comps):
            total = total + matrix_ref[q * comps + target, 0] * source[q]
        out_ref[target // 2, 0, target % 2] = total.astype(out_ref.dtype)


def window(spectrum, picked):
    count = spectrum.shape[0]
    if count > GATHER_MAX:
        inverse, forward = make_tables(count)
        signal = jnp.einsum(
            "fbcvm,cft->bvmt", spectrum.astype(jnp.float32), inverse, precision=lax.Precision.HIGHEST
        )
        keep = lax.broadcasted_iota(jnp.int32, signal.shape, 3) < picked[..., None]
        signal = jnp.where(keep, signal, jnp.zeros_like(signal))
        result = jnp.einsum("bvmt,cft->fbcvm", signal, forward, precision=lax.Precision.HIGHEST)
        return result.astype(jnp.bfloat16)
    _, blocks, comps, points, width = spectrum.shape
    size = picked.shape[0]
    return pl.pallas_call(
        window_kernel,
        grid=(blocks,),
        in_specs=[
            pl.BlockSpec((size, 1, points, width), lambda b: (0, b, 0, 0)),
            pl.BlockSpec((count, 1, comps, points, width), lambda b: (0, b, 0, 0, 0)),
        ],
        out_specs=pl.BlockSpec((count, 1, comps, points, width), lambda b: (0, b, 0, 0, 0)),
        out_shape=jax.ShapeDtypeStruct(spectrum.shape, jnp.bfloat16),
    )(picked, spectrum)


def piece_count(tiles, parts):
    return parts // math.gcd(tiles, parts)


def to_pieces(x, parts):
    tiles, comps, points, width = x.shape
    k = piece_count(tiles, parts)
    if k == 1:
        return x
    x = x.reshape(tiles, comps, points, k, width // k)
    return jnp.transpose(x, (0, 3, 1, 2, 4)).reshape(tiles * k, comps, points, width // k)


def from_pieces(x, tiles):
    count, comps, points, width = x.shape
    k = count // tiles
    if k == 1:
        return x
    x = x.reshape(tiles, k, comps, points, width)
    return jnp.transpose(x, (0, 2, 3, 1, 4)).reshape(tiles, comps, points, k * width)


def onset_pieces(onset, tiles, parts, place):
    points = onset.shape[0]
    k = piece_count(tiles, parts)
    blocks = tiles * k
    each = blocks // parts
    split = onset.reshape(points, blocks, TILE // k)
    split = jnp.transpose(split, (1, 0, 2))
    return lax.dynamic_slice_in_dim(split, place * each, each, 0)


def exchange(x, parts):
    tiles = x.shape[0]
    pieces = to_pieces(x, parts)
    got = lax.all_to_all(pieces, "freq", split_axis=0, concat_axis=0, tiled=True)
    return got.reshape((parts, got.shape[0] // parts) + got.shape[1:])


def exchange_back(y, tiles):
    flat = y.reshape((y.shape[0] * y.shape[1],) + y.shape[2:])
    got = lax.all_to_all(flat, "freq", split_axis=0, concat_axis=0, tiled=True)
    return from_pieces(got, tiles)


def coefficients(v_tiles, mask, plus):
    form = "irjt,jvt->ivjr"
    p_re = plus[:, 0]
    p_im = plus[:, 1]
    z_real = jnp.einsum(
        form, v_tiles[:, 0], p_re, preferred_element_type=jnp.float32
    ) + jnp.einsum(form, v_tiles[:, 1], p_im, preferred_element_type=jnp.float32)
    z_imag = jnp.einsum(
        form, v_tiles[:, 0], p_im, preferred_element_type=jnp.float32
    ) - jnp.einsum(form, v_tiles[:, 1], p_re, preferred_element_type=jnp.float32)
    z_real = jnp.where(mask, z_real, 0.0).astype(jnp.bfloat16)
    z_imag = jnp.where(mask, z_imag, 0.0).astype(jnp.bfloat16)
    return z_real, z_imag


def expand_rows(u_tiles, z_real, z_imag):
    other = "jrit,ivjr->ivt"
    y_real = jnp.einsum(
        other, u_tiles[:, 0], z_real, preferred_element_type=jnp.float32
    ) - jnp.einsum(other, u_tiles[:, 1], z_imag, preferred_element_type=jnp.float32)
    y_imag = jnp.einsum(
        other, u_tiles[:, 0], z_imag, preferred_element_type=jnp.float32
    ) + jnp.einsum(other, u_tiles[:, 1], z_real, preferred_element_type=jnp.float32)
    return jnp.stack([y_real, y_imag], axis=1)


def adjoint_local(u_tiles, v_tiles, mask, minus):
    form = "jrit,ivt->ivjr"
    m_re = minus[:, 0]
    m_im = minus[:, 1]
    w_real = jnp.einsum(
        form, u_tiles[:, 0], m_re, preferred_element_type=jnp.float32
    ) + jnp.einsum(form, u_tiles[:, 1], m_im, preferred_element_type=jnp.float32)
    w_imag = jnp.einsum(
        form, u_tiles[:, 0], m_im, preferred_element_type=jnp.float32
    ) - jnp.einsum(form, u_tiles[:, 1], m_re, preferred_element_type=jnp.float32)
    w_real = jnp.where(mask, w_real, 0.0).astype(jnp.bfloat16)
    w_imag = jnp.where(mask, w_imag, 0.0).astype(jnp.bfloat16)
    other = "irjt,ivjr->jvt"
    x_real = jnp.einsum(
        other, v_tiles[:, 0], w_real, preferred_element_type=jnp.float32
    ) - jnp.einsum(other, v_tiles[:, 1], w_imag, preferred_element_type=jnp.float32)
    x_imag = jnp.einsum(
        other, v_tiles[:, 0], w_imag, preferred_element_type=jnp.float32
    ) + jnp.einsum(other, v_tiles[:, 1], w_real, preferred_element_type=jnp.float32)
    return jnp.stack([x_real, x_imag], axis=1)


def reduce_src(partial):
    count = lax.axis_size("src")
    if count != 2:
        return lax.psum_scatter(
            partial.astype(jnp.bfloat16), "src", scatter_dimension=0, tiled=True
        )
    place = lax.axis_index("src")
    half = partial.shape[0] // 2
    mine = lax.dynamic_slice_in_dim(partial, place * half, half, 0)
    other = lax.dynamic_slice_in_dim(partial, (1 - place) * half, half, 0)
    got = lax.ppermute(other.astype(jnp.bfloat16), "src", perm=[(0, 1), (1, 0)])
    return (mine.astype(jnp.bfloat16).astype(jnp.float32) + got.astype(jnp.float32)).astype(jnp.bfloat16)


def gather_src(x):
    count = lax.axis_size("src")
    if count != 2:
        return lax.all_gather(x, "src", axis=0, tiled=True)
    place = lax.axis_index("src")
    got = lax.ppermute(x, "src", perm=[(0, 1), (1, 0)])
    pair = jnp.stack([x, got])
    order = jnp.stack([place, 1 - place])
    return jnp.take(pair, order, axis=0).reshape((2 * x.shape[0],) + x.shape[1:])


def tile_major(x):
    comps, points, width = x.shape
    return jnp.transpose(x.reshape(comps, points, width // TILE, TILE), (2, 0, 1, 3))


def tile_minor(x):
    tiles, comps, points, width = x.shape
    return jnp.transpose(x, (1, 2, 0, 3)).reshape(comps, points, tiles * width)


def per_device(focus_direct, u_factors, v_factors, tile_ranks, onset_rec, onset_src):
    parts = lax.axis_size("freq")
    place = lax.axis_index("freq")
    u_fac = u_factors[0]
    v_fac = v_factors[0]
    col_tiles = u_fac.shape[0]
    row_tiles = v_fac.shape[0]
    u_tiles = u_fac.reshape(col_tiles, 2, RANK, row_tiles, TILE)
    v_tiles = v_fac.reshape(row_tiles, 2, RANK, col_tiles, TILE)
    rank_index = jnp.arange(RANK, dtype=jnp.int32)
    mask = (rank_index[None, None, :] < tile_ranks[0][:, :, None])[:, None]
    rec_tiles = onset_rec.shape[1] // TILE
    rec_picked = window_gather(parts, onset_pieces(onset_rec, rec_tiles, parts, place))
    src_picked = window_gather(parts, onset_pieces(onset_src, col_tiles, parts, place))
    direct = tile_major(focus_direct[0])
    direct_f32 = direct.astype(jnp.float32)
    plus = direct
    minus = None
    for sweep in range(ITERS):
        z_real, z_imag = coefficients(v_tiles, mask, plus)
        partial_terms = expand_rows(u_tiles, z_real, z_imag)
        summed = reduce_src(partial_terms)
        traces = exchange(summed, parts)
        windowed = window(traces, rec_picked)
        minus = exchange_back(windowed, rec_tiles)
        minus_all = gather_src(minus)
        adjoint = adjoint_local(u_tiles, v_tiles, mask, minus_all)
        source_traces = exchange(adjoint.astype(jnp.bfloat16), parts)
        src_windowed = window(source_traces, src_picked)
        returned = exchange_back(src_windowed, col_tiles).astype(jnp.float32)
        plus = (direct_f32 + returned).astype(jnp.bfloat16)
    return (tile_minor(plus)[None], tile_minor(minus)[None])


def solution(mesh):
    placed = (
        P("freq", None, ("groups", "vp"), "src"),
        P("freq", "src", None, None, None),
        P("freq", None, None, None, "src"),
        P("freq", None, "src"),
        P(("groups", "vp"), "src"),
        P(("groups", "vp"), "src"),
    )
    return jax.shard_map(
        per_device,
        mesh=mesh,
        in_specs=placed,
        out_specs=(
            P("freq", None, ("groups", "vp"), "src"),
            P("freq", None, ("groups", "vp"), "src"),
        ),
        check_vma=False,
    )
```

```python
import math

import jax
import jax.numpy as jnp
from jax import lax
from jax.experimental import pallas as pl
from jax.sharding import PartitionSpec as P

TILE = 256
RANK = 32
NT = 256
FLO = 8
ITERS = 2
GATHER_MAX = 4


def make_tables(count):
    index = FLO + jnp.arange(count, dtype=jnp.int32)
    sample = jnp.arange(NT, dtype=jnp.int32)
    phase = (index[:, None] * sample[None, :] % NT).astype(jnp.float32) * (2.0 * math.pi / NT)
    cosine = jnp.cos(phase)
    sine = jnp.sin(phase)
    inverse = jnp.stack([cosine, -sine]) * (2.0 / NT)
    forward = jnp.stack([cosine, -sine])
    return (inverse, forward)


def gather_kernel(table_ref, onset_ref, out_ref):
    rows = onset_ref.shape[1]
    width = onset_ref.shape[2]
    size = out_ref.shape[0]
    sample = lax.broadcasted_iota(jnp.int32, (NT, width), 0)
    for row in range(rows):
        place = jnp.clip(onset_ref[0, row : row + 1, :], 0, NT) - 1
        pick = (sample == place).astype(jnp.bfloat16)
        parts = jnp.dot(table_ref[...], pick, preferred_element_type=jnp.float32)
        out_ref[:, 0, row, :] = parts[:size] + parts[size:]


def window_gather(count, onset):
    if count > GATHER_MAX:
        return onset
    inverse, forward = make_tables(count)
    terms = jnp.einsum("cft,dgt->tgdfc", forward, inverse, precision=lax.Precision.HIGHEST)
    size = 4 * count * count
    table = jnp.cumsum(terms.reshape(NT, size), axis=0)
    high = table.astype(jnp.bfloat16)
    rest = table - high.astype(jnp.float32)
    low = rest.astype(jnp.bfloat16)
    stacked = jnp.concatenate([high, low], axis=1).T
    blocks, points, width = onset.shape
    rows = 8
    return pl.pallas_call(
        gather_kernel,
        grid=(blocks, points // rows),
        in_specs=[
            pl.BlockSpec((2 * size, NT), lambda b, r: (0, 0)),
            pl.BlockSpec((1, rows, width), lambda b, r: (b, r, 0)),
        ],
        out_specs=pl.BlockSpec((size, 1, rows, width), lambda b, r: (0, b, r, 0)),
        out_shape=jax.ShapeDtypeStruct((size, blocks, points, width), jnp.float32),
    )(stacked, onset)


def window_kernel(matrix_ref, spectrum_ref, out_ref):
    count = spectrum_ref.shape[0]
    comps = 2 * count
    source = [spectrum_ref[q // 2, 0, q % 2].astype(jnp.float32) for q in range(comps)]
    for target in range(comps):
        total = matrix_ref[target, 0] * source[0]
        for q in range(1, comps):
            total = total + matrix_ref[q * comps + target, 0] * source[q]
        out_ref[target // 2, 0, target % 2] = total.astype(out_ref.dtype)


def window(spectrum, picked):
    count = spectrum.shape[0]
    if count > GATHER_MAX:
        inverse, forward = make_tables(count)
        signal = jnp.einsum(
            "fbcvm,cft->bvmt", spectrum.astype(jnp.float32), inverse, precision=lax.Precision.HIGHEST
        )
        keep = lax.broadcasted_iota(jnp.int32, signal.shape, 3) < picked[..., None]
        signal = jnp.where(keep, signal, jnp.zeros_like(signal))
        result = jnp.einsum("bvmt,cft->fbcvm", signal, forward, precision=lax.Precision.HIGHEST)
        return result.astype(jnp.bfloat16)
    _, blocks, comps, points, width = spectrum.shape
    size = picked.shape[0]
    rows = 24 if points % 24 == 0 else points
    return pl.pallas_call(
        window_kernel,
        grid=(blocks, points // rows),
        in_specs=[
            pl.BlockSpec((size, 1, rows, width), lambda b, r: (0, b, r, 0)),
            pl.BlockSpec((count, 1, comps, rows, width), lambda b, r: (0, b, 0, r, 0)),
        ],
        out_specs=pl.BlockSpec((count, 1, comps, rows, width), lambda b, r: (0, b, 0, r, 0)),
        out_shape=jax.ShapeDtypeStruct(spectrum.shape, jnp.bfloat16),
    )(picked, spectrum)


def piece_count(tiles, parts):
    return parts // math.gcd(tiles, parts)


def to_pieces(x, parts):
    tiles, comps, points, width = x.shape
    k = piece_count(tiles, parts)
    if k == 1:
        return x
    x = x.reshape(tiles, comps, points, k, width // k)
    return jnp.transpose(x, (0, 3, 1, 2, 4)).reshape(tiles * k, comps, points, width // k)


def from_pieces(x, tiles):
    count, comps, points, width = x.shape
    k = count // tiles
    if k == 1:
        return x
    x = x.reshape(tiles, k, comps, points, width)
    return jnp.transpose(x, (0, 2, 3, 1, 4)).reshape(tiles, comps, points, k * width)


def onset_pieces(onset, tiles, parts, place):
    points = onset.shape[0]
    k = piece_count(tiles, parts)
    blocks = tiles * k
    each = blocks // parts
    split = onset.reshape(points, blocks, TILE // k)
    split = jnp.transpose(split, (1, 0, 2))
    return lax.dynamic_slice_in_dim(split, place * each, each, 0)


def exchange(x, parts):
    tiles = x.shape[0]
    pieces = to_pieces(x, parts)
    got = lax.all_to_all(pieces, "freq", split_axis=0, concat_axis=0, tiled=True)
    return got.reshape((parts, got.shape[0] // parts) + got.shape[1:])


def exchange_back(y, tiles):
    flat = y.reshape((y.shape[0] * y.shape[1],) + y.shape[2:])
    got = lax.all_to_all(flat, "freq", split_axis=0, concat_axis=0, tiled=True)
    return from_pieces(got, tiles)


def coefficients(v_tiles, mask, plus):
    form = "irjt,jvt->ivjr"
    p_re = plus[:, 0]
    p_im = plus[:, 1]
    z_real = jnp.einsum(
        form, v_tiles[:, 0], p_re, preferred_element_type=jnp.float32
    ) + jnp.einsum(form, v_tiles[:, 1], p_im, preferred_element_type=jnp.float32)
    z_imag = jnp.einsum(
        form, v_tiles[:, 0], p_im, preferred_element_type=jnp.float32
    ) - jnp.einsum(form, v_tiles[:, 1], p_re, preferred_element_type=jnp.float32)
    z_real = jnp.where(mask, z_real, 0.0).astype(jnp.bfloat16)
    z_imag = jnp.where(mask, z_imag, 0.0).astype(jnp.bfloat16)
    return z_real, z_imag


def expand_rows(u_tiles, z_real, z_imag):
    other = "jrit,ivjr->ivt"
    y_real = jnp.einsum(
        other, u_tiles[:, 0], z_real, preferred_element_type=jnp.float32
    ) - jnp.einsum(other, u_tiles[:, 1], z_imag, preferred_element_type=jnp.float32)
    y_imag = jnp.einsum(
        other, u_tiles[:, 0], z_imag, preferred_element_type=jnp.float32
    ) + jnp.einsum(other, u_tiles[:, 1], z_real, preferred_element_type=jnp.float32)
    return jnp.stack([y_real, y_imag], axis=1)


def adjoint_local(u_tiles, v_tiles, mask, minus):
    form = "jrit,ivt->ivjr"
    m_re = minus[:, 0]
    m_im = minus[:, 1]
    w_real = jnp.einsum(
        form, u_tiles[:, 0], m_re, preferred_element_type=jnp.float32
    ) + jnp.einsum(form, u_tiles[:, 1], m_im, preferred_element_type=jnp.float32)
    w_imag = jnp.einsum(
        form, u_tiles[:, 0], m_im, preferred_element_type=jnp.float32
    ) - jnp.einsum(form, u_tiles[:, 1], m_re, preferred_element_type=jnp.float32)
    w_real = jnp.where(mask, w_real, 0.0).astype(jnp.bfloat16)
    w_imag = jnp.where(mask, w_imag, 0.0).astype(jnp.bfloat16)
    other = "irjt,ivjr->jvt"
    x_real = jnp.einsum(
        other, v_tiles[:, 0], w_real, preferred_element_type=jnp.float32
    ) - jnp.einsum(other, v_tiles[:, 1], w_imag, preferred_element_type=jnp.float32)
    x_imag = jnp.einsum(
        other, v_tiles[:, 0], w_imag, preferred_element_type=jnp.float32
    ) + jnp.einsum(other, v_tiles[:, 1], w_real, preferred_element_type=jnp.float32)
    return jnp.stack([x_real, x_imag], axis=1)


def reduce_src(partial):
    count = lax.axis_size("src")
    if count != 2:
        return lax.psum_scatter(
            partial.astype(jnp.bfloat16), "src", scatter_dimension=0, tiled=True
        )
    place = lax.axis_index("src")
    half = partial.shape[0] // 2
    mine = lax.dynamic_slice_in_dim(partial, place * half, half, 0)
    other = lax.dynamic_slice_in_dim(partial, (1 - place) * half, half, 0)
    got = lax.ppermute(other.astype(jnp.bfloat16), "src", perm=[(0, 1), (1, 0)])
    return (mine.astype(jnp.bfloat16).astype(jnp.float32) + got.astype(jnp.float32)).astype(jnp.bfloat16)


def tile_major(x):
    comps, points, width = x.shape
    return jnp.transpose(x.reshape(comps, points, width // TILE, TILE), (2, 0, 1, 3))


def tile_minor(x):
    tiles, comps, points, width = x.shape
    return jnp.transpose(x, (1, 2, 0, 3)).reshape(comps, points, tiles * width)


def per_device(focus_direct, u_factors, v_factors, tile_ranks, onset_rec, onset_src):
    parts = lax.axis_size("freq")
    place = lax.axis_index("freq")
    u_fac = u_factors[0]
    v_fac = v_factors[0]
    col_tiles = u_fac.shape[0]
    row_tiles = v_fac.shape[0]
    u_tiles = u_fac.reshape(col_tiles, 2, RANK, row_tiles, TILE)
    v_tiles = v_fac.reshape(row_tiles, 2, RANK, col_tiles, TILE)
    rank_index = jnp.arange(RANK, dtype=jnp.int32)
    mask = (rank_index[None, None, :] < tile_ranks[0][:, :, None])[:, None]
    rec_tiles = onset_rec.shape[1] // TILE
    rec_picked = window_gather(parts, onset_pieces(onset_rec, rec_tiles, parts, place))
    src_picked = window_gather(parts, onset_pieces(onset_src, col_tiles, parts, place))
    direct = tile_major(focus_direct[0])
    direct_f32 = direct.astype(jnp.float32)
    plus = direct
    minus = None
    for sweep in range(ITERS):
        z_real, z_imag = coefficients(v_tiles, mask, plus)
        partial_terms = expand_rows(u_tiles, z_real, z_imag)
        summed = reduce_src(partial_terms)
        traces = exchange(summed, parts)
        windowed = window(traces, rec_picked)
        minus = exchange_back(windowed, rec_tiles)
        minus_all = lax.all_gather(minus, "src", axis=0, tiled=True)
        adjoint = adjoint_local(u_tiles, v_tiles, mask, minus_all)
        source_traces = exchange(adjoint.astype(jnp.bfloat16), parts)
        src_windowed = window(source_traces, src_picked)
        returned = exchange_back(src_windowed, col_tiles).astype(jnp.float32)
        plus = (direct_f32 + returned).astype(jnp.bfloat16)
    return (tile_minor(plus)[None], tile_minor(minus)[None])


def solution(mesh):
    placed = (
        P("freq", None, ("groups", "vp"), "src"),
        P("freq", "src", None, None, None),
        P("freq", None, None, None, "src"),
        P("freq", None, "src"),
        P(("groups", "vp"), "src"),
        P(("groups", "vp"), "src"),
    )
    return jax.shard_map(
        per_device,
        mesh=mesh,
        in_specs=placed,
        out_specs=(
            P("freq", None, ("groups", "vp"), "src"),
            P("freq", None, ("groups", "vp"), "src"),
        ),
        check_vma=False,
    )
```

```python
import math

import jax
import jax.numpy as jnp
from jax import lax
from jax.experimental import pallas as pl
from jax.sharding import PartitionSpec as P

TILE = 256
RANK = 32
NT = 256
FLO = 8
ITERS = 2
GATHER_MAX = 4


def make_tables(count):
    index = FLO + jnp.arange(count, dtype=jnp.int32)
    sample = jnp.arange(NT, dtype=jnp.int32)
    phase = (index[:, None] * sample[None, :] % NT).astype(jnp.float32) * (2.0 * math.pi / NT)
    cosine = jnp.cos(phase)
    sine = jnp.sin(phase)
    inverse = jnp.stack([cosine, -sine]) * (2.0 / NT)
    forward = jnp.stack([cosine, -sine])
    return (inverse, forward)


def gather_kernel(table_ref, onset_ref, out_ref):
    rows = onset_ref.shape[1]
    width = onset_ref.shape[2]
    size = out_ref.shape[0]
    sample = lax.broadcasted_iota(jnp.int32, (NT, width), 0)
    for row in range(rows):
        place = jnp.clip(onset_ref[0, row : row + 1, :], 0, NT) - 1
        pick = (sample == place).astype(jnp.bfloat16)
        parts = jnp.dot(table_ref[...], pick, preferred_element_type=jnp.float32)
        out_ref[:, 0, row, :] = parts[:size] + parts[size:]


def window_gather(count, onset):
    if count > GATHER_MAX:
        return onset
    inverse, forward = make_tables(count)
    terms = jnp.einsum("cft,dgt->tgdfc", forward, inverse, precision=lax.Precision.HIGHEST)
    size = 4 * count * count
    table = jnp.cumsum(terms.reshape(NT, size), axis=0)
    high = table.astype(jnp.bfloat16)
    rest = table - high.astype(jnp.float32)
    low = rest.astype(jnp.bfloat16)
    stacked = jnp.concatenate([high, low], axis=1).T
    blocks, points, width = onset.shape
    rows = 8
    return pl.pallas_call(
        gather_kernel,
        grid=(blocks, points // rows),
        in_specs=[
            pl.BlockSpec((2 * size, NT), lambda b, r: (0, 0)),
            pl.BlockSpec((1, rows, width), lambda b, r: (b, r, 0)),
        ],
        out_specs=pl.BlockSpec((size, 1, rows, width), lambda b, r: (0, b, r, 0)),
        out_shape=jax.ShapeDtypeStruct((size, blocks, points, width), jnp.float32),
    )(stacked, onset)


def window_kernel(matrix_ref, spectrum_ref, out_ref):
    count = spectrum_ref.shape[0]
    comps = 2 * count
    source = [spectrum_ref[q // 2, 0, q % 2].astype(jnp.float32) for q in range(comps)]
    for target in range(comps):
        total = matrix_ref[target, 0] * source[0]
        for q in range(1, comps):
            total = total + matrix_ref[q * comps + target, 0] * source[q]
        out_ref[target // 2, 0, target % 2] = total.astype(out_ref.dtype)


def window(spectrum, picked):
    count = spectrum.shape[0]
    if count > GATHER_MAX:
        inverse, forward = make_tables(count)
        signal = jnp.einsum(
            "fbcvm,cft->bvmt", spectrum.astype(jnp.float32), inverse, precision=lax.Precision.HIGHEST
        )
        keep = lax.broadcasted_iota(jnp.int32, signal.shape, 3) < picked[..., None]
        signal = jnp.where(keep, signal, jnp.zeros_like(signal))
        result = jnp.einsum("bvmt,cft->fbcvm", signal, forward, precision=lax.Precision.HIGHEST)
        return result.astype(jnp.bfloat16)
    _, blocks, comps, points, width = spectrum.shape
    size = picked.shape[0]
    return pl.pallas_call(
        window_kernel,
        grid=(blocks,),
        in_specs=[
            pl.BlockSpec((size, 1, points, width), lambda b: (0, b, 0, 0)),
            pl.BlockSpec((count, 1, comps, points, width), lambda b: (0, b, 0, 0, 0)),
        ],
        out_specs=pl.BlockSpec((count, 1, comps, points, width), lambda b: (0, b, 0, 0, 0)),
        out_shape=jax.ShapeDtypeStruct(spectrum.shape, jnp.bfloat16),
    )(picked, spectrum)


def piece_count(tiles, parts):
    return parts // math.gcd(tiles, parts)


def to_pieces(x, parts):
    tiles, comps, points, width = x.shape
    k = piece_count(tiles, parts)
    if k == 1:
        return x
    x = x.reshape(tiles, comps, points, k, width // k)
    return jnp.transpose(x, (0, 3, 1, 2, 4)).reshape(tiles * k, comps, points, width // k)


def from_pieces(x, tiles):
    count, comps, points, width = x.shape
    k = count // tiles
    if k == 1:
        return x
    x = x.reshape(tiles, k, comps, points, width)
    return jnp.transpose(x, (0, 2, 3, 1, 4)).reshape(tiles, comps, points, k * width)


def onset_pieces(onset, tiles, parts, place):
    points = onset.shape[0]
    k = piece_count(tiles, parts)
    blocks = tiles * k
    each = blocks // parts
    split = onset.reshape(points, blocks, TILE // k)
    split = jnp.transpose(split, (1, 0, 2))
    return lax.dynamic_slice_in_dim(split, place * each, each, 0)


def exchange(x, parts):
    tiles = x.shape[0]
    pieces = to_pieces(x, parts)
    got = lax.all_to_all(pieces, "freq", split_axis=0, concat_axis=0, tiled=True)
    return got.reshape((parts, got.shape[0] // parts) + got.shape[1:])


def exchange_back(y, tiles):
    flat = y.reshape((y.shape[0] * y.shape[1],) + y.shape[2:])
    got = lax.all_to_all(flat, "freq", split_axis=0, concat_axis=0, tiled=True)
    return from_pieces(got, tiles)


def coefficients(v_tiles, mask, plus):
    form = "irjt,jvt->ivjr"
    p_re = plus[:, 0]
    p_im = plus[:, 1]
    z_real = jnp.einsum(
        form, v_tiles[:, 0], p_re, preferred_element_type=jnp.float32
    ) + jnp.einsum(form, v_tiles[:, 1], p_im, preferred_element_type=jnp.float32)
    z_imag = jnp.einsum(
        form, v_tiles[:, 0], p_im, preferred_element_type=jnp.float32
    ) - jnp.einsum(form, v_tiles[:, 1], p_re, preferred_element_type=jnp.float32)
    z_real = jnp.where(mask, z_real, 0.0).astype(jnp.bfloat16)
    z_imag = jnp.where(mask, z_imag, 0.0).astype(jnp.bfloat16)
    return z_real, z_imag


def expand_rows(u_tiles, z_real, z_imag):
    other = "jrit,ivjr->ivt"
    y_real = jnp.einsum(
        other, u_tiles[:, 0], z_real, preferred_element_type=jnp.float32
    ) - jnp.einsum(other, u_tiles[:, 1], z_imag, preferred_element_type=jnp.float32)
    y_imag = jnp.einsum(
        other, u_tiles[:, 0], z_imag, preferred_element_type=jnp.float32
    ) + jnp.einsum(other, u_tiles[:, 1], z_real, preferred_element_type=jnp.float32)
    return jnp.stack([y_real, y_imag], axis=1)


def adjoint_local(u_tiles, v_tiles, mask, minus):
    form = "jrit,ivt->ivjr"
    m_re = minus[:, 0]
    m_im = minus[:, 1]
    w_real = jnp.einsum(
        form, u_tiles[:, 0], m_re, preferred_element_type=jnp.float32
    ) + jnp.einsum(form, u_tiles[:, 1], m_im, preferred_element_type=jnp.float32)
    w_imag = jnp.einsum(
        form, u_tiles[:, 0], m_im, preferred_element_type=jnp.float32
    ) - jnp.einsum(form, u_tiles[:, 1], m_re, preferred_element_type=jnp.float32)
    w_real = jnp.where(mask, w_real, 0.0).astype(jnp.bfloat16)
    w_imag = jnp.where(mask, w_imag, 0.0).astype(jnp.bfloat16)
    other = "irjt,ivjr->jvt"
    x_real = jnp.einsum(
        other, v_tiles[:, 0], w_real, preferred_element_type=jnp.float32
    ) - jnp.einsum(other, v_tiles[:, 1], w_imag, preferred_element_type=jnp.float32)
    x_imag = jnp.einsum(
        other, v_tiles[:, 0], w_imag, preferred_element_type=jnp.float32
    ) + jnp.einsum(other, v_tiles[:, 1], w_real, preferred_element_type=jnp.float32)
    return jnp.stack([x_real, x_imag], axis=1)


def reduce_src(partial):
    count = lax.axis_size("src")
    if count != 2:
        return lax.psum_scatter(
            partial.astype(jnp.bfloat16), "src", scatter_dimension=0, tiled=True
        )
    place = lax.axis_index("src")
    half = partial.shape[0] // 2
    mine = lax.dynamic_slice_in_dim(partial, place * half, half, 0)
    other = lax.dynamic_slice_in_dim(partial, (1 - place) * half, half, 0)
    got = lax.ppermute(other.astype(jnp.bfloat16), "src", perm=[(0, 1), (1, 0)])
    return (mine.astype(jnp.bfloat16).astype(jnp.float32) + got.astype(jnp.float32)).astype(jnp.bfloat16)


def tile_major(x):
    comps, points, width = x.shape
    return jnp.transpose(x.reshape(comps, points, width // TILE, TILE), (2, 0, 1, 3))


def tile_minor(x):
    tiles, comps, points, width = x.shape
    return jnp.transpose(x, (1, 2, 0, 3)).reshape(comps, points, tiles * width)


def per_device(focus_direct, u_factors, v_factors, tile_ranks, onset_rec, onset_src):
    parts = lax.axis_size("freq")
    place = lax.axis_index("freq")
    u_fac = u_factors[0]
    v_fac = v_factors[0]
    col_tiles = u_fac.shape[0]
    row_tiles = v_fac.shape[0]
    u_tiles = u_fac.reshape(col_tiles, 2, RANK, row_tiles, TILE)
    v_tiles = v_fac.reshape(row_tiles, 2, RANK, col_tiles, TILE)
    rank_index = jnp.arange(RANK, dtype=jnp.int32)
    mask = (rank_index[None, None, :] < tile_ranks[0][:, :, None])[:, None]
    rec_tiles = onset_rec.shape[1] // TILE
    rec_picked = window_gather(parts, onset_pieces(onset_rec, rec_tiles, parts, place))
    src_picked = window_gather(parts, onset_pieces(onset_src, col_tiles, parts, place))
    direct = lax.optimization_barrier(tile_major(focus_direct[0]))
    direct_f32 = direct.astype(jnp.float32)
    plus = direct
    minus = None
    for sweep in range(ITERS):
        z_real, z_imag = coefficients(v_tiles, mask, plus)
        partial_terms = expand_rows(u_tiles, z_real, z_imag)
        summed = reduce_src(partial_terms)
        traces = exchange(summed, parts)
        windowed = window(traces, rec_picked)
        minus = exchange_back(windowed, rec_tiles)
        minus_all = lax.all_gather(minus, "src", axis=0, tiled=True)
        adjoint = adjoint_local(u_tiles, v_tiles, mask, minus_all)
        source_traces = exchange(adjoint.astype(jnp.bfloat16), parts)
        src_windowed = window(source_traces, src_picked)
        returned = exchange_back(src_windowed, col_tiles).astype(jnp.float32)
        plus = (direct_f32 + returned).astype(jnp.bfloat16)
    return (tile_minor(plus)[None], tile_minor(minus)[None])


def solution(mesh):
    placed = (
        P("freq", None, ("groups", "vp"), "src"),
        P("freq", "src", None, None, None),
        P("freq", None, None, None, "src"),
        P("freq", None, "src"),
        P(("groups", "vp"), "src"),
        P(("groups", "vp"), "src"),
    )
    return jax.shard_map(
        per_device,
        mesh=mesh,
        in_specs=placed,
        out_specs=(
            P("freq", None, ("groups", "vp"), "src"),
            P("freq", None, ("groups", "vp"), "src"),
        ),
        check_vma=False,
    )
```

```python
import math

import jax
import jax.numpy as jnp
from jax import lax
from jax.experimental import pallas as pl
from jax.sharding import PartitionSpec as P

TILE = 256
RANK = 32
NT = 256
FLO = 8
ITERS = 2
GATHER_MAX = 4


def make_tables(count):
    index = FLO + jnp.arange(count, dtype=jnp.int32)
    sample = jnp.arange(NT, dtype=jnp.int32)
    phase = (index[:, None] * sample[None, :] % NT).astype(jnp.float32) * (2.0 * math.pi / NT)
    cosine = jnp.cos(phase)
    sine = jnp.sin(phase)
    inverse = jnp.stack([cosine, -sine]) * (2.0 / NT)
    forward = jnp.stack([cosine, -sine])
    return (inverse, forward)


def gather_kernel(table_ref, onset_ref, out_ref):
    rows = onset_ref.shape[1]
    width = onset_ref.shape[2]
    size = out_ref.shape[0]
    sample = lax.broadcasted_iota(jnp.int32, (NT, width), 0)
    for row in range(rows):
        place = jnp.clip(onset_ref[0, row : row + 1, :], 0, NT) - 1
        pick = (sample == place).astype(jnp.bfloat16)
        parts = jnp.dot(table_ref[...], pick, preferred_element_type=jnp.float32)
        out_ref[:, 0, row, :] = parts[:size] + parts[size:]


def window_gather(count, onset, target=None):
    if count > GATHER_MAX:
        return onset
    inverse, forward = make_tables(count)
    terms = jnp.einsum("cft,dgt->tgdfc", forward, inverse, precision=lax.Precision.HIGHEST)
    size = 4 * count * count
    table = jnp.cumsum(terms.reshape(NT, size), axis=0)
    if target is not None:
        table = table.reshape(NT, 2 * count, count, 2)
        table = lax.dynamic_index_in_dim(table, target, 2, keepdims=False)
        size = 4 * count
        table = table.reshape(NT, size)
    high = table.astype(jnp.bfloat16)
    rest = table - high.astype(jnp.float32)
    low = rest.astype(jnp.bfloat16)
    stacked = jnp.concatenate([high, low], axis=1).T
    blocks, points, width = onset.shape
    rows = 8
    return pl.pallas_call(
        gather_kernel,
        grid=(blocks, points // rows),
        in_specs=[
            pl.BlockSpec((2 * size, NT), lambda b, r: (0, 0)),
            pl.BlockSpec((1, rows, width), lambda b, r: (b, r, 0)),
        ],
        out_specs=pl.BlockSpec((size, 1, rows, width), lambda b, r: (0, b, r, 0)),
        out_shape=jax.ShapeDtypeStruct((size, blocks, points, width), jnp.float32),
    )(stacked, onset)


def window_kernel(matrix_ref, spectrum_ref, out_ref):
    count = spectrum_ref.shape[0]
    comps = 2 * count
    source = [spectrum_ref[q // 2, 0, q % 2].astype(jnp.float32) for q in range(comps)]
    for target in range(comps):
        total = matrix_ref[target, 0] * source[0]
        for q in range(1, comps):
            total = total + matrix_ref[q * comps + target, 0] * source[q]
        out_ref[target // 2, 0, target % 2] = total.astype(out_ref.dtype)


def own_window_kernel(matrix_ref, spectrum_ref, out_ref):
    count = spectrum_ref.shape[0]
    comps = 2 * count
    source = [spectrum_ref[q // 2, 0, q % 2].astype(jnp.float32) for q in range(comps)]
    for target in range(2):
        total = matrix_ref[target, 0] * source[0]
        for q in range(1, comps):
            total = total + matrix_ref[q * 2 + target, 0] * source[q]
        out_ref[0, target] = total.astype(out_ref.dtype)


def own_window(spectrum, picked):
    _, blocks, comps, points, width = spectrum.shape
    size = picked.shape[0]
    return pl.pallas_call(
        own_window_kernel,
        grid=(blocks,),
        in_specs=[
            pl.BlockSpec((size, 1, points, width), lambda b: (0, b, 0, 0)),
            pl.BlockSpec((spectrum.shape[0], 1, comps, points, width), lambda b: (0, b, 0, 0, 0)),
        ],
        out_specs=pl.BlockSpec((1, comps, points, width), lambda b: (b, 0, 0, 0)),
        out_shape=jax.ShapeDtypeStruct((blocks, comps, points, width), jnp.bfloat16),
    )(picked, spectrum)


def window(spectrum, picked):
    count = spectrum.shape[0]
    if count > GATHER_MAX:
        inverse, forward = make_tables(count)
        signal = jnp.einsum(
            "fbcvm,cft->bvmt", spectrum.astype(jnp.float32), inverse, precision=lax.Precision.HIGHEST
        )
        keep = lax.broadcasted_iota(jnp.int32, signal.shape, 3) < picked[..., None]
        signal = jnp.where(keep, signal, jnp.zeros_like(signal))
        result = jnp.einsum("bvmt,cft->fbcvm", signal, forward, precision=lax.Precision.HIGHEST)
        return result.astype(jnp.bfloat16)
    _, blocks, comps, points, width = spectrum.shape
    size = picked.shape[0]
    return pl.pallas_call(
        window_kernel,
        grid=(blocks,),
        in_specs=[
            pl.BlockSpec((size, 1, points, width), lambda b: (0, b, 0, 0)),
            pl.BlockSpec((count, 1, comps, points, width), lambda b: (0, b, 0, 0, 0)),
        ],
        out_specs=pl.BlockSpec((count, 1, comps, points, width), lambda b: (0, b, 0, 0, 0)),
        out_shape=jax.ShapeDtypeStruct(spectrum.shape, jnp.bfloat16),
    )(picked, spectrum)


def piece_count(tiles, parts):
    return parts // math.gcd(tiles, parts)


def to_pieces(x, parts):
    tiles, comps, points, width = x.shape
    k = piece_count(tiles, parts)
    if k == 1:
        return x
    x = x.reshape(tiles, comps, points, k, width // k)
    return jnp.transpose(x, (0, 3, 1, 2, 4)).reshape(tiles * k, comps, points, width // k)


def from_pieces(x, tiles):
    count, comps, points, width = x.shape
    k = count // tiles
    if k == 1:
        return x
    x = x.reshape(tiles, k, comps, points, width)
    return jnp.transpose(x, (0, 2, 3, 1, 4)).reshape(tiles, comps, points, k * width)


def onset_pieces(onset, tiles, parts, place):
    points = onset.shape[0]
    k = piece_count(tiles, parts)
    blocks = tiles * k
    each = blocks // parts
    split = onset.reshape(points, blocks, TILE // k)
    split = jnp.transpose(split, (1, 0, 2))
    return lax.dynamic_slice_in_dim(split, place * each, each, 0)


def exchange(x, parts):
    tiles = x.shape[0]
    pieces = to_pieces(x, parts)
    got = lax.all_to_all(pieces, "freq", split_axis=0, concat_axis=0, tiled=True)
    return got.reshape((parts, got.shape[0] // parts) + got.shape[1:])


def exchange_back(y, tiles):
    flat = y.reshape((y.shape[0] * y.shape[1],) + y.shape[2:])
    got = lax.all_to_all(flat, "freq", split_axis=0, concat_axis=0, tiled=True)
    return from_pieces(got, tiles)


def coefficients(v_tiles, mask, plus):
    form = "irjt,jvt->ivjr"
    p_re = plus[:, 0]
    p_im = plus[:, 1]
    z_real = jnp.einsum(
        form, v_tiles[:, 0], p_re, preferred_element_type=jnp.float32
    ) + jnp.einsum(form, v_tiles[:, 1], p_im, preferred_element_type=jnp.float32)
    z_imag = jnp.einsum(
        form, v_tiles[:, 0], p_im, preferred_element_type=jnp.float32
    ) - jnp.einsum(form, v_tiles[:, 1], p_re, preferred_element_type=jnp.float32)
    z_real = jnp.where(mask, z_real, 0.0).astype(jnp.bfloat16)
    z_imag = jnp.where(mask, z_imag, 0.0).astype(jnp.bfloat16)
    return z_real, z_imag


def expand_rows(u_tiles, z_real, z_imag):
    other = "jrit,ivjr->ivt"
    y_real = jnp.einsum(
        other, u_tiles[:, 0], z_real, preferred_element_type=jnp.float32
    ) - jnp.einsum(other, u_tiles[:, 1], z_imag, preferred_element_type=jnp.float32)
    y_imag = jnp.einsum(
        other, u_tiles[:, 0], z_imag, preferred_element_type=jnp.float32
    ) + jnp.einsum(other, u_tiles[:, 1], z_real, preferred_element_type=jnp.float32)
    return jnp.stack([y_real, y_imag], axis=1)


def adjoint_local(u_tiles, v_tiles, mask, minus):
    form = "jrit,ivt->ivjr"
    m_re = minus[:, 0]
    m_im = minus[:, 1]
    w_real = jnp.einsum(
        form, u_tiles[:, 0], m_re, preferred_element_type=jnp.float32
    ) + jnp.einsum(form, u_tiles[:, 1], m_im, preferred_element_type=jnp.float32)
    w_imag = jnp.einsum(
        form, u_tiles[:, 0], m_im, preferred_element_type=jnp.float32
    ) - jnp.einsum(form, u_tiles[:, 1], m_re, preferred_element_type=jnp.float32)
    w_real = jnp.where(mask, w_real, 0.0).astype(jnp.bfloat16)
    w_imag = jnp.where(mask, w_imag, 0.0).astype(jnp.bfloat16)
    other = "irjt,ivjr->jvt"
    x_real = jnp.einsum(
        other, v_tiles[:, 0], w_real, preferred_element_type=jnp.float32
    ) - jnp.einsum(other, v_tiles[:, 1], w_imag, preferred_element_type=jnp.float32)
    x_imag = jnp.einsum(
        other, v_tiles[:, 0], w_imag, preferred_element_type=jnp.float32
    ) + jnp.einsum(other, v_tiles[:, 1], w_real, preferred_element_type=jnp.float32)
    return jnp.stack([x_real, x_imag], axis=1)


def reduce_src(partial):
    count = lax.axis_size("src")
    if count != 2:
        return lax.psum_scatter(
            partial.astype(jnp.bfloat16), "src", scatter_dimension=0, tiled=True
        )
    place = lax.axis_index("src")
    half = partial.shape[0] // 2
    mine = lax.dynamic_slice_in_dim(partial, place * half, half, 0)
    other = lax.dynamic_slice_in_dim(partial, (1 - place) * half, half, 0)
    got = lax.ppermute(other.astype(jnp.bfloat16), "src", perm=[(0, 1), (1, 0)])
    return (mine.astype(jnp.bfloat16).astype(jnp.float32) + got.astype(jnp.float32)).astype(jnp.bfloat16)


def tile_major(x):
    comps, points, width = x.shape
    return jnp.transpose(x.reshape(comps, points, width // TILE, TILE), (2, 0, 1, 3))


def tile_minor(x):
    tiles, comps, points, width = x.shape
    return jnp.transpose(x, (1, 2, 0, 3)).reshape(comps, points, tiles * width)


def per_device(focus_direct, u_factors, v_factors, tile_ranks, onset_rec, onset_src):
    parts = lax.axis_size("freq")
    place = lax.axis_index("freq")
    u_fac = u_factors[0]
    v_fac = v_factors[0]
    col_tiles = u_fac.shape[0]
    row_tiles = v_fac.shape[0]
    u_tiles = u_fac.reshape(col_tiles, 2, RANK, row_tiles, TILE)
    v_tiles = v_fac.reshape(row_tiles, 2, RANK, col_tiles, TILE)
    rank_index = jnp.arange(RANK, dtype=jnp.int32)
    mask = (rank_index[None, None, :] < tile_ranks[0][:, :, None])[:, None]
    rec_tiles = onset_rec.shape[1] // TILE
    own_rec = parts <= GATHER_MAX
    if own_rec:
        rec_picked = window_gather(parts, onset_pieces(onset_rec, rec_tiles, 1, 0), place)
    else:
        rec_picked = window_gather(parts, onset_pieces(onset_rec, rec_tiles, parts, place))
    src_picked = window_gather(parts, onset_pieces(onset_src, col_tiles, parts, place))
    direct = tile_major(focus_direct[0])
    direct_f32 = direct.astype(jnp.float32)
    plus = direct
    minus = None
    for sweep in range(ITERS):
        z_real, z_imag = coefficients(v_tiles, mask, plus)
        partial_terms = expand_rows(u_tiles, z_real, z_imag)
        summed = reduce_src(partial_terms)
        if own_rec:
            traces = lax.all_gather(summed, "freq", axis=0, tiled=False)
            minus = own_window(traces, rec_picked)
        else:
            traces = exchange(summed, parts)
            windowed = window(traces, rec_picked)
            minus = exchange_back(windowed, rec_tiles)
        minus_all = lax.all_gather(minus, "src", axis=0, tiled=True)
        adjoint = adjoint_local(u_tiles, v_tiles, mask, minus_all)
        source_traces = exchange(adjoint.astype(jnp.bfloat16), parts)
        src_windowed = window(source_traces, src_picked)
        returned = exchange_back(src_windowed, col_tiles).astype(jnp.float32)
        plus = (direct_f32 + returned).astype(jnp.bfloat16)
    return (tile_minor(plus)[None], tile_minor(minus)[None])


def solution(mesh):
    placed = (
        P("freq", None, ("groups", "vp"), "src"),
        P("freq", "src", None, None, None),
        P("freq", None, None, None, "src"),
        P("freq", None, "src"),
        P(("groups", "vp"), "src"),
        P(("groups", "vp"), "src"),
    )
    return jax.shard_map(
        per_device,
        mesh=mesh,
        in_specs=placed,
        out_specs=(
            P("freq", None, ("groups", "vp"), "src"),
            P("freq", None, ("groups", "vp"), "src"),
        ),
        check_vma=False,
    )
```

```python
import math

import jax
import jax.numpy as jnp
from jax import lax
from jax.experimental import pallas as pl
from jax.sharding import PartitionSpec as P

TILE = 256
RANK = 32
NT = 256
FLO = 8
ITERS = 2
GATHER_MAX = 4


def make_tables(count):
    index = FLO + jnp.arange(count, dtype=jnp.int32)
    sample = jnp.arange(NT, dtype=jnp.int32)
    phase = (index[:, None] * sample[None, :] % NT).astype(jnp.float32) * (2.0 * math.pi / NT)
    cosine = jnp.cos(phase)
    sine = jnp.sin(phase)
    inverse = jnp.stack([cosine, -sine]) * (2.0 / NT)
    forward = jnp.stack([cosine, -sine])
    return (inverse, forward)


def gather_kernel(table_ref, onset_ref, out_ref):
    rows = onset_ref.shape[1]
    width = onset_ref.shape[2]
    size = out_ref.shape[0]
    sample = lax.broadcasted_iota(jnp.int32, (NT, width), 0)
    for row in range(rows):
        place = jnp.clip(onset_ref[0, row : row + 1, :], 0, NT) - 1
        pick = (sample == place).astype(jnp.bfloat16)
        parts = jnp.dot(table_ref[...], pick, preferred_element_type=jnp.float32)
        out_ref[:, 0, row, :] = parts[:size] + parts[size:]


def window_gather(count, onset):
    if count > GATHER_MAX:
        return onset
    inverse, forward = make_tables(count)
    terms = jnp.einsum("cft,dgt->tgdfc", forward, inverse, precision=lax.Precision.HIGHEST)
    size = 4 * count * count
    table = jnp.cumsum(terms.reshape(NT, size), axis=0)
    high = table.astype(jnp.bfloat16)
    rest = table - high.astype(jnp.float32)
    low = rest.astype(jnp.bfloat16)
    stacked = jnp.concatenate([high, low], axis=1).T
    blocks, points, width = onset.shape
    rows = 8
    return pl.pallas_call(
        gather_kernel,
        grid=(blocks, points // rows),
        in_specs=[
            pl.BlockSpec((2 * size, NT), lambda b, r: (0, 0)),
            pl.BlockSpec((1, rows, width), lambda b, r: (b, r, 0)),
        ],
        out_specs=pl.BlockSpec((size, 1, rows, width), lambda b, r: (0, b, r, 0)),
        out_shape=jax.ShapeDtypeStruct((size, blocks, points, width), jnp.float32),
    )(stacked, onset)


def window_kernel(matrix_ref, spectrum_ref, out_ref):
    count = spectrum_ref.shape[0]
    comps = 2 * count
    source = [spectrum_ref[q // 2, 0, q % 2].astype(jnp.float32) for q in range(comps)]
    for target in range(comps):
        total = matrix_ref[target, 0] * source[0]
        for q in range(1, comps):
            total = total + matrix_ref[q * comps + target, 0] * source[q]
        out_ref[target // 2, 0, target % 2] = total.astype(out_ref.dtype)


def window(spectrum, picked):
    count = spectrum.shape[0]
    if count > GATHER_MAX:
        inverse, forward = make_tables(count)
        signal = jnp.einsum(
            "fbcvm,cft->bvmt", spectrum.astype(jnp.float32), inverse, precision=lax.Precision.HIGHEST
        )
        keep = lax.broadcasted_iota(jnp.int32, signal.shape, 3) < picked[..., None]
        signal = jnp.where(keep, signal, jnp.zeros_like(signal))
        result = jnp.einsum("bvmt,cft->fbcvm", signal, forward, precision=lax.Precision.HIGHEST)
        return result.astype(jnp.bfloat16)
    _, blocks, comps, points, width = spectrum.shape
    size = picked.shape[0]
    return pl.pallas_call(
        window_kernel,
        grid=(blocks,),
        in_specs=[
            pl.BlockSpec((size, 1, points, width), lambda b: (0, b, 0, 0)),
            pl.BlockSpec((count, 1, comps, points, width), lambda b: (0, b, 0, 0, 0)),
        ],
        out_specs=pl.BlockSpec((count, 1, comps, points, width), lambda b: (0, b, 0, 0, 0)),
        out_shape=jax.ShapeDtypeStruct(spectrum.shape, jnp.bfloat16),
    )(picked, spectrum)


def piece_count(tiles, parts):
    return parts // math.gcd(tiles, parts)


def to_pieces(x, parts):
    tiles, comps, points, width = x.shape
    k = piece_count(tiles, parts)
    if k == 1:
        return x
    x = x.reshape(tiles, comps, points, k, width // k)
    return jnp.transpose(x, (0, 3, 1, 2, 4)).reshape(tiles * k, comps, points, width // k)


def from_pieces(x, tiles):
    count, comps, points, width = x.shape
    k = count // tiles
    if k == 1:
        return x
    x = x.reshape(tiles, k, comps, points, width)
    return jnp.transpose(x, (0, 2, 3, 1, 4)).reshape(tiles, comps, points, k * width)


def onset_pieces(onset, tiles, parts, place):
    points = onset.shape[0]
    k = piece_count(tiles, parts)
    blocks = tiles * k
    each = blocks // parts
    split = onset.reshape(points, blocks, TILE // k)
    split = jnp.transpose(split, (1, 0, 2))
    return lax.dynamic_slice_in_dim(split, place * each, each, 0)


def exchange(x, parts):
    tiles = x.shape[0]
    pieces = to_pieces(x, parts)
    got = lax.all_to_all(pieces, "freq", split_axis=0, concat_axis=0, tiled=True)
    return got.reshape((parts, got.shape[0] // parts) + got.shape[1:])


def exchange_back(y, tiles):
    flat = y.reshape((y.shape[0] * y.shape[1],) + y.shape[2:])
    got = lax.all_to_all(flat, "freq", split_axis=0, concat_axis=0, tiled=True)
    return from_pieces(got, tiles)


def coefficients(v_tiles, mask, plus):
    form = "irjt,jvt->ivjr"
    p_re = plus[:, 0]
    p_im = plus[:, 1]
    z_real = jnp.einsum(
        form, v_tiles[:, 0], p_re, preferred_element_type=jnp.float32
    ) + jnp.einsum(form, v_tiles[:, 1], p_im, preferred_element_type=jnp.float32)
    z_imag = jnp.einsum(
        form, v_tiles[:, 0], p_im, preferred_element_type=jnp.float32
    ) - jnp.einsum(form, v_tiles[:, 1], p_re, preferred_element_type=jnp.float32)
    z_real = jnp.where(mask, z_real, 0.0).astype(jnp.bfloat16)
    z_imag = jnp.where(mask, z_imag, 0.0).astype(jnp.bfloat16)
    return z_real, z_imag


def expand_rows(u_tiles, z_real, z_imag):
    other = "jrit,ivjr->ivt"
    y_real = jnp.einsum(
        other, u_tiles[:, 0], z_real, preferred_element_type=jnp.float32
    ) - jnp.einsum(other, u_tiles[:, 1], z_imag, preferred_element_type=jnp.float32)
    y_imag = jnp.einsum(
        other, u_tiles[:, 0], z_imag, preferred_element_type=jnp.float32
    ) + jnp.einsum(other, u_tiles[:, 1], z_real, preferred_element_type=jnp.float32)
    return jnp.stack([y_real, y_imag], axis=1)


def adjoint_local(u_tiles, v_tiles, mask, minus):
    form = "jrit,ivt->ivjr"
    m_re = minus[:, 0]
    m_im = minus[:, 1]
    w_real = jnp.einsum(
        form, u_tiles[:, 0], m_re, preferred_element_type=jnp.float32
    ) + jnp.einsum(form, u_tiles[:, 1], m_im, preferred_element_type=jnp.float32)
    w_imag = jnp.einsum(
        form, u_tiles[:, 0], m_im, preferred_element_type=jnp.float32
    ) - jnp.einsum(form, u_tiles[:, 1], m_re, preferred_element_type=jnp.float32)
    w_real = jnp.where(mask, w_real, 0.0).astype(jnp.bfloat16)
    w_imag = jnp.where(mask, w_imag, 0.0).astype(jnp.bfloat16)
    other = "irjt,ivjr->jvt"
    x_real = jnp.einsum(
        other, v_tiles[:, 0], w_real, preferred_element_type=jnp.float32
    ) - jnp.einsum(other, v_tiles[:, 1], w_imag, preferred_element_type=jnp.float32)
    x_imag = jnp.einsum(
        other, v_tiles[:, 0], w_imag, preferred_element_type=jnp.float32
    ) + jnp.einsum(other, v_tiles[:, 1], w_real, preferred_element_type=jnp.float32)
    return jnp.stack([x_real, x_imag], axis=1)


def reduce_src(partial):
    count = lax.axis_size("src")
    if count != 2:
        return lax.psum_scatter(
            partial.astype(jnp.bfloat16), "src", scatter_dimension=0, tiled=True
        )
    place = lax.axis_index("src")
    half = partial.shape[0] // 2
    mine = lax.dynamic_slice_in_dim(partial, place * half, half, 0)
    other = lax.dynamic_slice_in_dim(partial, (1 - place) * half, half, 0)
    got = lax.ppermute(other.astype(jnp.bfloat16), "src", perm=[(0, 1), (1, 0)])
    return (mine.astype(jnp.bfloat16).astype(jnp.float32) + got.astype(jnp.float32)).astype(jnp.bfloat16)


def expand_reduce(u_tiles, z_real, z_imag):
    count = lax.axis_size("src")
    if count != 2:
        return reduce_src(expand_rows(u_tiles, z_real, z_imag))
    place = lax.axis_index("src")
    half = z_real.shape[0] // 2

    def rows(start):
        u_part = lax.dynamic_slice_in_dim(u_tiles, start, half, 3)
        re_part = lax.dynamic_slice_in_dim(z_real, start, half, 0)
        im_part = lax.dynamic_slice_in_dim(z_imag, start, half, 0)
        return expand_rows(u_part, re_part, im_part)

    other = rows((1 - place) * half).astype(jnp.bfloat16)
    got = lax.ppermute(other, "src", perm=[(0, 1), (1, 0)])
    mine = rows(place * half)
    return (mine.astype(jnp.bfloat16).astype(jnp.float32) + got.astype(jnp.float32)).astype(jnp.bfloat16)


def tile_major(x):
    comps, points, width = x.shape
    return jnp.transpose(x.reshape(comps, points, width // TILE, TILE), (2, 0, 1, 3))


def tile_minor(x):
    tiles, comps, points, width = x.shape
    return jnp.transpose(x, (1, 2, 0, 3)).reshape(comps, points, tiles * width)


def per_device(focus_direct, u_factors, v_factors, tile_ranks, onset_rec, onset_src):
    parts = lax.axis_size("freq")
    place = lax.axis_index("freq")
    u_fac = u_factors[0]
    v_fac = v_factors[0]
    col_tiles = u_fac.shape[0]
    row_tiles = v_fac.shape[0]
    u_tiles = u_fac.reshape(col_tiles, 2, RANK, row_tiles, TILE)
    v_tiles = v_fac.reshape(row_tiles, 2, RANK, col_tiles, TILE)
    rank_index = jnp.arange(RANK, dtype=jnp.int32)
    mask = (rank_index[None, None, :] < tile_ranks[0][:, :, None])[:, None]
    rec_tiles = onset_rec.shape[1] // TILE
    rec_picked = window_gather(parts, onset_pieces(onset_rec, rec_tiles, parts, place))
    src_picked = window_gather(parts, onset_pieces(onset_src, col_tiles, parts, place))
    direct = tile_major(focus_direct[0])
    direct_f32 = direct.astype(jnp.float32)
    plus = direct
    minus = None
    for sweep in range(ITERS):
        z_real, z_imag = coefficients(v_tiles, mask, plus)
        summed = expand_reduce(u_tiles, z_real, z_imag)
        traces = exchange(summed, parts)
        windowed = window(traces, rec_picked)
        minus = exchange_back(windowed, rec_tiles)
        minus_all = lax.all_gather(minus, "src", axis=0, tiled=True)
        adjoint = adjoint_local(u_tiles, v_tiles, mask, minus_all)
        source_traces = exchange(adjoint.astype(jnp.bfloat16), parts)
        src_windowed = window(source_traces, src_picked)
        returned = exchange_back(src_windowed, col_tiles).astype(jnp.float32)
        plus = (direct_f32 + returned).astype(jnp.bfloat16)
    return (tile_minor(plus)[None], tile_minor(minus)[None])


def solution(mesh):
    placed = (
        P("freq", None, ("groups", "vp"), "src"),
        P("freq", "src", None, None, None),
        P("freq", None, None, None, "src"),
        P("freq", None, "src"),
        P(("groups", "vp"), "src"),
        P(("groups", "vp"), "src"),
    )
    return jax.shard_map(
        per_device,
        mesh=mesh,
        in_specs=placed,
        out_specs=(
            P("freq", None, ("groups", "vp"), "src"),
            P("freq", None, ("groups", "vp"), "src"),
        ),
        check_vma=False,
    )
```

```python
import math

import jax
import jax.numpy as jnp
from jax import lax
from jax.experimental import pallas as pl
from jax.sharding import PartitionSpec as P

TILE = 256
RANK = 32
NT = 256
FLO = 8
ITERS = 2
GATHER_MAX = 4


def make_tables(count):
    index = FLO + jnp.arange(count, dtype=jnp.int32)
    sample = jnp.arange(NT, dtype=jnp.int32)
    phase = (index[:, None] * sample[None, :] % NT).astype(jnp.float32) * (2.0 * math.pi / NT)
    cosine = jnp.cos(phase)
    sine = jnp.sin(phase)
    inverse = jnp.stack([cosine, -sine]) * (2.0 / NT)
    forward = jnp.stack([cosine, -sine])
    return (inverse, forward)


def gather_kernel(table_ref, onset_ref, out_ref):
    rows = onset_ref.shape[1]
    width = onset_ref.shape[2]
    size = out_ref.shape[0]
    sample = lax.broadcasted_iota(jnp.int32, (NT, width), 0)
    for row in range(rows):
        place = jnp.clip(onset_ref[0, row : row + 1, :], 0, NT) - 1
        pick = (sample == place).astype(jnp.bfloat16)
        parts = jnp.dot(table_ref[...], pick, preferred_element_type=jnp.float32)
        out_ref[:, 0, row, :] = parts[:size] + parts[size:]


def window_gather(count, onset):
    if count > GATHER_MAX:
        return onset
    inverse, forward = make_tables(count)
    terms = jnp.einsum("cft,dgt->tgdfc", forward, inverse, precision=lax.Precision.HIGHEST)
    size = 4 * count * count
    table = jnp.cumsum(terms.reshape(NT, size), axis=0)
    high = table.astype(jnp.bfloat16)
    rest = table - high.astype(jnp.float32)
    low = rest.astype(jnp.bfloat16)
    stacked = jnp.concatenate([high, low], axis=1).T
    blocks, points, width = onset.shape
    rows = 8
    return pl.pallas_call(
        gather_kernel,
        grid=(blocks, points // rows),
        in_specs=[
            pl.BlockSpec((2 * size, NT), lambda b, r: (0, 0)),
            pl.BlockSpec((1, rows, width), lambda b, r: (b, r, 0)),
        ],
        out_specs=pl.BlockSpec((size, 1, rows, width), lambda b, r: (0, b, r, 0)),
        out_shape=jax.ShapeDtypeStruct((size, blocks, points, width), jnp.float32),
    )(stacked, onset)


def window_kernel(matrix_ref, spectrum_ref, out_ref):
    count = spectrum_ref.shape[0]
    comps = 2 * count
    source = [spectrum_ref[q // 2, 0, q % 2].astype(jnp.float32) for q in range(comps)]
    for target in range(comps):
        total = matrix_ref[target, 0] * source[0]
        for q in range(1, comps):
            total = total + matrix_ref[q * comps + target, 0] * source[q]
        out_ref[target // 2, 0, target % 2] = total.astype(out_ref.dtype)


def window(spectrum, picked):
    count = spectrum.shape[0]
    if count > GATHER_MAX:
        inverse, forward = make_tables(count)
        signal = jnp.einsum(
            "fbcvm,cft->bvmt", spectrum.astype(jnp.float32), inverse, precision=lax.Precision.HIGHEST
        )
        keep = lax.broadcasted_iota(jnp.int32, signal.shape, 3) < picked[..., None]
        signal = jnp.where(keep, signal, jnp.zeros_like(signal))
        result = jnp.einsum("bvmt,cft->fbcvm", signal, forward, precision=lax.Precision.HIGHEST)
        return result.astype(jnp.bfloat16)
    _, blocks, comps, points, width = spectrum.shape
    size = picked.shape[0]
    return pl.pallas_call(
        window_kernel,
        grid=(blocks,),
        in_specs=[
            pl.BlockSpec((size, 1, points, width), lambda b: (0, b, 0, 0)),
            pl.BlockSpec((count, 1, comps, points, width), lambda b: (0, b, 0, 0, 0)),
        ],
        out_specs=pl.BlockSpec((count, 1, comps, points, width), lambda b: (0, b, 0, 0, 0)),
        out_shape=jax.ShapeDtypeStruct(spectrum.shape, jnp.bfloat16),
    )(picked, spectrum)


def piece_count(tiles, parts):
    return parts // math.gcd(tiles, parts)


def to_pieces(x, parts):
    tiles, comps, points, width = x.shape
    k = piece_count(tiles, parts)
    if k == 1:
        return x
    x = x.reshape(tiles, comps, points, k, width // k)
    return jnp.transpose(x, (0, 3, 1, 2, 4)).reshape(tiles * k, comps, points, width // k)


def from_pieces(x, tiles):
    count, comps, points, width = x.shape
    k = count // tiles
    if k == 1:
        return x
    x = x.reshape(tiles, k, comps, points, width)
    return jnp.transpose(x, (0, 2, 3, 1, 4)).reshape(tiles, comps, points, k * width)


def onset_pieces(onset, tiles, parts, place):
    points = onset.shape[0]
    k = piece_count(tiles, parts)
    blocks = tiles * k
    each = blocks // parts
    split = onset.reshape(points, blocks, TILE // k)
    split = jnp.transpose(split, (1, 0, 2))
    return lax.dynamic_slice_in_dim(split, place * each, each, 0)


def exchange(x, parts):
    tiles = x.shape[0]
    pieces = to_pieces(x, parts)
    got = lax.all_to_all(pieces, "freq", split_axis=0, concat_axis=0, tiled=True)
    return got.reshape((parts, got.shape[0] // parts) + got.shape[1:])


def exchange_back(y, tiles):
    flat = y.reshape((y.shape[0] * y.shape[1],) + y.shape[2:])
    got = lax.all_to_all(flat, "freq", split_axis=0, concat_axis=0, tiled=True)
    return from_pieces(got, tiles)


def coefficients(v_tiles, mask, plus):
    turned = jnp.stack([plus[:, 1], -plus[:, 0]], axis=1)
    both = jnp.stack([plus, turned])
    z = jnp.einsum("icrjt,ojcvt->oivjr", v_tiles, both, preferred_element_type=jnp.float32)
    z = jnp.where(mask[None], z, 0.0).astype(jnp.bfloat16)
    return z[0], z[1]


def expand_rows(u_tiles, z_real, z_imag):
    both = jnp.stack([jnp.stack([z_real, -z_imag]), jnp.stack([z_imag, z_real])])
    return jnp.einsum("jcrit,ocivjr->iovt", u_tiles, both, preferred_element_type=jnp.float32)


def adjoint_local(u_tiles, v_tiles, mask, minus):
    turned = jnp.stack([minus[:, 1], -minus[:, 0]], axis=1)
    both = jnp.stack([minus, turned])
    w = jnp.einsum("jcrit,oicvt->oivjr", u_tiles, both, preferred_element_type=jnp.float32)
    w = jnp.where(mask[None], w, 0.0).astype(jnp.bfloat16)
    w_real, w_imag = w[0], w[1]
    parts = jnp.stack([jnp.stack([w_real, -w_imag]), jnp.stack([w_imag, w_real])])
    return jnp.einsum("icrjt,ocivjr->jovt", v_tiles, parts, preferred_element_type=jnp.float32)


def reduce_src(partial):
    count = lax.axis_size("src")
    if count != 2:
        return lax.psum_scatter(
            partial.astype(jnp.bfloat16), "src", scatter_dimension=0, tiled=True
        )
    place = lax.axis_index("src")
    half = partial.shape[0] // 2
    mine = lax.dynamic_slice_in_dim(partial, place * half, half, 0)
    other = lax.dynamic_slice_in_dim(partial, (1 - place) * half, half, 0)
    got = lax.ppermute(other.astype(jnp.bfloat16), "src", perm=[(0, 1), (1, 0)])
    return (mine.astype(jnp.bfloat16).astype(jnp.float32) + got.astype(jnp.float32)).astype(jnp.bfloat16)


def tile_major(x):
    comps, points, width = x.shape
    return jnp.transpose(x.reshape(comps, points, width // TILE, TILE), (2, 0, 1, 3))


def tile_minor(x):
    tiles, comps, points, width = x.shape
    return jnp.transpose(x, (1, 2, 0, 3)).reshape(comps, points, tiles * width)


def per_device(focus_direct, u_factors, v_factors, tile_ranks, onset_rec, onset_src):
    parts = lax.axis_size("freq")
    place = lax.axis_index("freq")
    u_fac = u_factors[0]
    v_fac = v_factors[0]
    col_tiles = u_fac.shape[0]
    row_tiles = v_fac.shape[0]
    u_tiles = u_fac.reshape(col_tiles, 2, RANK, row_tiles, TILE)
    v_tiles = v_fac.reshape(row_tiles, 2, RANK, col_tiles, TILE)
    rank_index = jnp.arange(RANK, dtype=jnp.int32)
    mask = (rank_index[None, None, :] < tile_ranks[0][:, :, None])[:, None]
    rec_tiles = onset_rec.shape[1] // TILE
    rec_picked = window_gather(parts, onset_pieces(onset_rec, rec_tiles, parts, place))
    src_picked = window_gather(parts, onset_pieces(onset_src, col_tiles, parts, place))
    direct = tile_major(focus_direct[0])
    direct_f32 = direct.astype(jnp.float32)
    plus = direct
    minus = None
    for sweep in range(ITERS):
        z_real, z_imag = coefficients(v_tiles, mask, plus)
        partial_terms = expand_rows(u_tiles, z_real, z_imag)
        summed = reduce_src(partial_terms)
        traces = exchange(summed, parts)
        windowed = window(traces, rec_picked)
        minus = exchange_back(windowed, rec_tiles)
        minus_all = lax.all_gather(minus, "src", axis=0, tiled=True)
        adjoint = adjoint_local(u_tiles, v_tiles, mask, minus_all)
        source_traces = exchange(adjoint.astype(jnp.bfloat16), parts)
        src_windowed = window(source_traces, src_picked)
        returned = exchange_back(src_windowed, col_tiles).astype(jnp.float32)
        plus = (direct_f32 + returned).astype(jnp.bfloat16)
    return (tile_minor(plus)[None], tile_minor(minus)[None])


def solution(mesh):
    placed = (
        P("freq", None, ("groups", "vp"), "src"),
        P("freq", "src", None, None, None),
        P("freq", None, None, None, "src"),
        P("freq", None, "src"),
        P(("groups", "vp"), "src"),
        P(("groups", "vp"), "src"),
    )
    return jax.shard_map(
        per_device,
        mesh=mesh,
        in_specs=placed,
        out_specs=(
            P("freq", None, ("groups", "vp"), "src"),
            P("freq", None, ("groups", "vp"), "src"),
        ),
        check_vma=False,
    )
```

```python
import math

import jax
import jax.numpy as jnp
from jax import lax
from jax.experimental import pallas as pl
from jax.sharding import PartitionSpec as P

TILE = 256
RANK = 32
NT = 256
FLO = 8
ITERS = 2
GATHER_MAX = 4


def make_tables(count):
    index = FLO + jnp.arange(count, dtype=jnp.int32)
    sample = jnp.arange(NT, dtype=jnp.int32)
    phase = (index[:, None] * sample[None, :] % NT).astype(jnp.float32) * (2.0 * math.pi / NT)
    cosine = jnp.cos(phase)
    sine = jnp.sin(phase)
    inverse = jnp.stack([cosine, -sine]) * (2.0 / NT)
    forward = jnp.stack([cosine, -sine])
    return (inverse, forward)


def gather_kernel(table_ref, onset_ref, out_ref):
    rows = onset_ref.shape[1]
    width = onset_ref.shape[2]
    sample = lax.broadcasted_iota(jnp.int32, (NT, width), 0)
    for row in range(rows):
        place = jnp.clip(onset_ref[0, row : row + 1, :], 0, NT) - 1
        pick = (sample == place).astype(jnp.bfloat16)
        parts = jnp.dot(table_ref[...], pick, preferred_element_type=jnp.float32)
        out_ref[:, 0, row, :] = parts.astype(out_ref.dtype)


def window_gather(count, onset):
    if count > GATHER_MAX:
        return onset
    inverse, forward = make_tables(count)
    terms = jnp.einsum("cft,dgt->tgdfc", forward, inverse, precision=lax.Precision.HIGHEST)
    size = 4 * count * count
    table = jnp.cumsum(terms.reshape(NT, size), axis=0)
    stacked = table.astype(jnp.bfloat16).T
    blocks, points, width = onset.shape
    rows = 8
    return pl.pallas_call(
        gather_kernel,
        grid=(blocks, points // rows),
        in_specs=[
            pl.BlockSpec((size, NT), lambda b, r: (0, 0)),
            pl.BlockSpec((1, rows, width), lambda b, r: (b, r, 0)),
        ],
        out_specs=pl.BlockSpec((size, 1, rows, width), lambda b, r: (0, b, r, 0)),
        out_shape=jax.ShapeDtypeStruct((size, blocks, points, width), jnp.bfloat16),
    )(stacked, onset)


def window_kernel(matrix_ref, spectrum_ref, out_ref):
    count = spectrum_ref.shape[0]
    comps = 2 * count
    source = [spectrum_ref[q // 2, 0, q % 2].astype(jnp.float32) for q in range(comps)]
    for target in range(comps):
        total = matrix_ref[target, 0].astype(jnp.float32) * source[0]
        for q in range(1, comps):
            total = total + matrix_ref[q * comps + target, 0].astype(jnp.float32) * source[q]
        out_ref[target // 2, 0, target % 2] = total.astype(out_ref.dtype)


def window(spectrum, picked):
    count = spectrum.shape[0]
    if count > GATHER_MAX:
        inverse, forward = make_tables(count)
        signal = jnp.einsum(
            "fbcvm,cft->bvmt", spectrum.astype(jnp.float32), inverse, precision=lax.Precision.HIGHEST
        )
        keep = lax.broadcasted_iota(jnp.int32, signal.shape, 3) < picked[..., None]
        signal = jnp.where(keep, signal, jnp.zeros_like(signal))
        result = jnp.einsum("bvmt,cft->fbcvm", signal, forward, precision=lax.Precision.HIGHEST)
        return result.astype(jnp.bfloat16)
    _, blocks, comps, points, width = spectrum.shape
    size = picked.shape[0]
    return pl.pallas_call(
        window_kernel,
        grid=(blocks,),
        in_specs=[
            pl.BlockSpec((size, 1, points, width), lambda b: (0, b, 0, 0)),
            pl.BlockSpec((count, 1, comps, points, width), lambda b: (0, b, 0, 0, 0)),
        ],
        out_specs=pl.BlockSpec((count, 1, comps, points, width), lambda b: (0, b, 0, 0, 0)),
        out_shape=jax.ShapeDtypeStruct(spectrum.shape, jnp.bfloat16),
    )(picked, spectrum)


def piece_count(tiles, parts):
    return parts // math.gcd(tiles, parts)


def to_pieces(x, parts):
    tiles, comps, points, width = x.shape
    k = piece_count(tiles, parts)
    if k == 1:
        return x
    x = x.reshape(tiles, comps, points, k, width // k)
    return jnp.transpose(x, (0, 3, 1, 2, 4)).reshape(tiles * k, comps, points, width // k)


def from_pieces(x, tiles):
    count, comps, points, width = x.shape
    k = count // tiles
    if k == 1:
        return x
    x = x.reshape(tiles, k, comps, points, width)
    return jnp.transpose(x, (0, 2, 3, 1, 4)).reshape(tiles, comps, points, k * width)


def onset_pieces(onset, tiles, parts, place):
    points = onset.shape[0]
    k = piece_count(tiles, parts)
    blocks = tiles * k
    each = blocks // parts
    split = onset.reshape(points, blocks, TILE // k)
    split = jnp.transpose(split, (1, 0, 2))
    return lax.dynamic_slice_in_dim(split, place * each, each, 0)


def exchange(x, parts):
    tiles = x.shape[0]
    pieces = to_pieces(x, parts)
    got = lax.all_to_all(pieces, "freq", split_axis=0, concat_axis=0, tiled=True)
    return got.reshape((parts, got.shape[0] // parts) + got.shape[1:])


def exchange_back(y, tiles):
    flat = y.reshape((y.shape[0] * y.shape[1],) + y.shape[2:])
    got = lax.all_to_all(flat, "freq", split_axis=0, concat_axis=0, tiled=True)
    return from_pieces(got, tiles)


def coefficients(v_tiles, mask, plus):
    turned = jnp.stack([plus[:, 1], -plus[:, 0]], axis=1)
    both = jnp.stack([plus, turned])
    z = jnp.einsum("icrjt,ojcvt->oivjr", v_tiles, both, preferred_element_type=jnp.float32)
    z = jnp.where(mask[None], z, 0.0).astype(jnp.bfloat16)
    return z[0], z[1]


def expand_rows(u_tiles, z_real, z_imag):
    both = jnp.stack([jnp.stack([z_real, -z_imag]), jnp.stack([z_imag, z_real])])
    return jnp.einsum("jcrit,ocivjr->iovt", u_tiles, both, preferred_element_type=jnp.float32)


def adjoint_local(u_tiles, v_tiles, mask, minus):
    turned = jnp.stack([minus[:, 1], -minus[:, 0]], axis=1)
    both = jnp.stack([minus, turned])
    w = jnp.einsum("jcrit,oicvt->oivjr", u_tiles, both, preferred_element_type=jnp.float32)
    w = jnp.where(mask[None], w, 0.0).astype(jnp.bfloat16)
    w_real, w_imag = w[0], w[1]
    parts = jnp.stack([jnp.stack([w_real, -w_imag]), jnp.stack([w_imag, w_real])])
    return jnp.einsum("icrjt,ocivjr->jovt", v_tiles, parts, preferred_element_type=jnp.float32)


def reduce_src(partial):
    count = lax.axis_size("src")
    if count != 2:
        return lax.psum_scatter(
            partial.astype(jnp.bfloat16), "src", scatter_dimension=0, tiled=True
        )
    place = lax.axis_index("src")
    half = partial.shape[0] // 2
    mine = lax.dynamic_slice_in_dim(partial, place * half, half, 0)
    other = lax.dynamic_slice_in_dim(partial, (1 - place) * half, half, 0)
    got = lax.ppermute(other.astype(jnp.bfloat16), "src", perm=[(0, 1), (1, 0)])
    return (mine.astype(jnp.bfloat16).astype(jnp.float32) + got.astype(jnp.float32)).astype(jnp.bfloat16)


def tile_major(x):
    comps, points, width = x.shape
    return jnp.transpose(x.reshape(comps, points, width // TILE, TILE), (2, 0, 1, 3))


def tile_minor(x):
    tiles, comps, points, width = x.shape
    return jnp.transpose(x, (1, 2, 0, 3)).reshape(comps, points, tiles * width)


def per_device(focus_direct, u_factors, v_factors, tile_ranks, onset_rec, onset_src):
    parts = lax.axis_size("freq")
    place = lax.axis_index("freq")
    u_fac = u_factors[0]
    v_fac = v_factors[0]
    col_tiles = u_fac.shape[0]
    row_tiles = v_fac.shape[0]
    u_tiles = u_fac.reshape(col_tiles, 2, RANK, row_tiles, TILE)
    v_tiles = v_fac.reshape(row_tiles, 2, RANK, col_tiles, TILE)
    rank_index = jnp.arange(RANK, dtype=jnp.int32)
    mask = (rank_index[None, None, :] < tile_ranks[0][:, :, None])[:, None]
    rec_tiles = onset_rec.shape[1] // TILE
    rec_picked = window_gather(parts, onset_pieces(onset_rec, rec_tiles, parts, place))
    src_picked = window_gather(parts, onset_pieces(onset_src, col_tiles, parts, place))
    direct = tile_major(focus_direct[0])
    direct_f32 = direct.astype(jnp.float32)
    plus = direct
    minus = None
    for sweep in range(ITERS):
        z_real, z_imag = coefficients(v_tiles, mask, plus)
        partial_terms = expand_rows(u_tiles, z_real, z_imag)
        summed = reduce_src(partial_terms)
        traces = exchange(summed, parts)
        windowed = window(traces, rec_picked)
        minus = exchange_back(windowed, rec_tiles)
        minus_all = lax.all_gather(minus, "src", axis=0, tiled=True)
        adjoint = adjoint_local(u_tiles, v_tiles, mask, minus_all)
        source_traces = exchange(adjoint.astype(jnp.bfloat16), parts)
        src_windowed = window(source_traces, src_picked)
        returned = exchange_back(src_windowed, col_tiles).astype(jnp.float32)
        plus = (direct_f32 + returned).astype(jnp.bfloat16)
    return (tile_minor(plus)[None], tile_minor(minus)[None])


def solution(mesh):
    placed = (
        P("freq", None, ("groups", "vp"), "src"),
        P("freq", "src", None, None, None),
        P("freq", None, None, None, "src"),
        P("freq", None, "src"),
        P(("groups", "vp"), "src"),
        P(("groups", "vp"), "src"),
    )
    return jax.shard_map(
        per_device,
        mesh=mesh,
        in_specs=placed,
        out_specs=(
            P("freq", None, ("groups", "vp"), "src"),
            P("freq", None, ("groups", "vp"), "src"),
        ),
        check_vma=False,
    )
```

```python
import math

import jax
import jax.numpy as jnp
from jax import lax
from jax.experimental import pallas as pl
from jax.sharding import PartitionSpec as P

TILE = 256
RANK = 32
NT = 256
FLO = 8
ITERS = 2
GATHER_MAX = 4


def make_tables(count):
    index = FLO + jnp.arange(count, dtype=jnp.int32)
    sample = jnp.arange(NT, dtype=jnp.int32)
    phase = (index[:, None] * sample[None, :] % NT).astype(jnp.float32) * (2.0 * math.pi / NT)
    cosine = jnp.cos(phase)
    sine = jnp.sin(phase)
    inverse = jnp.stack([cosine, -sine]) * (2.0 / NT)
    forward = jnp.stack([cosine, -sine])
    return (inverse, forward)


def gather_kernel(table_ref, onset_ref, out_ref):
    rows = onset_ref.shape[1]
    width = onset_ref.shape[2]
    sample = lax.broadcasted_iota(jnp.int32, (NT, width), 0)
    for row in range(rows):
        place = jnp.clip(onset_ref[0, row : row + 1, :], 0, NT) - 1
        pick = (sample == place).astype(jnp.bfloat16)
        parts = jnp.dot(table_ref[...], pick, preferred_element_type=jnp.float32)
        out_ref[:, 0, row, :] = parts.astype(out_ref.dtype)


def window_gather(count, onset):
    if count > GATHER_MAX:
        return onset
    inverse, forward = make_tables(count)
    terms = jnp.einsum("cft,dgt->tgdfc", forward, inverse, precision=lax.Precision.HIGHEST)
    size = 4 * count * count
    table = jnp.cumsum(terms.reshape(NT, size), axis=0)
    stacked = table.astype(jnp.bfloat16).T
    blocks, points, width = onset.shape
    rows = 8
    return pl.pallas_call(
        gather_kernel,
        grid=(blocks, points // rows),
        in_specs=[
            pl.BlockSpec((size, NT), lambda b, r: (0, 0)),
            pl.BlockSpec((1, rows, width), lambda b, r: (b, r, 0)),
        ],
        out_specs=pl.BlockSpec((size, 1, rows, width), lambda b, r: (0, b, r, 0)),
        out_shape=jax.ShapeDtypeStruct((size, blocks, points, width), jnp.bfloat16),
    )(stacked, onset)


def window_kernel(matrix_ref, spectrum_ref, out_ref):
    count = spectrum_ref.shape[0]
    comps = 2 * count
    for block in range(spectrum_ref.shape[1]):
        source = [spectrum_ref[q // 2, block, q % 2].astype(jnp.float32) for q in range(comps)]
        for target in range(comps):
            total = matrix_ref[target, block].astype(jnp.float32) * source[0]
            for q in range(1, comps):
                total = total + matrix_ref[q * comps + target, block].astype(jnp.float32) * source[q]
            out_ref[target // 2, block, target % 2] = total.astype(out_ref.dtype)


def window(spectrum, picked):
    count = spectrum.shape[0]
    if count > GATHER_MAX:
        inverse, forward = make_tables(count)
        signal = jnp.einsum(
            "fbcvm,cft->bvmt", spectrum.astype(jnp.float32), inverse, precision=lax.Precision.HIGHEST
        )
        keep = lax.broadcasted_iota(jnp.int32, signal.shape, 3) < picked[..., None]
        signal = jnp.where(keep, signal, jnp.zeros_like(signal))
        result = jnp.einsum("bvmt,cft->fbcvm", signal, forward, precision=lax.Precision.HIGHEST)
        return result.astype(jnp.bfloat16)
    _, blocks, comps, points, width = spectrum.shape
    size = picked.shape[0]
    step = 2 if blocks % 2 == 0 else 1
    return pl.pallas_call(
        window_kernel,
        grid=(blocks // step,),
        in_specs=[
            pl.BlockSpec((size, step, points, width), lambda b: (0, b, 0, 0)),
            pl.BlockSpec((count, step, comps, points, width), lambda b: (0, b, 0, 0, 0)),
        ],
        out_specs=pl.BlockSpec((count, step, comps, points, width), lambda b: (0, b, 0, 0, 0)),
        out_shape=jax.ShapeDtypeStruct(spectrum.shape, jnp.bfloat16),
    )(picked, spectrum)


def piece_count(tiles, parts):
    return parts // math.gcd(tiles, parts)


def to_pieces(x, parts):
    tiles, comps, points, width = x.shape
    k = piece_count(tiles, parts)
    if k == 1:
        return x
    x = x.reshape(tiles, comps, points, k, width // k)
    return jnp.transpose(x, (0, 3, 1, 2, 4)).reshape(tiles * k, comps, points, width // k)


def from_pieces(x, tiles):
    count, comps, points, width = x.shape
    k = count // tiles
    if k == 1:
        return x
    x = x.reshape(tiles, k, comps, points, width)
    return jnp.transpose(x, (0, 2, 3, 1, 4)).reshape(tiles, comps, points, k * width)


def onset_pieces(onset, tiles, parts, place):
    points = onset.shape[0]
    k = piece_count(tiles, parts)
    blocks = tiles * k
    each = blocks // parts
    split = onset.reshape(points, blocks, TILE // k)
    split = jnp.transpose(split, (1, 0, 2))
    return lax.dynamic_slice_in_dim(split, place * each, each, 0)


def exchange(x, parts):
    tiles = x.shape[0]
    pieces = to_pieces(x, parts)
    got = lax.all_to_all(pieces, "freq", split_axis=0, concat_axis=0, tiled=True)
    return got.reshape((parts, got.shape[0] // parts) + got.shape[1:])


def exchange_back(y, tiles):
    flat = y.reshape((y.shape[0] * y.shape[1],) + y.shape[2:])
    got = lax.all_to_all(flat, "freq", split_axis=0, concat_axis=0, tiled=True)
    return from_pieces(got, tiles)


def coefficients(v_tiles, mask, plus):
    turned = jnp.stack([plus[:, 1], -plus[:, 0]], axis=1)
    both = jnp.stack([plus, turned])
    z = jnp.einsum("icrjt,ojcvt->oivjr", v_tiles, both, preferred_element_type=jnp.float32)
    z = jnp.where(mask[None], z, 0.0).astype(jnp.bfloat16)
    return z[0], z[1]


def expand_rows(u_tiles, z_real, z_imag):
    both = jnp.stack([jnp.stack([z_real, -z_imag]), jnp.stack([z_imag, z_real])])
    return jnp.einsum("jcrit,ocivjr->iovt", u_tiles, both, preferred_element_type=jnp.float32)


def adjoint_local(u_tiles, v_tiles, mask, minus):
    turned = jnp.stack([minus[:, 1], -minus[:, 0]], axis=1)
    both = jnp.stack([minus, turned])
    w = jnp.einsum("jcrit,oicvt->oivjr", u_tiles, both, preferred_element_type=jnp.float32)
    w = jnp.where(mask[None], w, 0.0).astype(jnp.bfloat16)
    w_real, w_imag = w[0], w[1]
    parts = jnp.stack([jnp.stack([w_real, -w_imag]), jnp.stack([w_imag, w_real])])
    return jnp.einsum("icrjt,ocivjr->jovt", v_tiles, parts, preferred_element_type=jnp.float32)


def reduce_src(partial):
    count = lax.axis_size("src")
    if count != 2:
        return lax.psum_scatter(
            partial.astype(jnp.bfloat16), "src", scatter_dimension=0, tiled=True
        )
    place = lax.axis_index("src")
    half = partial.shape[0] // 2
    mine = lax.dynamic_slice_in_dim(partial, place * half, half, 0)
    other = lax.dynamic_slice_in_dim(partial, (1 - place) * half, half, 0)
    got = lax.ppermute(other.astype(jnp.bfloat16), "src", perm=[(0, 1), (1, 0)])
    return (mine.astype(jnp.bfloat16).astype(jnp.float32) + got.astype(jnp.float32)).astype(jnp.bfloat16)


def tile_major(x):
    comps, points, width = x.shape
    return jnp.transpose(x.reshape(comps, points, width // TILE, TILE), (2, 0, 1, 3))


def tile_minor(x):
    tiles, comps, points, width = x.shape
    return jnp.transpose(x, (1, 2, 0, 3)).reshape(comps, points, tiles * width)


def per_device(focus_direct, u_factors, v_factors, tile_ranks, onset_rec, onset_src):
    parts = lax.axis_size("freq")
    place = lax.axis_index("freq")
    u_fac = u_factors[0]
    v_fac = v_factors[0]
    col_tiles = u_fac.shape[0]
    row_tiles = v_fac.shape[0]
    u_tiles = u_fac.reshape(col_tiles, 2, RANK, row_tiles, TILE)
    v_tiles = v_fac.reshape(row_tiles, 2, RANK, col_tiles, TILE)
    rank_index = jnp.arange(RANK, dtype=jnp.int32)
    mask = (rank_index[None, None, :] < tile_ranks[0][:, :, None])[:, None]
    rec_tiles = onset_rec.shape[1] // TILE
    rec_picked = window_gather(parts, onset_pieces(onset_rec, rec_tiles, parts, place))
    src_picked = window_gather(parts, onset_pieces(onset_src, col_tiles, parts, place))
    direct = tile_major(focus_direct[0])
    direct_f32 = direct.astype(jnp.float32)
    plus = direct
    minus = None
    for sweep in range(ITERS):
        z_real, z_imag = coefficients(v_tiles, mask, plus)
        partial_terms = expand_rows(u_tiles, z_real, z_imag)
        summed = reduce_src(partial_terms)
        traces = exchange(summed, parts)
        windowed = window(traces, rec_picked)
        minus = exchange_back(windowed, rec_tiles)
        minus_all = lax.all_gather(minus, "src", axis=0, tiled=True)
        adjoint = adjoint_local(u_tiles, v_tiles, mask, minus_all)
        source_traces = exchange(adjoint.astype(jnp.bfloat16), parts)
        src_windowed = window(source_traces, src_picked)
        returned = exchange_back(src_windowed, col_tiles).astype(jnp.float32)
        plus = (direct_f32 + returned).astype(jnp.bfloat16)
    return (tile_minor(plus)[None], tile_minor(minus)[None])


def solution(mesh):
    placed = (
        P("freq", None, ("groups", "vp"), "src"),
        P("freq", "src", None, None, None),
        P("freq", None, None, None, "src"),
        P("freq", None, "src"),
        P(("groups", "vp"), "src"),
        P(("groups", "vp"), "src"),
    )
    return jax.shard_map(
        per_device,
        mesh=mesh,
        in_specs=placed,
        out_specs=(
            P("freq", None, ("groups", "vp"), "src"),
            P("freq", None, ("groups", "vp"), "src"),
        ),
        check_vma=False,
    )
```

```python
import math

import jax
import jax.numpy as jnp
from jax import lax
from jax.experimental import pallas as pl
from jax.sharding import PartitionSpec as P

TILE = 256
RANK = 32
NT = 256
FLO = 8
ITERS = 2
GATHER_MAX = 4


def make_tables(count):
    index = FLO + jnp.arange(count, dtype=jnp.int32)
    sample = jnp.arange(NT, dtype=jnp.int32)
    phase = (index[:, None] * sample[None, :] % NT).astype(jnp.float32) * (2.0 * math.pi / NT)
    cosine = jnp.cos(phase)
    sine = jnp.sin(phase)
    inverse = jnp.stack([cosine, -sine]) * (2.0 / NT)
    forward = jnp.stack([cosine, -sine])
    return (inverse, forward)


def gather_kernel(table_ref, onset_ref, out_ref):
    rows = onset_ref.shape[1]
    width = onset_ref.shape[2]
    sample = lax.broadcasted_iota(jnp.int32, (NT, width), 0)
    for row in range(rows):
        place = jnp.clip(onset_ref[0, row : row + 1, :], 0, NT) - 1
        pick = (sample == place).astype(jnp.bfloat16)
        parts = jnp.dot(table_ref[...], pick, preferred_element_type=jnp.float32)
        out_ref[:, 0, row, :] = parts.astype(out_ref.dtype)


def window_gather(count, onset):
    if count > GATHER_MAX:
        return onset
    inverse, forward = make_tables(count)
    terms = jnp.einsum("cft,dgt->tgdfc", forward, inverse, precision=lax.Precision.HIGHEST)
    size = 4 * count * count
    table = jnp.cumsum(terms.reshape(NT, size), axis=0)
    stacked = table.astype(jnp.bfloat16).T
    blocks, points, width = onset.shape
    rows = 8
    return pl.pallas_call(
        gather_kernel,
        grid=(blocks, points // rows),
        in_specs=[
            pl.BlockSpec((size, NT), lambda b, r: (0, 0)),
            pl.BlockSpec((1, rows, width), lambda b, r: (b, r, 0)),
        ],
        out_specs=pl.BlockSpec((size, 1, rows, width), lambda b, r: (0, b, r, 0)),
        out_shape=jax.ShapeDtypeStruct((size, blocks, points, width), jnp.bfloat16),
    )(stacked, onset)


def window_kernel(matrix_ref, spectrum_ref, out_ref):
    count = spectrum_ref.shape[0]
    comps = 2 * count
    source = [spectrum_ref[q // 2, 0, q % 2].astype(jnp.float32) for q in range(comps)]
    for target in range(comps):
        total = matrix_ref[target, 0].astype(jnp.float32) * source[0]
        for q in range(1, comps):
            total = total + matrix_ref[q * comps + target, 0].astype(jnp.float32) * source[q]
        out_ref[target // 2, 0, target % 2] = total.astype(out_ref.dtype)


def window(spectrum, picked):
    count = spectrum.shape[0]
    if count > GATHER_MAX:
        inverse, forward = make_tables(count)
        signal = jnp.einsum(
            "fbcvm,cft->bvmt", spectrum.astype(jnp.float32), inverse, precision=lax.Precision.HIGHEST
        )
        keep = lax.broadcasted_iota(jnp.int32, signal.shape, 3) < picked[..., None]
        signal = jnp.where(keep, signal, jnp.zeros_like(signal))
        result = jnp.einsum("bvmt,cft->fbcvm", signal, forward, precision=lax.Precision.HIGHEST)
        return result.astype(jnp.bfloat16)
    _, blocks, comps, points, width = spectrum.shape
    size = picked.shape[0]
    return pl.pallas_call(
        window_kernel,
        grid=(blocks,),
        in_specs=[
            pl.BlockSpec((size, 1, points, width), lambda b: (0, b, 0, 0)),
            pl.BlockSpec((count, 1, comps, points, width), lambda b: (0, b, 0, 0, 0)),
        ],
        out_specs=pl.BlockSpec((count, 1, comps, points, width), lambda b: (0, b, 0, 0, 0)),
        out_shape=jax.ShapeDtypeStruct(spectrum.shape, jnp.bfloat16),
    )(picked, spectrum)


def piece_count(tiles, parts):
    return parts // math.gcd(tiles, parts)


def to_pieces(x, parts):
    tiles, comps, points, width = x.shape
    k = piece_count(tiles, parts)
    if k == 1:
        return x
    x = x.reshape(tiles, comps, points, k, width // k)
    return jnp.transpose(x, (0, 3, 1, 2, 4)).reshape(tiles * k, comps, points, width // k)


def from_pieces(x, tiles):
    count, comps, points, width = x.shape
    k = count // tiles
    if k == 1:
        return x
    x = x.reshape(tiles, k, comps, points, width)
    return jnp.transpose(x, (0, 2, 3, 1, 4)).reshape(tiles, comps, points, k * width)


def onset_pieces(onset, tiles, parts, place):
    points = onset.shape[0]
    k = piece_count(tiles, parts)
    blocks = tiles * k
    each = blocks // parts
    split = onset.reshape(points, blocks, TILE // k)
    split = jnp.transpose(split, (1, 0, 2))
    return lax.dynamic_slice_in_dim(split, place * each, each, 0)


def exchange(x, parts):
    tiles = x.shape[0]
    pieces = to_pieces(x, parts)
    got = lax.all_to_all(pieces, "freq", split_axis=0, concat_axis=0, tiled=True)
    return got.reshape((parts, got.shape[0] // parts) + got.shape[1:])


def exchange_back(y, tiles):
    flat = y.reshape((y.shape[0] * y.shape[1],) + y.shape[2:])
    got = lax.all_to_all(flat, "freq", split_axis=0, concat_axis=0, tiled=True)
    return from_pieces(got, tiles)


def coefficients(v_tiles, mask, plus):
    turned = jnp.stack([plus[:, 1], -plus[:, 0]], axis=1)
    both = jnp.stack([plus, turned])
    z = jnp.einsum("icrjt,ojcvt->oivjr", v_tiles, both, preferred_element_type=jnp.float32)
    z = jnp.where(mask[None], z, 0.0).astype(jnp.bfloat16)
    return z[0], z[1]


def expand_rows(u_tiles, z_real, z_imag):
    both = jnp.stack([jnp.stack([z_real, -z_imag]), jnp.stack([z_imag, z_real])])
    product = jnp.einsum("jcrit,ocivjr->iovt", u_tiles, both, preferred_element_type=jnp.float32)
    return product.astype(jnp.bfloat16)


def adjoint_local(u_tiles, v_tiles, mask, minus):
    turned = jnp.stack([minus[:, 1], -minus[:, 0]], axis=1)
    both = jnp.stack([minus, turned])
    w = jnp.einsum("jcrit,oicvt->oivjr", u_tiles, both, preferred_element_type=jnp.float32)
    w = jnp.where(mask[None], w, 0.0).astype(jnp.bfloat16)
    w_real, w_imag = w[0], w[1]
    parts = jnp.stack([jnp.stack([w_real, -w_imag]), jnp.stack([w_imag, w_real])])
    return jnp.einsum("icrjt,ocivjr->jovt", v_tiles, parts, preferred_element_type=jnp.float32)


def reduce_src(partial):
    count = lax.axis_size("src")
    if count != 2:
        return lax.psum_scatter(
            partial.astype(jnp.bfloat16), "src", scatter_dimension=0, tiled=True
        )
    place = lax.axis_index("src")
    half = partial.shape[0] // 2
    mine = lax.dynamic_slice_in_dim(partial, place * half, half, 0)
    other = lax.dynamic_slice_in_dim(partial, (1 - place) * half, half, 0)
    got = lax.ppermute(other, "src", perm=[(0, 1), (1, 0)])
    return (mine.astype(jnp.float32) + got.astype(jnp.float32)).astype(jnp.bfloat16)


def tile_major(x):
    comps, points, width = x.shape
    return jnp.transpose(x.reshape(comps, points, width // TILE, TILE), (2, 0, 1, 3))


def tile_minor(x):
    tiles, comps, points, width = x.shape
    return jnp.transpose(x, (1, 2, 0, 3)).reshape(comps, points, tiles * width)


def per_device(focus_direct, u_factors, v_factors, tile_ranks, onset_rec, onset_src):
    parts = lax.axis_size("freq")
    place = lax.axis_index("freq")
    u_fac = u_factors[0]
    v_fac = v_factors[0]
    col_tiles = u_fac.shape[0]
    row_tiles = v_fac.shape[0]
    u_tiles = u_fac.reshape(col_tiles, 2, RANK, row_tiles, TILE)
    v_tiles = v_fac.reshape(row_tiles, 2, RANK, col_tiles, TILE)
    rank_index = jnp.arange(RANK, dtype=jnp.int32)
    mask = (rank_index[None, None, :] < tile_ranks[0][:, :, None])[:, None]
    rec_tiles = onset_rec.shape[1] // TILE
    rec_picked = window_gather(parts, onset_pieces(onset_rec, rec_tiles, parts, place))
    src_picked = window_gather(parts, onset_pieces(onset_src, col_tiles, parts, place))
    direct = tile_major(focus_direct[0])
    direct_f32 = direct.astype(jnp.float32)
    plus = direct
    minus = None
    for sweep in range(ITERS):
        z_real, z_imag = coefficients(v_tiles, mask, plus)
        partial_terms = expand_rows(u_tiles, z_real, z_imag)
        summed = reduce_src(partial_terms)
        traces = exchange(summed, parts)
        windowed = window(traces, rec_picked)
        minus = exchange_back(windowed, rec_tiles)
        minus_all = lax.all_gather(minus, "src", axis=0, tiled=True)
        adjoint = adjoint_local(u_tiles, v_tiles, mask, minus_all)
        source_traces = exchange(adjoint.astype(jnp.bfloat16), parts)
        src_windowed = window(source_traces, src_picked)
        returned = exchange_back(src_windowed, col_tiles).astype(jnp.float32)
        plus = (direct_f32 + returned).astype(jnp.bfloat16)
    return (tile_minor(plus)[None], tile_minor(minus)[None])


def solution(mesh):
    placed = (
        P("freq", None, ("groups", "vp"), "src"),
        P("freq", "src", None, None, None),
        P("freq", None, None, None, "src"),
        P("freq", None, "src"),
        P(("groups", "vp"), "src"),
        P(("groups", "vp"), "src"),
    )
    return jax.shard_map(
        per_device,
        mesh=mesh,
        in_specs=placed,
        out_specs=(
            P("freq", None, ("groups", "vp"), "src"),
            P("freq", None, ("groups", "vp"), "src"),
        ),
        check_vma=False,
    )
```

```python
import math

import jax
import jax.numpy as jnp
from jax import lax
from jax.experimental import pallas as pl
from jax.sharding import PartitionSpec as P

TILE = 256
RANK = 32
NT = 256
FLO = 8
ITERS = 2
GATHER_MAX = 4


def make_tables(count):
    index = FLO + jnp.arange(count, dtype=jnp.int32)
    sample = jnp.arange(NT, dtype=jnp.int32)
    phase = (index[:, None] * sample[None, :] % NT).astype(jnp.float32) * (2.0 * math.pi / NT)
    cosine = jnp.cos(phase)
    sine = jnp.sin(phase)
    inverse = jnp.stack([cosine, -sine]) * (2.0 / NT)
    forward = jnp.stack([cosine, -sine])
    return (inverse, forward)


def gather_kernel(table_ref, onset_ref, out_ref):
    rows = onset_ref.shape[1]
    width = onset_ref.shape[2]
    sample = lax.broadcasted_iota(jnp.int32, (NT, width), 0)
    for row in range(rows):
        place = jnp.clip(onset_ref[0, row : row + 1, :], 0, NT) - 1
        pick = (sample == place).astype(jnp.bfloat16)
        parts = jnp.dot(table_ref[...], pick, preferred_element_type=jnp.float32)
        out_ref[:, 0, row, :] = parts.astype(out_ref.dtype)


def window_gather(count, onset):
    if count > GATHER_MAX:
        return onset
    inverse, forward = make_tables(count)
    terms = jnp.einsum("cft,dgt->tgdfc", forward, inverse, precision=lax.Precision.HIGHEST)
    size = 4 * count * count
    table = jnp.cumsum(terms.reshape(NT, size), axis=0)
    stacked = table.astype(jnp.bfloat16).T
    blocks, points, width = onset.shape
    rows = 8
    return pl.pallas_call(
        gather_kernel,
        grid=(blocks, points // rows),
        in_specs=[
            pl.BlockSpec((size, NT), lambda b, r: (0, 0)),
            pl.BlockSpec((1, rows, width), lambda b, r: (b, r, 0)),
        ],
        out_specs=pl.BlockSpec((size, 1, rows, width), lambda b, r: (0, b, r, 0)),
        out_shape=jax.ShapeDtypeStruct((size, blocks, points, width), jnp.bfloat16),
    )(stacked, onset)


def window_kernel(matrix_ref, spectrum_ref, out_ref):
    count = spectrum_ref.shape[0]
    comps = 2 * count
    source = [spectrum_ref[q // 2, 0, q % 2].astype(jnp.float32) for q in range(comps)]
    for target in range(comps):
        total = matrix_ref[target, 0].astype(jnp.float32) * source[0]
        for q in range(1, comps):
            total = total + matrix_ref[q * comps + target, 0].astype(jnp.float32) * source[q]
        out_ref[target // 2, 0, target % 2] = total.astype(out_ref.dtype)


def window(spectrum, picked):
    count = spectrum.shape[0]
    if count > GATHER_MAX:
        inverse, forward = make_tables(count)
        signal = jnp.einsum(
            "fbcvm,cft->bvmt", spectrum.astype(jnp.float32), inverse, precision=lax.Precision.HIGHEST
        )
        keep = lax.broadcasted_iota(jnp.int32, signal.shape, 3) < picked[..., None]
        signal = jnp.where(keep, signal, jnp.zeros_like(signal))
        result = jnp.einsum("bvmt,cft->fbcvm", signal, forward, precision=lax.Precision.HIGHEST)
        return result.astype(jnp.bfloat16)
    _, blocks, comps, points, width = spectrum.shape
    size = picked.shape[0]
    return pl.pallas_call(
        window_kernel,
        grid=(blocks,),
        in_specs=[
            pl.BlockSpec((size, 1, points, width), lambda b: (0, b, 0, 0)),
            pl.BlockSpec((count, 1, comps, points, width), lambda b: (0, b, 0, 0, 0)),
        ],
        out_specs=pl.BlockSpec((count, 1, comps, points, width), lambda b: (0, b, 0, 0, 0)),
        out_shape=jax.ShapeDtypeStruct(spectrum.shape, jnp.bfloat16),
    )(picked, spectrum)


def piece_count(tiles, parts):
    return parts // math.gcd(tiles, parts)


def to_pieces(x, parts):
    tiles, comps, points, width = x.shape
    k = piece_count(tiles, parts)
    if k == 1:
        return x
    x = x.reshape(tiles, comps, points, k, width // k)
    return jnp.transpose(x, (0, 3, 1, 2, 4)).reshape(tiles * k, comps, points, width // k)


def from_pieces(x, tiles):
    count, comps, points, width = x.shape
    k = count // tiles
    if k == 1:
        return x
    x = x.reshape(tiles, k, comps, points, width)
    return jnp.transpose(x, (0, 2, 3, 1, 4)).reshape(tiles, comps, points, k * width)


def onset_pieces(onset, tiles, parts, place):
    points = onset.shape[0]
    k = piece_count(tiles, parts)
    blocks = tiles * k
    each = blocks // parts
    split = onset.reshape(points, blocks, TILE // k)
    split = jnp.transpose(split, (1, 0, 2))
    return lax.dynamic_slice_in_dim(split, place * each, each, 0)


def exchange(x, parts):
    tiles = x.shape[0]
    pieces = to_pieces(x, parts)
    got = lax.all_to_all(pieces, "freq", split_axis=0, concat_axis=0, tiled=True)
    return got.reshape((parts, got.shape[0] // parts) + got.shape[1:])


def exchange_back(y, tiles):
    flat = y.reshape((y.shape[0] * y.shape[1],) + y.shape[2:])
    got = lax.all_to_all(flat, "freq", split_axis=0, concat_axis=0, tiled=True)
    return from_pieces(got, tiles)


def coefficients(v_tiles, mask, plus):
    turned = jnp.stack([plus[:, 1], -plus[:, 0]], axis=1)
    both = jnp.stack([plus, turned, -turned])
    z = jnp.einsum("icrjt,ojcvt->oivjr", v_tiles, both, preferred_element_type=jnp.float32)
    z = jnp.where(mask[None], z, 0.0).astype(jnp.bfloat16)
    return z[0], z[1], z[2]


def expand_rows(u_tiles, z_real, z_imag, z_minus):
    both = jnp.stack([jnp.stack([z_real, z_minus]), jnp.stack([z_imag, z_real])])
    return jnp.einsum("jcrit,ocivjr->iovt", u_tiles, both, preferred_element_type=jnp.float32)


def adjoint_local(u_tiles, v_tiles, mask, minus):
    turned = jnp.stack([minus[:, 1], -minus[:, 0]], axis=1)
    both = jnp.stack([minus, turned])
    w = jnp.einsum("jcrit,oicvt->oivjr", u_tiles, both, preferred_element_type=jnp.float32)
    w = jnp.where(mask[None], w, 0.0).astype(jnp.bfloat16)
    w_real, w_imag = w[0], w[1]
    parts = jnp.stack([jnp.stack([w_real, -w_imag]), jnp.stack([w_imag, w_real])])
    return jnp.einsum("icrjt,ocivjr->jovt", v_tiles, parts, preferred_element_type=jnp.float32)


def reduce_src(partial):
    count = lax.axis_size("src")
    if count != 2:
        return lax.psum_scatter(
            partial.astype(jnp.bfloat16), "src", scatter_dimension=0, tiled=True
        )
    place = lax.axis_index("src")
    half = partial.shape[0] // 2
    mine = lax.dynamic_slice_in_dim(partial, place * half, half, 0)
    other = lax.dynamic_slice_in_dim(partial, (1 - place) * half, half, 0)
    got = lax.ppermute(other.astype(jnp.bfloat16), "src", perm=[(0, 1), (1, 0)])
    return (mine.astype(jnp.bfloat16).astype(jnp.float32) + got.astype(jnp.float32)).astype(jnp.bfloat16)


def tile_major(x):
    comps, points, width = x.shape
    return jnp.transpose(x.reshape(comps, points, width // TILE, TILE), (2, 0, 1, 3))


def tile_minor(x):
    tiles, comps, points, width = x.shape
    return jnp.transpose(x, (1, 2, 0, 3)).reshape(comps, points, tiles * width)


def per_device(focus_direct, u_factors, v_factors, tile_ranks, onset_rec, onset_src):
    parts = lax.axis_size("freq")
    place = lax.axis_index("freq")
    u_fac = u_factors[0]
    v_fac = v_factors[0]
    col_tiles = u_fac.shape[0]
    row_tiles = v_fac.shape[0]
    u_tiles = u_fac.reshape(col_tiles, 2, RANK, row_tiles, TILE)
    v_tiles = v_fac.reshape(row_tiles, 2, RANK, col_tiles, TILE)
    rank_index = jnp.arange(RANK, dtype=jnp.int32)
    mask = (rank_index[None, None, :] < tile_ranks[0][:, :, None])[:, None]
    rec_tiles = onset_rec.shape[1] // TILE
    rec_picked = window_gather(parts, onset_pieces(onset_rec, rec_tiles, parts, place))
    src_picked = window_gather(parts, onset_pieces(onset_src, col_tiles, parts, place))
    direct = tile_major(focus_direct[0])
    direct_f32 = direct.astype(jnp.float32)
    plus = direct
    minus = None
    for sweep in range(ITERS):
        z_real, z_imag, z_minus = coefficients(v_tiles, mask, plus)
        partial_terms = expand_rows(u_tiles, z_real, z_imag, z_minus)
        summed = reduce_src(partial_terms)
        traces = exchange(summed, parts)
        windowed = window(traces, rec_picked)
        minus = exchange_back(windowed, rec_tiles)
        minus_all = lax.all_gather(minus, "src", axis=0, tiled=True)
        adjoint = adjoint_local(u_tiles, v_tiles, mask, minus_all)
        source_traces = exchange(adjoint.astype(jnp.bfloat16), parts)
        src_windowed = window(source_traces, src_picked)
        returned = exchange_back(src_windowed, col_tiles).astype(jnp.float32)
        plus = (direct_f32 + returned).astype(jnp.bfloat16)
    return (tile_minor(plus)[None], tile_minor(minus)[None])


def solution(mesh):
    placed = (
        P("freq", None, ("groups", "vp"), "src"),
        P("freq", "src", None, None, None),
        P("freq", None, None, None, "src"),
        P("freq", None, "src"),
        P(("groups", "vp"), "src"),
        P(("groups", "vp"), "src"),
    )
    return jax.shard_map(
        per_device,
        mesh=mesh,
        in_specs=placed,
        out_specs=(
            P("freq", None, ("groups", "vp"), "src"),
            P("freq", None, ("groups", "vp"), "src"),
        ),
        check_vma=False,
    )
```

```python
import math

import jax
import jax.numpy as jnp
from jax import lax
from jax.experimental import pallas as pl
from jax.sharding import PartitionSpec as P

TILE = 256
RANK = 32
NT = 256
FLO = 8
ITERS = 2
GATHER_MAX = 4


def make_tables(count):
    index = FLO + jnp.arange(count, dtype=jnp.int32)
    sample = jnp.arange(NT, dtype=jnp.int32)
    phase = (index[:, None] * sample[None, :] % NT).astype(jnp.float32) * (2.0 * math.pi / NT)
    cosine = jnp.cos(phase)
    sine = jnp.sin(phase)
    inverse = jnp.stack([cosine, -sine]) * (2.0 / NT)
    forward = jnp.stack([cosine, -sine])
    return (inverse, forward)


def gather_kernel(table_ref, onset_ref, out_ref):
    rows = onset_ref.shape[1]
    width = onset_ref.shape[2]
    sample = lax.broadcasted_iota(jnp.int32, (NT, width), 0)
    for row in range(rows):
        place = jnp.clip(onset_ref[0, row : row + 1, :], 0, NT) - 1
        pick = (sample == place).astype(jnp.bfloat16)
        parts = jnp.dot(table_ref[...], pick, preferred_element_type=jnp.float32)
        out_ref[:, 0, row, :] = parts.astype(out_ref.dtype)


def window_gather(count, onset):
    if count > GATHER_MAX:
        return onset
    inverse, forward = make_tables(count)
    terms = jnp.einsum("cft,dgt->tgdfc", forward, inverse, precision=lax.Precision.HIGHEST)
    size = 4 * count * count
    table = jnp.cumsum(terms.reshape(NT, size), axis=0)
    stacked = table.astype(jnp.bfloat16).T
    blocks, points, width = onset.shape
    rows = 8
    return pl.pallas_call(
        gather_kernel,
        grid=(blocks, points // rows),
        in_specs=[
            pl.BlockSpec((size, NT), lambda b, r: (0, 0)),
            pl.BlockSpec((1, rows, width), lambda b, r: (b, r, 0)),
        ],
        out_specs=pl.BlockSpec((size, 1, rows, width), lambda b, r: (0, b, r, 0)),
        out_shape=jax.ShapeDtypeStruct((size, blocks, points, width), jnp.bfloat16),
    )(stacked, onset)


def window_kernel(matrix_ref, spectrum_ref, out_ref):
    count = spectrum_ref.shape[0]
    comps = 2 * count
    for block in range(spectrum_ref.shape[1]):
        source = [spectrum_ref[q // 2, block, q % 2].astype(jnp.float32) for q in range(comps)]
        for target in range(comps):
            total = matrix_ref[target, block].astype(jnp.float32) * source[0]
            for q in range(1, comps):
                total = total + matrix_ref[q * comps + target, block].astype(jnp.float32) * source[q]
            out_ref[target // 2, block, target % 2] = total.astype(out_ref.dtype)


def window(spectrum, picked):
    count = spectrum.shape[0]
    if count > GATHER_MAX:
        inverse, forward = make_tables(count)
        signal = jnp.einsum(
            "fbcvm,cft->bvmt", spectrum.astype(jnp.float32), inverse, precision=lax.Precision.HIGHEST
        )
        keep = lax.broadcasted_iota(jnp.int32, signal.shape, 3) < picked[..., None]
        signal = jnp.where(keep, signal, jnp.zeros_like(signal))
        result = jnp.einsum("bvmt,cft->fbcvm", signal, forward, precision=lax.Precision.HIGHEST)
        return result.astype(jnp.bfloat16)
    _, blocks, comps, points, width = spectrum.shape
    size = picked.shape[0]
    step = 2 if blocks % 2 == 0 else 1
    return pl.pallas_call(
        window_kernel,
        grid=(blocks // step,),
        in_specs=[
            pl.BlockSpec((size, step, points, width), lambda b: (0, b, 0, 0)),
            pl.BlockSpec((count, step, comps, points, width), lambda b: (0, b, 0, 0, 0)),
        ],
        out_specs=pl.BlockSpec((count, step, comps, points, width), lambda b: (0, b, 0, 0, 0)),
        out_shape=jax.ShapeDtypeStruct(spectrum.shape, jnp.bfloat16),
    )(picked, spectrum)


def piece_count(tiles, parts):
    return parts // math.gcd(tiles, parts)


def to_pieces(x, parts):
    tiles, comps, points, width = x.shape
    k = piece_count(tiles, parts)
    if k == 1:
        return x
    x = x.reshape(tiles, comps, points, k, width // k)
    return jnp.transpose(x, (0, 3, 1, 2, 4)).reshape(tiles * k, comps, points, width // k)


def from_pieces(x, tiles):
    count, comps, points, width = x.shape
    k = count // tiles
    if k == 1:
        return x
    x = x.reshape(tiles, k, comps, points, width)
    return jnp.transpose(x, (0, 2, 3, 1, 4)).reshape(tiles, comps, points, k * width)


def onset_pieces(onset, tiles, parts, place):
    points = onset.shape[0]
    k = piece_count(tiles, parts)
    blocks = tiles * k
    each = blocks // parts
    split = onset.reshape(points, blocks, TILE // k)
    split = jnp.transpose(split, (1, 0, 2))
    return lax.dynamic_slice_in_dim(split, place * each, each, 0)


def exchange(x, parts):
    tiles = x.shape[0]
    pieces = to_pieces(x, parts)
    got = lax.all_to_all(pieces, "freq", split_axis=0, concat_axis=0, tiled=True)
    return got.reshape((parts, got.shape[0] // parts) + got.shape[1:])


def exchange_back(y, tiles):
    flat = y.reshape((y.shape[0] * y.shape[1],) + y.shape[2:])
    got = lax.all_to_all(flat, "freq", split_axis=0, concat_axis=0, tiled=True)
    return from_pieces(got, tiles)


def coefficients(v_tiles, mask, plus):
    turned = jnp.stack([plus[:, 1], -plus[:, 0]], axis=1)
    both = jnp.stack([plus, turned])
    z = jnp.einsum("icrjt,ojcvt->oivjr", v_tiles, both, preferred_element_type=jnp.float32)
    z = jnp.where(mask[None], z, 0.0).astype(jnp.bfloat16)
    return z[0], z[1]


def expand_rows(u_tiles, z_real, z_imag):
    both = jnp.stack([jnp.stack([z_real, -z_imag]), jnp.stack([z_imag, z_real])])
    product = jnp.einsum("jcrit,ocivjr->iovt", u_tiles, both, preferred_element_type=jnp.float32)
    return product.astype(jnp.bfloat16)


def adjoint_local(u_tiles, v_tiles, mask, minus):
    turned = jnp.stack([minus[:, 1], -minus[:, 0]], axis=1)
    both = jnp.stack([minus, turned])
    w = jnp.einsum("jcrit,oicvt->oivjr", u_tiles, both, preferred_element_type=jnp.float32)
    w = jnp.where(mask[None], w, 0.0).astype(jnp.bfloat16)
    w_real, w_imag = w[0], w[1]
    parts = jnp.stack([jnp.stack([w_real, -w_imag]), jnp.stack([w_imag, w_real])])
    return jnp.einsum("icrjt,ocivjr->jovt", v_tiles, parts, preferred_element_type=jnp.float32)


def reduce_src(partial):
    count = lax.axis_size("src")
    if count != 2:
        return lax.psum_scatter(
            partial.astype(jnp.bfloat16), "src", scatter_dimension=0, tiled=True
        )
    place = lax.axis_index("src")
    half = partial.shape[0] // 2
    mine = lax.dynamic_slice_in_dim(partial, place * half, half, 0)
    other = lax.dynamic_slice_in_dim(partial, (1 - place) * half, half, 0)
    got = lax.ppermute(other, "src", perm=[(0, 1), (1, 0)])
    return (mine.astype(jnp.float32) + got.astype(jnp.float32)).astype(jnp.bfloat16)


def tile_major(x):
    comps, points, width = x.shape
    return jnp.transpose(x.reshape(comps, points, width // TILE, TILE), (2, 0, 1, 3))


def tile_minor(x):
    tiles, comps, points, width = x.shape
    return jnp.transpose(x, (1, 2, 0, 3)).reshape(comps, points, tiles * width)


def per_device(focus_direct, u_factors, v_factors, tile_ranks, onset_rec, onset_src):
    parts = lax.axis_size("freq")
    place = lax.axis_index("freq")
    u_fac = u_factors[0]
    v_fac = v_factors[0]
    col_tiles = u_fac.shape[0]
    row_tiles = v_fac.shape[0]
    u_tiles = u_fac.reshape(col_tiles, 2, RANK, row_tiles, TILE)
    v_tiles = v_fac.reshape(row_tiles, 2, RANK, col_tiles, TILE)
    rank_index = jnp.arange(RANK, dtype=jnp.int32)
    mask = (rank_index[None, None, :] < tile_ranks[0][:, :, None])[:, None]
    rec_tiles = onset_rec.shape[1] // TILE
    rec_picked = window_gather(parts, onset_pieces(onset_rec, rec_tiles, parts, place))
    src_picked = window_gather(parts, onset_pieces(onset_src, col_tiles, parts, place))
    direct = tile_major(focus_direct[0])
    direct_f32 = direct.astype(jnp.float32)
    plus = direct
    minus = None
    for sweep in range(ITERS):
        z_real, z_imag = coefficients(v_tiles, mask, plus)
        partial_terms = expand_rows(u_tiles, z_real, z_imag)
        summed = reduce_src(partial_terms)
        traces = exchange(summed, parts)
        windowed = window(traces, rec_picked)
        minus = exchange_back(windowed, rec_tiles)
        minus_all = lax.all_gather(minus, "src", axis=0, tiled=True)
        adjoint = adjoint_local(u_tiles, v_tiles, mask, minus_all)
        source_traces = exchange(adjoint.astype(jnp.bfloat16), parts)
        src_windowed = window(source_traces, src_picked)
        returned = exchange_back(src_windowed, col_tiles).astype(jnp.float32)
        plus = (direct_f32 + returned).astype(jnp.bfloat16)
    return (tile_minor(plus)[None], tile_minor(minus)[None])


def solution(mesh):
    placed = (
        P("freq", None, ("groups", "vp"), "src"),
        P("freq", "src", None, None, None),
        P("freq", None, None, None, "src"),
        P("freq", None, "src"),
        P(("groups", "vp"), "src"),
        P(("groups", "vp"), "src"),
    )
    return jax.shard_map(
        per_device,
        mesh=mesh,
        in_specs=placed,
        out_specs=(
            P("freq", None, ("groups", "vp"), "src"),
            P("freq", None, ("groups", "vp"), "src"),
        ),
        check_vma=False,
    )
```

```python
import math

import jax
import jax.numpy as jnp
from jax import lax
from jax.experimental import pallas as pl
from jax.sharding import PartitionSpec as P

TILE = 256
RANK = 32
NT = 256
FLO = 8
ITERS = 2
GATHER_MAX = 4


def make_tables(count):
    index = FLO + jnp.arange(count, dtype=jnp.int32)
    sample = jnp.arange(NT, dtype=jnp.int32)
    phase = (index[:, None] * sample[None, :] % NT).astype(jnp.float32) * (2.0 * math.pi / NT)
    cosine = jnp.cos(phase)
    sine = jnp.sin(phase)
    inverse = jnp.stack([cosine, -sine]) * (2.0 / NT)
    forward = jnp.stack([cosine, -sine])
    return (inverse, forward)


def gather_kernel(table_ref, onset_ref, out_ref):
    rows = onset_ref.shape[1]
    width = onset_ref.shape[2]
    sample = lax.broadcasted_iota(jnp.int32, (NT, width), 0)
    for row in range(rows):
        place = jnp.clip(onset_ref[0, row : row + 1, :], 0, NT) - 1
        pick = (sample == place).astype(jnp.bfloat16)
        parts = jnp.dot(table_ref[...], pick, preferred_element_type=jnp.float32)
        out_ref[:, 0, row, :] = parts.astype(out_ref.dtype)


def window_gather(count, onset):
    if count > GATHER_MAX:
        return onset
    inverse, forward = make_tables(count)
    terms = jnp.einsum("cft,dgt->tgdfc", forward, inverse, precision=lax.Precision.HIGHEST)
    size = 4 * count * count
    table = jnp.cumsum(terms.reshape(NT, size), axis=0)
    stacked = table.astype(jnp.bfloat16).T
    blocks, points, width = onset.shape
    rows = 16 if points % 16 == 0 else 8
    return pl.pallas_call(
        gather_kernel,
        grid=(blocks, points // rows),
        in_specs=[
            pl.BlockSpec((size, NT), lambda b, r: (0, 0)),
            pl.BlockSpec((1, rows, width), lambda b, r: (b, r, 0)),
        ],
        out_specs=pl.BlockSpec((size, 1, rows, width), lambda b, r: (0, b, r, 0)),
        out_shape=jax.ShapeDtypeStruct((size, blocks, points, width), jnp.bfloat16),
    )(stacked, onset)


def window_kernel(matrix_ref, spectrum_ref, out_ref):
    count = spectrum_ref.shape[0]
    comps = 2 * count
    for block in range(spectrum_ref.shape[1]):
        source = [spectrum_ref[q // 2, block, q % 2].astype(jnp.float32) for q in range(comps)]
        for target in range(comps):
            total = matrix_ref[target, block].astype(jnp.float32) * source[0]
            for q in range(1, comps):
                total = total + matrix_ref[q * comps + target, block].astype(jnp.float32) * source[q]
            out_ref[target // 2, block, target % 2] = total.astype(out_ref.dtype)


def window(spectrum, picked):
    count = spectrum.shape[0]
    if count > GATHER_MAX:
        inverse, forward = make_tables(count)
        signal = jnp.einsum(
            "fbcvm,cft->bvmt", spectrum.astype(jnp.float32), inverse, precision=lax.Precision.HIGHEST
        )
        keep = lax.broadcasted_iota(jnp.int32, signal.shape, 3) < picked[..., None]
        signal = jnp.where(keep, signal, jnp.zeros_like(signal))
        result = jnp.einsum("bvmt,cft->fbcvm", signal, forward, precision=lax.Precision.HIGHEST)
        return result.astype(jnp.bfloat16)
    _, blocks, comps, points, width = spectrum.shape
    size = picked.shape[0]
    step = 2 if blocks % 2 == 0 else 1
    return pl.pallas_call(
        window_kernel,
        grid=(blocks // step,),
        in_specs=[
            pl.BlockSpec((size, step, points, width), lambda b: (0, b, 0, 0)),
            pl.BlockSpec((count, step, comps, points, width), lambda b: (0, b, 0, 0, 0)),
        ],
        out_specs=pl.BlockSpec((count, step, comps, points, width), lambda b: (0, b, 0, 0, 0)),
        out_shape=jax.ShapeDtypeStruct(spectrum.shape, jnp.bfloat16),
    )(picked, spectrum)


def piece_count(tiles, parts):
    return parts // math.gcd(tiles, parts)


def to_pieces(x, parts):
    tiles, comps, points, width = x.shape
    k = piece_count(tiles, parts)
    if k == 1:
        return x
    x = x.reshape(tiles, comps, points, k, width // k)
    return jnp.transpose(x, (0, 3, 1, 2, 4)).reshape(tiles * k, comps, points, width // k)


def from_pieces(x, tiles):
    count, comps, points, width = x.shape
    k = count // tiles
    if k == 1:
        return x
    x = x.reshape(tiles, k, comps, points, width)
    return jnp.transpose(x, (0, 2, 3, 1, 4)).reshape(tiles, comps, points, k * width)


def onset_pieces(onset, tiles, parts, place):
    points = onset.shape[0]
    k = piece_count(tiles, parts)
    blocks = tiles * k
    each = blocks // parts
    split = onset.reshape(points, blocks, TILE // k)
    split = jnp.transpose(split, (1, 0, 2))
    return lax.dynamic_slice_in_dim(split, place * each, each, 0)


def exchange(x, parts):
    tiles = x.shape[0]
    pieces = to_pieces(x, parts)
    got = lax.all_to_all(pieces, "freq", split_axis=0, concat_axis=0, tiled=True)
    return got.reshape((parts, got.shape[0] // parts) + got.shape[1:])


def exchange_back(y, tiles):
    flat = y.reshape((y.shape[0] * y.shape[1],) + y.shape[2:])
    got = lax.all_to_all(flat, "freq", split_axis=0, concat_axis=0, tiled=True)
    return from_pieces(got, tiles)


def coefficients(v_tiles, mask, plus):
    turned = jnp.stack([plus[:, 1], -plus[:, 0]], axis=1)
    both = jnp.stack([plus, turned])
    z = jnp.einsum("icrjt,ojcvt->oivjr", v_tiles, both, preferred_element_type=jnp.float32)
    z = jnp.where(mask[None], z, 0.0).astype(jnp.bfloat16)
    return z[0], z[1]


def expand_rows(u_tiles, z_real, z_imag):
    both = jnp.stack([jnp.stack([z_real, -z_imag]), jnp.stack([z_imag, z_real])])
    product = jnp.einsum("jcrit,ocivjr->iovt", u_tiles, both, preferred_element_type=jnp.float32)
    return product.astype(jnp.bfloat16)


def adjoint_local(u_tiles, v_tiles, mask, minus):
    turned = jnp.stack([minus[:, 1], -minus[:, 0]], axis=1)
    both = jnp.stack([minus, turned])
    w = jnp.einsum("jcrit,oicvt->oivjr", u_tiles, both, preferred_element_type=jnp.float32)
    w = jnp.where(mask[None], w, 0.0).astype(jnp.bfloat16)
    w_real, w_imag = w[0], w[1]
    parts = jnp.stack([jnp.stack([w_real, -w_imag]), jnp.stack([w_imag, w_real])])
    return jnp.einsum("icrjt,ocivjr->jovt", v_tiles, parts, preferred_element_type=jnp.float32)


def reduce_src(partial):
    count = lax.axis_size("src")
    if count != 2:
        return lax.psum_scatter(
            partial.astype(jnp.bfloat16), "src", scatter_dimension=0, tiled=True
        )
    place = lax.axis_index("src")
    half = partial.shape[0] // 2
    mine = lax.dynamic_slice_in_dim(partial, place * half, half, 0)
    other = lax.dynamic_slice_in_dim(partial, (1 - place) * half, half, 0)
    got = lax.ppermute(other, "src", perm=[(0, 1), (1, 0)])
    return (mine.astype(jnp.float32) + got.astype(jnp.float32)).astype(jnp.bfloat16)


def tile_major(x):
    comps, points, width = x.shape
    return jnp.transpose(x.reshape(comps, points, width // TILE, TILE), (2, 0, 1, 3))


def tile_minor(x):
    tiles, comps, points, width = x.shape
    return jnp.transpose(x, (1, 2, 0, 3)).reshape(comps, points, tiles * width)


def per_device(focus_direct, u_factors, v_factors, tile_ranks, onset_rec, onset_src):
    parts = lax.axis_size("freq")
    place = lax.axis_index("freq")
    u_fac = u_factors[0]
    v_fac = v_factors[0]
    col_tiles = u_fac.shape[0]
    row_tiles = v_fac.shape[0]
    u_tiles = u_fac.reshape(col_tiles, 2, RANK, row_tiles, TILE)
    v_tiles = v_fac.reshape(row_tiles, 2, RANK, col_tiles, TILE)
    rank_index = jnp.arange(RANK, dtype=jnp.int32)
    mask = (rank_index[None, None, :] < tile_ranks[0][:, :, None])[:, None]
    rec_tiles = onset_rec.shape[1] // TILE
    rec_picked = window_gather(parts, onset_pieces(onset_rec, rec_tiles, parts, place))
    src_picked = window_gather(parts, onset_pieces(onset_src, col_tiles, parts, place))
    direct = tile_major(focus_direct[0])
    direct_f32 = direct.astype(jnp.float32)
    plus = direct
    minus = None
    for sweep in range(ITERS):
        z_real, z_imag = coefficients(v_tiles, mask, plus)
        partial_terms = expand_rows(u_tiles, z_real, z_imag)
        summed = reduce_src(partial_terms)
        traces = exchange(summed, parts)
        windowed = window(traces, rec_picked)
        minus = exchange_back(windowed, rec_tiles)
        minus_all = lax.all_gather(minus, "src", axis=0, tiled=True)
        adjoint = adjoint_local(u_tiles, v_tiles, mask, minus_all)
        source_traces = exchange(adjoint.astype(jnp.bfloat16), parts)
        src_windowed = window(source_traces, src_picked)
        returned = exchange_back(src_windowed, col_tiles).astype(jnp.float32)
        plus = (direct_f32 + returned).astype(jnp.bfloat16)
    return (tile_minor(plus)[None], tile_minor(minus)[None])


def solution(mesh):
    placed = (
        P("freq", None, ("groups", "vp"), "src"),
        P("freq", "src", None, None, None),
        P("freq", None, None, None, "src"),
        P("freq", None, "src"),
        P(("groups", "vp"), "src"),
        P(("groups", "vp"), "src"),
    )
    return jax.shard_map(
        per_device,
        mesh=mesh,
        in_specs=placed,
        out_specs=(
            P("freq", None, ("groups", "vp"), "src"),
            P("freq", None, ("groups", "vp"), "src"),
        ),
        check_vma=False,
    )
```

```python
import math

import jax
import jax.numpy as jnp
from jax import lax
from jax.experimental import pallas as pl
from jax.sharding import PartitionSpec as P

TILE = 256
RANK = 32
NT = 256
FLO = 8
ITERS = 2
GATHER_MAX = 4


def make_tables(count):
    index = FLO + jnp.arange(count, dtype=jnp.int32)
    sample = jnp.arange(NT, dtype=jnp.int32)
    phase = (index[:, None] * sample[None, :] % NT).astype(jnp.float32) * (2.0 * math.pi / NT)
    cosine = jnp.cos(phase)
    sine = jnp.sin(phase)
    inverse = jnp.stack([cosine, -sine]) * (2.0 / NT)
    forward = jnp.stack([cosine, -sine])
    return (inverse, forward)


def gather_kernel(table_ref, onset_ref, out_ref):
    rows = onset_ref.shape[1]
    width = onset_ref.shape[2]
    sample = lax.broadcasted_iota(jnp.int32, (NT, width), 0)
    for row in range(rows):
        place = jnp.clip(onset_ref[0, row : row + 1, :], 0, NT) - 1
        pick = (sample == place).astype(jnp.bfloat16)
        parts = jnp.dot(table_ref[...], pick, preferred_element_type=jnp.float32)
        out_ref[:, 0, row, :] = parts.astype(out_ref.dtype)


def window_gather(count, onset):
    if count > GATHER_MAX:
        return onset
    inverse, forward = make_tables(count)
    terms = jnp.einsum("cft,dgt->tgdfc", forward, inverse, precision=lax.Precision.HIGHEST)
    size = 4 * count * count
    table = jnp.cumsum(terms.reshape(NT, size), axis=0)
    stacked = table.astype(jnp.bfloat16).T
    blocks, points, width = onset.shape
    rows = 24 if points % 24 == 0 else 8
    return pl.pallas_call(
        gather_kernel,
        grid=(blocks, points // rows),
        in_specs=[
            pl.BlockSpec((size, NT), lambda b, r: (0, 0)),
            pl.BlockSpec((1, rows, width), lambda b, r: (b, r, 0)),
        ],
        out_specs=pl.BlockSpec((size, 1, rows, width), lambda b, r: (0, b, r, 0)),
        out_shape=jax.ShapeDtypeStruct((size, blocks, points, width), jnp.bfloat16),
    )(stacked, onset)


def window_kernel(matrix_ref, spectrum_ref, out_ref):
    count = spectrum_ref.shape[0]
    comps = 2 * count
    for block in range(spectrum_ref.shape[1]):
        source = [spectrum_ref[q // 2, block, q % 2].astype(jnp.float32) for q in range(comps)]
        for target in range(comps):
            total = matrix_ref[target, block].astype(jnp.float32) * source[0]
            for q in range(1, comps):
                total = total + matrix_ref[q * comps + target, block].astype(jnp.float32) * source[q]
            out_ref[target // 2, block, target % 2] = total.astype(out_ref.dtype)


def window(spectrum, picked):
    count = spectrum.shape[0]
    if count > GATHER_MAX:
        inverse, forward = make_tables(count)
        signal = jnp.einsum(
            "fbcvm,cft->bvmt", spectrum.astype(jnp.float32), inverse, precision=lax.Precision.HIGHEST
        )
        keep = lax.broadcasted_iota(jnp.int32, signal.shape, 3) < picked[..., None]
        signal = jnp.where(keep, signal, jnp.zeros_like(signal))
        result = jnp.einsum("bvmt,cft->fbcvm", signal, forward, precision=lax.Precision.HIGHEST)
        return result.astype(jnp.bfloat16)
    _, blocks, comps, points, width = spectrum.shape
    size = picked.shape[0]
    step = 2 if blocks % 2 == 0 else 1
    return pl.pallas_call(
        window_kernel,
        grid=(blocks // step,),
        in_specs=[
            pl.BlockSpec((size, step, points, width), lambda b: (0, b, 0, 0)),
            pl.BlockSpec((count, step, comps, points, width), lambda b: (0, b, 0, 0, 0)),
        ],
        out_specs=pl.BlockSpec((count, step, comps, points, width), lambda b: (0, b, 0, 0, 0)),
        out_shape=jax.ShapeDtypeStruct(spectrum.shape, jnp.bfloat16),
    )(picked, spectrum)


def piece_count(tiles, parts):
    return parts // math.gcd(tiles, parts)


def to_pieces(x, parts):
    tiles, comps, points, width = x.shape
    k = piece_count(tiles, parts)
    if k == 1:
        return x
    x = x.reshape(tiles, comps, points, k, width // k)
    return jnp.transpose(x, (0, 3, 1, 2, 4)).reshape(tiles * k, comps, points, width // k)


def from_pieces(x, tiles):
    count, comps, points, width = x.shape
    k = count // tiles
    if k == 1:
        return x
    x = x.reshape(tiles, k, comps, points, width)
    return jnp.transpose(x, (0, 2, 3, 1, 4)).reshape(tiles, comps, points, k * width)


def onset_pieces(onset, tiles, parts, place):
    points = onset.shape[0]
    k = piece_count(tiles, parts)
    blocks = tiles * k
    each = blocks // parts
    split = onset.reshape(points, blocks, TILE // k)
    split = jnp.transpose(split, (1, 0, 2))
    return lax.dynamic_slice_in_dim(split, place * each, each, 0)


def exchange(x, parts):
    tiles = x.shape[0]
    pieces = to_pieces(x, parts)
    got = lax.all_to_all(pieces, "freq", split_axis=0, concat_axis=0, tiled=True)
    return got.reshape((parts, got.shape[0] // parts) + got.shape[1:])


def exchange_back(y, tiles):
    flat = y.reshape((y.shape[0] * y.shape[1],) + y.shape[2:])
    got = lax.all_to_all(flat, "freq", split_axis=0, concat_axis=0, tiled=True)
    return from_pieces(got, tiles)


def coefficients(v_tiles, mask, plus):
    turned = jnp.stack([plus[:, 1], -plus[:, 0]], axis=1)
    both = jnp.stack([plus, turned])
    z = jnp.einsum("icrjt,ojcvt->oivjr", v_tiles, both, preferred_element_type=jnp.float32)
    z = jnp.where(mask[None], z, 0.0).astype(jnp.bfloat16)
    return z[0], z[1]


def expand_rows(u_tiles, z_real, z_imag):
    both = jnp.stack([jnp.stack([z_real, -z_imag]), jnp.stack([z_imag, z_real])])
    product = jnp.einsum("jcrit,ocivjr->iovt", u_tiles, both, preferred_element_type=jnp.float32)
    return product.astype(jnp.bfloat16)


def adjoint_local(u_tiles, v_tiles, mask, minus):
    turned = jnp.stack([minus[:, 1], -minus[:, 0]], axis=1)
    both = jnp.stack([minus, turned])
    w = jnp.einsum("jcrit,oicvt->oivjr", u_tiles, both, preferred_element_type=jnp.float32)
    w = jnp.where(mask[None], w, 0.0).astype(jnp.bfloat16)
    w_real, w_imag = w[0], w[1]
    parts = jnp.stack([jnp.stack([w_real, -w_imag]), jnp.stack([w_imag, w_real])])
    return jnp.einsum("icrjt,ocivjr->jovt", v_tiles, parts, preferred_element_type=jnp.float32)


def reduce_src(partial):
    count = lax.axis_size("src")
    if count != 2:
        return lax.psum_scatter(
            partial.astype(jnp.bfloat16), "src", scatter_dimension=0, tiled=True
        )
    place = lax.axis_index("src")
    half = partial.shape[0] // 2
    mine = lax.dynamic_slice_in_dim(partial, place * half, half, 0)
    other = lax.dynamic_slice_in_dim(partial, (1 - place) * half, half, 0)
    got = lax.ppermute(other, "src", perm=[(0, 1), (1, 0)])
    return (mine.astype(jnp.float32) + got.astype(jnp.float32)).astype(jnp.bfloat16)


def tile_major(x):
    comps, points, width = x.shape
    return jnp.transpose(x.reshape(comps, points, width // TILE, TILE), (2, 0, 1, 3))


def tile_minor(x):
    tiles, comps, points, width = x.shape
    return jnp.transpose(x, (1, 2, 0, 3)).reshape(comps, points, tiles * width)


def per_device(focus_direct, u_factors, v_factors, tile_ranks, onset_rec, onset_src):
    parts = lax.axis_size("freq")
    place = lax.axis_index("freq")
    u_fac = u_factors[0]
    v_fac = v_factors[0]
    col_tiles = u_fac.shape[0]
    row_tiles = v_fac.shape[0]
    u_tiles = u_fac.reshape(col_tiles, 2, RANK, row_tiles, TILE)
    v_tiles = v_fac.reshape(row_tiles, 2, RANK, col_tiles, TILE)
    rank_index = jnp.arange(RANK, dtype=jnp.int32)
    mask = (rank_index[None, None, :] < tile_ranks[0][:, :, None])[:, None]
    rec_tiles = onset_rec.shape[1] // TILE
    rec_picked = window_gather(parts, onset_pieces(onset_rec, rec_tiles, parts, place))
    src_picked = window_gather(parts, onset_pieces(onset_src, col_tiles, parts, place))
    direct = tile_major(focus_direct[0])
    direct_f32 = direct.astype(jnp.float32)
    plus = direct
    minus = None
    for sweep in range(ITERS):
        z_real, z_imag = coefficients(v_tiles, mask, plus)
        partial_terms = expand_rows(u_tiles, z_real, z_imag)
        summed = reduce_src(partial_terms)
        traces = exchange(summed, parts)
        windowed = window(traces, rec_picked)
        minus = exchange_back(windowed, rec_tiles)
        minus_all = lax.all_gather(minus, "src", axis=0, tiled=True)
        adjoint = adjoint_local(u_tiles, v_tiles, mask, minus_all)
        source_traces = exchange(adjoint.astype(jnp.bfloat16), parts)
        src_windowed = window(source_traces, src_picked)
        returned = exchange_back(src_windowed, col_tiles).astype(jnp.float32)
        plus = (direct_f32 + returned).astype(jnp.bfloat16)
    return (tile_minor(plus)[None], tile_minor(minus)[None])


def solution(mesh):
    placed = (
        P("freq", None, ("groups", "vp"), "src"),
        P("freq", "src", None, None, None),
        P("freq", None, None, None, "src"),
        P("freq", None, "src"),
        P(("groups", "vp"), "src"),
        P(("groups", "vp"), "src"),
    )
    return jax.shard_map(
        per_device,
        mesh=mesh,
        in_specs=placed,
        out_specs=(
            P("freq", None, ("groups", "vp"), "src"),
            P("freq", None, ("groups", "vp"), "src"),
        ),
        check_vma=False,
    )
```
